128 devices in a mesh: req: 64 (over z, y, x), col: 2 (over core).
Axes of the slice: x: 4, y: 4, z: 4, core: 2. Of those that a mesh axis runs over, the one named last changes fastest.
Arguments:
- tokens: bfloat16 [32768, 1024], P(('req', 'col')), may hold values from -6 to 6
- norm_gain_pair: float32 [2, 1024], replicated, may hold values from 0.5 to 1.5
- query_key_value_weight: bfloat16 [3, 1024, 1024], P(None, None, 'col'), may hold values from -1 to 1
- head_gate_weight: bfloat16 [2, 1024, 8], P(None, None, 'col'), may hold values from -0.1875 to 0.1875
- decay_logit_bias: float32 [8], P('col'), may hold values from -1 to 1024, as said below
- adapter_down_factor: bfloat16 [64, 1024, 16], P('col'), may hold values from -0.1875 to 0.1875
- adapter_up_factor: bfloat16 [64, 16, 1024], P(None, None, 'col'), may hold values from -1.5 to 1.5
- lengths: int32 [64, 2, 3], P('req'), may hold values from 1 to 128, 256 in all within a row
- request_adapter_index: int32 [64, 6], P('req'), may hold values from 0 to 63
- request_cache_index: int32 [64, 6], P('req'), may hold values from 0 to 511
- caches: bfloat16 [256, 8, 128, 128], P('req', 'col'), may hold values from -6 to 6
- head_output_weight: bfloat16 [1024, 1024], P('col'), may hold values from -0.1875 to 0.1875
- feedforward_weight: bfloat16 [3, 1024, 2816], P(None, None, 'col'), may hold values from -0.1875 to 0.1875
Outputs:
- layer_out: bfloat16 [32768, 1024], P(('req', 'col'))
The draws below stay inside these ranges and needn't reach their ends.
Inputs may be any that keep to these rules, and one draw needn't show every extreme that they name: The 3 lengths of one device sum to 256, and the longest of them is exactly 128. `request_cache_index`: a value of 256 or more means that the request has no cached memory state. `decay_logit_bias`: at most the logarithm of 512.
All inputs are finite; a program needn't handle non-finite values.
Results may differ from the reference program's by a relative error of at most 0.015.
Values may be sent and summed in bfloat16 or wider, within the bound.
No kernel may reach another device: no remote copies, remote signals or barrier semaphores. Data moves between devices by JAX's collectives and lax.ppermute only.
A program may use at most 192 MiB of HBM per device.

```python
import math
import jax
import jax.numpy as jnp
import numpy as np
from jax import lax

MODEL_WIDTH = 1024
H = 8
DH = 128
FF = 2816
ADAPTER_RANK = 16
ADAPTER_TOTAL = 64
TOK_DEV = 256
SEQ_DEV = 3
SEQS = 6
TOK_GRP = 512
MOST = 128
TOKENS = 32768
CACHES = 256
N_REQ = 64
N_COL = 2


def draw_query_key_value_weight(key, part):
    base_key = jax.random.fold_in(key, 11)
    normal_key = jax.random.fold_in(base_key, 0)
    weights = jax.random.truncated_normal(normal_key, -4.0, 4.0, (3, MODEL_WIDTH, MODEL_WIDTH), jnp.float32) * (1.0 / math.sqrt(MODEL_WIDTH))
    return weights.astype(jnp.bfloat16)


def draw_decay_logit_bias(key, part):
    base_key = jax.random.fold_in(key, 23)
    top = math.log(4.0 * MOST)
    values = jax.random.uniform(base_key, (H,), jnp.float32, -1.0, top)
    return values.astype(jnp.float32)


def place_ends(values, own_key, low, top_value):
    index_at = [jax.random.randint(jax.random.fold_in(own_key, axis), (), 0, length) for axis, length in enumerate(values.shape)]
    longest = values.shape.index(max(values.shape))
    next_to = index_at[:longest] + [(index_at[longest] + 1) % values.shape[longest]] + index_at[longest + 1:]
    return values.at[tuple(index_at)].set(low).at[tuple(next_to)].set(top_value)


def steps_of(stream_key, extent, shards, low, largest):
    def one(position, parts):
        steps = jax.random.uniform(jax.random.fold_in(jax.random.fold_in(stream_key, 6), position), (parts,), jnp.float32, low / len(shards), largest / len(shards))
        return jnp.repeat(jnp.exp(steps), extent[position] // parts).reshape((-1,) + (1,) * (len(extent) - position - 1))

    factor_of = one(*shards[0])
    for cut in shards[1:]:
        factor_of = factor_of * one(*cut)
    return factor_of


def profile(number_of, total, bound, lean):
    weights = [(1 << 20) // math.isqrt(rank ** lean) + 1 for rank in range(2, number_of + 1)]
    rest, given = total - bound - (number_of - 1), [1] * (number_of - 1)
    while rest > 0:
        free = [i for i in range(number_of - 1) if given[i] < bound]
        whole, budget = sum([weights[i] for i in free]), rest
        for i in free:
            extra = min(bound - given[i], max(1, budget * weights[i] // whole), rest)
            given[i] = given[i] + extra
            rest = rest - extra
    return np.array([bound] + given)


def uneven_parts(rng, amount, total, limit, slope):
    if amount == 2:
        one = jax.random.randint(rng, (), max(1, total - limit), min(limit, total - 1) + 1)
        return jnp.stack([one, total - one])
    sizes = jnp.asarray(profile(amount, total, limit, slope), jnp.int32)
    couples = (amount - 1) // 2
    giver, receiver = sizes[1:1 + 2 * couples:2], sizes[2:2 + 2 * couples:2]
    room = jnp.minimum(giver - 1, limit - receiver)
    shifted = jax.random.randint(jax.random.fold_in(rng, 1), (couples,), 0, 1 << 20) % (room + 1)
    sizes = sizes.at[1:1 + 2 * couples:2].set(giver - shifted).at[2:2 + 2 * couples:2].set(receiver + shifted)
    return sizes[jax.random.permutation(jax.random.fold_in(rng, 2), amount)]


def scatter_about(stream_key, dims, deviation, limit, shards=(), kind=jnp.bfloat16):
    level = steps_of(stream_key, dims, shards, -0.22, 0.18) if shards else 1.0
    values = jax.random.normal(stream_key, dims, jnp.float32) * deviation * level
    return jnp.minimum(jnp.maximum(values, -limit), limit).astype(kind)


def setup_inputs(seed: int = 0) -> dict:
    arg_keys = jax.random.split(jax.random.key(seed), 14)
    return {
        "tokens": scatter_about(arg_keys[0], (TOKENS, MODEL_WIDTH), 1.0, 6.0, ((0, 128),)),
        "norm_gain_pair": jnp.clip(1.0 + 0.1 * jax.random.normal(arg_keys[1], (2, MODEL_WIDTH), jnp.float32), 0.5, 1.5),
        "query_key_value_weight": draw_query_key_value_weight(jax.random.fold_in(arg_keys[13], 71), 0),
        "head_gate_weight": scatter_about(arg_keys[3], (2, MODEL_WIDTH, H), MODEL_WIDTH ** -0.5, 0.1875, ((2, 2),)),
        "decay_logit_bias": draw_decay_logit_bias(jax.random.fold_in(arg_keys[13], 71), 0),
        "adapter_down_factor": scatter_about(arg_keys[5], (ADAPTER_TOTAL, MODEL_WIDTH, ADAPTER_RANK), MODEL_WIDTH ** -0.5, 0.1875, ((0, 2),)),
        "adapter_up_factor": scatter_about(arg_keys[6], (ADAPTER_TOTAL, ADAPTER_RANK, MODEL_WIDTH), ADAPTER_RANK ** -0.5, 1.5, ((2, 2),)),
        "lengths": jax.vmap(lambda own: uneven_parts(own, SEQ_DEV, TOK_DEV, MOST, 2))(jax.random.split(arg_keys[7], N_REQ * N_COL)).reshape((N_REQ, N_COL, SEQ_DEV)).astype(jnp.int32),
        "request_adapter_index": place_ends(jax.random.randint(arg_keys[8], (N_REQ, SEQS), 0, ADAPTER_TOTAL), jax.random.fold_in(arg_keys[8], 1), 0, ADAPTER_TOTAL - 1).astype(jnp.int32),
        "request_cache_index": place_ends(jax.random.randint(arg_keys[9], (N_REQ, SEQS), 0, 2 * CACHES), jax.random.fold_in(arg_keys[9], 1), 0, (2 * CACHES) - 1).astype(jnp.int32),
        "caches": scatter_about(arg_keys[10], (CACHES, H, DH, DH), 1.0, 6.0, ((0, 64), (1, 2))),
        "head_output_weight": scatter_about(arg_keys[11], (MODEL_WIDTH, MODEL_WIDTH), MODEL_WIDTH ** -0.5, 0.1875, ((0, 2),)),
        "feedforward_weight": scatter_about(arg_keys[12], (3, MODEL_WIDTH, FF), MODEL_WIDTH ** -0.5, 0.1875, ((2, 2),)),
    }


epsilon = 1e-05

def rms_scale(values, gain):
    widened = values.astype(jnp.float32)
    factor = lax.rsqrt(lax.optimization_barrier(jnp.mean(widened * widened, axis=-1, keepdims=True)) + epsilon)
    return (widened * factor * gain).astype(jnp.bfloat16)

def reference(tokens, norm_gain_pair, query_key_value_weight, head_gate_weight, decay_logit_bias, adapter_down_factor, adapter_up_factor, lengths, request_adapter_index, request_cache_index, caches, head_output_weight, feedforward_weight):
    scale = 1.0 / math.sqrt(DH)

    def group_layer(inputs):
        group_rows, nested_lengths, grouped_adapter_rows, group_caches = inputs
        group_lengths = nested_lengths.reshape(SEQS).astype(jnp.int32)
        count = group_rows.shape[0]
        normalized_rows = rms_scale(group_rows, norm_gain_pair[0])
        positions = jnp.arange(count, dtype=jnp.int32)
        ends = jnp.cumsum(group_lengths).astype(jnp.int32)
        starts = (ends - group_lengths).astype(jnp.int32)
        member = ((positions[:, None] >= starts[None, :]) & (positions[:, None] < ends[None, :])).astype(jnp.float32)
        segment = lax.optimization_barrier(jnp.sum((positions[:, None] >= ends[None, :]).astype(jnp.int32), axis=1))
        proj_q = jnp.dot(normalized_rows, query_key_value_weight[0], preferred_element_type=jnp.float32)
        proj_k = jnp.dot(normalized_rows, query_key_value_weight[1], preferred_element_type=jnp.float32)
        proj_v = jnp.dot(normalized_rows, query_key_value_weight[2], preferred_element_type=jnp.float32)
        low_rank_delta = jnp.zeros((count, ADAPTER_RANK), jnp.float32)
        for request_number in range(SEQS):
            adapter_term = jnp.dot(normalized_rows, adapter_down_factor[grouped_adapter_rows[request_number]], preferred_element_type=jnp.float32)
            low_rank_delta = low_rank_delta + member[:, request_number:request_number + 1] * adapter_term
        low_rank_delta = low_rank_delta.astype(jnp.bfloat16)
        delta = jnp.zeros((count, MODEL_WIDTH), jnp.float32)
        for request_number in range(SEQS):
            adapter_term = jnp.dot(low_rank_delta, adapter_up_factor[grouped_adapter_rows[request_number]], preferred_element_type=jnp.float32)
            delta = delta + member[:, request_number:request_number + 1] * adapter_term
        queries = (proj_q + delta).astype(jnp.bfloat16)
        keys = proj_k.astype(jnp.bfloat16)
        values = proj_v.astype(jnp.bfloat16)
        log_keep = jax.nn.log_sigmoid(jnp.dot(normalized_rows, head_gate_weight[0], preferred_element_type=jnp.float32) + decay_logit_bias[None, :])
        mix_gate = jax.nn.sigmoid(jnp.dot(normalized_rows, head_gate_weight[1], preferred_element_type=jnp.float32))
        running = jnp.cumsum(log_keep, axis=0)
        before = running - log_keep
        start_level = before[starts]
        level = running - lax.optimization_barrier(jnp.sum(member[:, :, None] * start_level[None, :, :], axis=1))
        states = []
        for request_number in range(SEQS):
            ident = group_caches[request_number]
            picked = caches[jnp.minimum(ident, CACHES - 1)]
            states.append(jnp.where(ident < CACHES, picked, jnp.zeros_like(picked)))
        allowed = (segment[:, None] == segment[None, :]) & (positions[None, :] <= positions[:, None])
        outputs = []
        for head in range(H):
            cols = slice(head * DH, (head + 1) * DH)
            q_head = queries[:, cols]
            k_head = keys[:, cols]
            v_head = values[:, cols]
            scores = jnp.dot(q_head, k_head.T, preferred_element_type=jnp.float32) * scale
            masked = jnp.where(allowed, scores, -jnp.inf)
            peak = lax.optimization_barrier(jnp.max(masked, axis=1, keepdims=True))
            weights = jnp.exp(masked - peak)
            probs = (weights / lax.optimization_barrier(jnp.sum(weights, axis=1, keepdims=True))).astype(jnp.bfloat16)
            attended = jnp.dot(probs, v_head, preferred_element_type=jnp.float32)
            gap = jnp.where(allowed, running[:, head][:, None] - running[:, head][None, :], -jnp.inf)
            memory_w = (scores * jnp.exp(gap)).astype(jnp.bfloat16)
            intra = jnp.dot(memory_w, v_head, preferred_element_type=jnp.float32)
            carried = jnp.zeros((count, DH), jnp.float32)
            for request_number in range(SEQS):
                adapter_term = jnp.dot(q_head, states[request_number][head], preferred_element_type=jnp.float32)
                carried = carried + member[:, request_number:request_number + 1] * adapter_term
            recalled = carried * jnp.exp(level[:, head])[:, None] + intra
            factor = lax.rsqrt(lax.optimization_barrier(jnp.mean(recalled * recalled, axis=1, keepdims=True)) + epsilon)
            outputs.append(attended + mix_gate[:, head:head + 1] * recalled * factor)
        head_out = jnp.concatenate(outputs, axis=1).astype(jnp.bfloat16)
        projected = jnp.dot(head_out, head_output_weight, preferred_element_type=jnp.float32)
        mixed = (group_rows.astype(jnp.float32) + projected).astype(jnp.bfloat16)
        normed_two = rms_scale(mixed, norm_gain_pair[1])
        gate = jnp.dot(normed_two, feedforward_weight[0], preferred_element_type=jnp.float32)
        upper = jnp.dot(normed_two, feedforward_weight[1], preferred_element_type=jnp.float32)
        hidden = (jax.nn.silu(gate) * upper).astype(jnp.bfloat16)
        feed = jnp.dot(hidden, feedforward_weight[2].T, preferred_element_type=jnp.float32)
        return (mixed.astype(jnp.float32) + feed).astype(jnp.bfloat16)
    grouped = tokens.reshape(N_REQ, TOK_GRP, MODEL_WIDTH)
    result = lax.map(group_layer, (grouped, lengths, request_adapter_index, request_cache_index))
    return result.reshape(TOKENS, MODEL_WIDTH)
```

```python
import math

import jax
import jax.numpy as jnp
import numpy as np
from jax import lax
from jax.sharding import Mesh
from jax.sharding import PartitionSpec as P

epsilon = 1e-05
ROWS = ("z", "y", "x", "col")


def rms_scale(values, gain):
    widened = values.astype(jnp.float32)
    factor = lax.rsqrt(jnp.mean(widened * widened, axis=-1, keepdims=True) + epsilon)
    return (widened * factor * gain).astype(jnp.bfloat16)


def swap(value):
    return lax.ppermute(value, "col", perm=[(0, 1), (1, 0)])


def pair_rows(mine, other, col):
    first = jnp.where(col == 0, mine, other)
    second = jnp.where(col == 0, other, mine)
    return jnp.concatenate([first, second], axis=0)


def on_device(
    tokens,
    norm_gain_pair,
    query_key_value_weight,
    head_gate_weight,
    decay_logit_bias,
    adapter_down_factor,
    adapter_up_factor,
    lengths,
    request_adapter_index,
    request_cache_index,
    caches,
    head_output_weight,
    feedforward_weight,
):
    tok_rows, width = tokens.shape
    col = lax.axis_index("col")
    col_count = 2
    group = tok_rows * col_count
    head_cols = query_key_value_weight.shape[2]
    local_heads = head_gate_weight.shape[2]
    head_size = head_cols // local_heads
    group_lengths = lengths[0].reshape(-1)
    scale = 1.0 / math.sqrt(head_size)

    ff_other = swap(feedforward_weight)
    down_other = swap(adapter_down_factor)

    plane = lax.all_gather(caches, ("y", "x"), axis=0, tiled=True)
    per_plane = plane.shape[0]
    line_index = lax.all_gather(request_cache_index[0], "z", axis=0)
    local = line_index - lax.axis_index("z") * per_plane
    valid = (local >= 0) & (local < per_plane)
    picked = plane[jnp.clip(local, 0, per_plane - 1)]
    slots = jnp.where(valid[:, :, None, None, None], picked, jnp.zeros_like(picked))
    states = lax.psum_scatter(slots, "z", scatter_dimension=0, tiled=True)[0]

    normalized_rows = rms_scale(tokens, norm_gain_pair[0])
    gathered = pair_rows(normalized_rows, swap(normalized_rows), col)
    positions = jnp.arange(group, dtype=jnp.int32)
    ends = jnp.cumsum(group_lengths)
    starts = ends - group_lengths
    member = (
        (positions[:, None] >= starts[None, :]) & (positions[:, None] < ends[None, :])
    ).astype(jnp.float32)
    segment = jnp.sum((positions[:, None] >= ends[None, :]).astype(jnp.int32), axis=1)
    projected = jnp.einsum(
        "td,kdc->ktc", gathered, query_key_value_weight, preferred_element_type=jnp.float32
    )
    half_adapters = adapter_down_factor.shape[0]
    mine_numbers = col * half_adapters + jnp.arange(half_adapters, dtype=jnp.int32)
    other_numbers = (1 - col) * half_adapters + jnp.arange(half_adapters, dtype=jnp.int32)
    wanted = request_adapter_index[0][:, None]
    select_mine = (wanted == mine_numbers[None, :]).astype(jnp.bfloat16)
    select_other = (wanted == other_numbers[None, :]).astype(jnp.bfloat16)
    chosen = (
        jnp.einsum("sa,adr->sdr", select_mine, adapter_down_factor, preferred_element_type=jnp.float32)
        + jnp.einsum("sa,adr->sdr", select_other, down_other, preferred_element_type=jnp.float32)
    ).astype(jnp.bfloat16)
    per_request = jnp.einsum("td,sdr->tsr", gathered, chosen, preferred_element_type=jnp.float32)
    low_rank_delta = jnp.sum(member[:, :, None] * per_request, axis=1)
    low_rank_delta = low_rank_delta.astype(jnp.bfloat16)
    adapter_onehot = (
        request_adapter_index[0][:, None]
        == jnp.arange(adapter_up_factor.shape[0], dtype=jnp.int32)[None, :]
    ).astype(jnp.bfloat16)
    up_chosen = jnp.einsum(
        "gq,qjl->gjl", adapter_onehot, adapter_up_factor, preferred_element_type=jnp.float32
    ).astype(jnp.bfloat16)
    delta_all = jnp.einsum(
        "tr,src->tsc", low_rank_delta, up_chosen, preferred_element_type=jnp.float32
    )
    delta = jnp.sum(member[:, :, None] * delta_all, axis=1)
    queries = (projected[0] + delta).astype(jnp.bfloat16).reshape(group, local_heads, head_size)
    keys = projected[1].astype(jnp.bfloat16).reshape(group, local_heads, head_size)
    values = projected[2].astype(jnp.bfloat16).reshape(group, local_heads, head_size)
    gate_terms = jnp.einsum(
        "td,kdh->kth", gathered, head_gate_weight, preferred_element_type=jnp.float32
    )
    log_keep = jax.nn.log_sigmoid(gate_terms[0] + decay_logit_bias[None, :])
    mix_gate = jax.nn.sigmoid(gate_terms[1])
    running = jnp.cumsum(log_keep, axis=0)
    before = running - log_keep
    start_hot = (positions[None, :] == starts[:, None]).astype(jnp.float32)
    start_level = jnp.sum(start_hot[:, :, None] * before[None, :, :], axis=1)
    level = running - jnp.sum(member[:, :, None] * start_level[None, :, :], axis=1)
    from_state = jnp.einsum("thi,shij->tshj", queries, states, preferred_element_type=jnp.float32)
    carried = jnp.sum(member[:, :, None, None] * from_state, axis=1) * jnp.exp(level)[:, :, None]

    scores = jnp.einsum("qhd,khd->hqk", queries, keys, preferred_element_type=jnp.float32) * scale
    allowed = (segment[:, None] == segment[None, :]) & (positions[None, :] <= positions[:, None])
    masked = jnp.where(allowed[None], scores, -jnp.inf)
    peak = jnp.max(masked, axis=2, keepdims=True)
    weights = jnp.exp(masked - peak)
    probs = (weights / jnp.sum(weights, axis=2, keepdims=True)).astype(jnp.bfloat16)
    attended = jnp.einsum("hqk,khd->qhd", probs, values, preferred_element_type=jnp.float32)
    gap = jnp.where(allowed[None], running.T[:, :, None] - running.T[:, None, :], -jnp.inf)
    memory_w = (scores * jnp.exp(gap)).astype(jnp.bfloat16)
    recalled = jnp.einsum("hqk,khd->qhd", memory_w, values, preferred_element_type=jnp.float32)
    recalled = recalled + carried
    factor = lax.rsqrt(jnp.mean(recalled * recalled, axis=2, keepdims=True) + epsilon)
    combined = attended + mix_gate[:, :, None] * recalled * factor
    head_out = combined.astype(jnp.bfloat16).reshape(group, head_cols)

    partial = jnp.dot(head_out, head_output_weight, preferred_element_type=jnp.float32)
    own = lax.dynamic_slice_in_dim(partial, col * tok_rows, tok_rows, axis=0)
    sent = lax.dynamic_slice_in_dim(partial, (1 - col) * tok_rows, tok_rows, axis=0)
    attn_proj = own + swap(sent)
    mixed = (tokens.astype(jnp.float32) + attn_proj).astype(jnp.bfloat16)
    normed_two = rms_scale(mixed, norm_gain_pair[1])

    def feed_half(weight):
        gate_up = jnp.einsum(
            "td,kdf->ktf", normed_two, weight[:2], preferred_element_type=jnp.float32
        )
        hidden = (jax.nn.silu(gate_up[0]) * gate_up[1]).astype(jnp.bfloat16)
        return jnp.einsum("tf,df->td", hidden, weight[2], preferred_element_type=jnp.float32)

    feed = feed_half(feedforward_weight) + feed_half(ff_other)
    return (mixed.astype(jnp.float32) + feed).astype(jnp.bfloat16)


def solution(mesh):
    n_req = mesh.shape["req"]
    side = round(n_req ** (1.0 / 3.0))
    devices = np.asarray(mesh.devices).reshape(side, side, n_req // (side * side), mesh.shape["col"])
    grid = Mesh(devices, ROWS)
    placed = (
        P(ROWS, None),
        P(),
        P(None, None, "col"),
        P(None, None, "col"),
        P("col"),
        P("col", None, None),
        P(None, None, "col"),
        P(ROWS[:3], None, None),
        P(ROWS[:3], None),
        P(ROWS[:3], None),
        P(ROWS[:3], "col", None, None),
        P("col", None),
        P(None, None, "col"),
    )
    return jax.shard_map(
        on_device, mesh=grid, in_specs=placed, out_specs=P(ROWS, None), check_vma=False
    )
```

```python
import math

import jax
import jax.numpy as jnp
import numpy as np
from jax import lax
from jax.sharding import Mesh
from jax.sharding import PartitionSpec as P

epsilon = 1e-05
ROWS = ("z", "y", "x", "col")


def rms_scale(values, gain):
    widened = values.astype(jnp.float32)
    factor = lax.rsqrt(jnp.mean(widened * widened, axis=-1, keepdims=True) + epsilon)
    return (widened * factor * gain).astype(jnp.bfloat16)


def swap(value):
    return lax.ppermute(value, "col", perm=[(0, 1), (1, 0)])


def pair_rows(mine, other, col):
    first = jnp.where(col == 0, mine, other)
    second = jnp.where(col == 0, other, mine)
    return jnp.concatenate([first, second], axis=0)


def on_device(
    tokens,
    norm_gain_pair,
    query_key_value_weight,
    head_gate_weight,
    decay_logit_bias,
    adapter_down_factor,
    adapter_up_factor,
    lengths,
    request_adapter_index,
    request_cache_index,
    caches,
    head_output_weight,
    feedforward_weight,
):
    tok_rows, width = tokens.shape
    col = lax.axis_index("col")
    col_count = 2
    group = tok_rows * col_count
    head_cols = query_key_value_weight.shape[2]
    local_heads = head_gate_weight.shape[2]
    head_size = head_cols // local_heads
    group_lengths = lengths[0].reshape(-1)
    scale = 1.0 / math.sqrt(head_size)

    ff_other = swap(feedforward_weight)
    down_other = swap(adapter_down_factor)

    plane = lax.all_gather(caches, ("y", "x"), axis=0, tiled=True)
    per_plane = plane.shape[0]
    z_count = lax.axis_size("z")
    z_here = lax.axis_index("z")
    own_index = request_cache_index[0]
    shifts = range(1, z_count)
    shifted = {
        d: lax.ppermute(own_index, "z", perm=[(i, (i + d) % z_count) for i in range(z_count)])
        for d in shifts
    }

    def pick(index_row):
        local = index_row - z_here * per_plane
        valid = (local >= 0) & (local < per_plane)
        parts = []
        for j in range(index_row.shape[0]):
            one = lax.dynamic_index_in_dim(plane, jnp.clip(local[j], 0, per_plane - 1), 0, keepdims=False)
            parts.append(jnp.where(valid[j], one, jnp.zeros_like(one)))
        return jnp.stack(parts)

    ahead = {d: None for d in shifts}
    for d in shifts:
        ahead[d] = shifted[z_count - d]
    states = pick(own_index).astype(jnp.float32)
    for d in shifts:
        sent = pick(ahead[d])
        got = lax.ppermute(sent, "z", perm=[(i, (i + d) % z_count) for i in range(z_count)])
        states = states + got.astype(jnp.float32)
    states = states.astype(jnp.bfloat16)

    normalized_rows = rms_scale(tokens, norm_gain_pair[0])
    gathered = pair_rows(normalized_rows, swap(normalized_rows), col)
    positions = jnp.arange(group, dtype=jnp.int32)
    ends = jnp.cumsum(group_lengths)
    starts = ends - group_lengths
    member = (
        (positions[:, None] >= starts[None, :]) & (positions[:, None] < ends[None, :])
    ).astype(jnp.float32)
    segment = jnp.sum((positions[:, None] >= ends[None, :]).astype(jnp.int32), axis=1)
    projected = jnp.einsum(
        "td,kdc->ktc", gathered, query_key_value_weight, preferred_element_type=jnp.float32
    )
    half_adapters = adapter_down_factor.shape[0]
    mine_numbers = col * half_adapters + jnp.arange(half_adapters, dtype=jnp.int32)
    other_numbers = (1 - col) * half_adapters + jnp.arange(half_adapters, dtype=jnp.int32)
    wanted = request_adapter_index[0][:, None]
    select_mine = (wanted == mine_numbers[None, :]).astype(jnp.bfloat16)
    select_other = (wanted == other_numbers[None, :]).astype(jnp.bfloat16)
    chosen = (
        jnp.einsum("sa,adr->sdr", select_mine, adapter_down_factor, preferred_element_type=jnp.float32)
        + jnp.einsum("sa,adr->sdr", select_other, down_other, preferred_element_type=jnp.float32)
    ).astype(jnp.bfloat16)
    per_request = jnp.einsum("td,sdr->tsr", gathered, chosen, preferred_element_type=jnp.float32)
    low_rank_delta = jnp.sum(member[:, :, None] * per_request, axis=1)
    low_rank_delta = low_rank_delta.astype(jnp.bfloat16)
    adapter_onehot = (
        request_adapter_index[0][:, None]
        == jnp.arange(adapter_up_factor.shape[0], dtype=jnp.int32)[None, :]
    ).astype(jnp.bfloat16)
    up_chosen = jnp.einsum(
        "gq,qjl->gjl", adapter_onehot, adapter_up_factor, preferred_element_type=jnp.float32
    ).astype(jnp.bfloat16)
    delta_all = jnp.einsum(
        "tr,src->tsc", low_rank_delta, up_chosen, preferred_element_type=jnp.float32
    )
    delta = jnp.sum(member[:, :, None] * delta_all, axis=1)
    queries = (projected[0] + delta).astype(jnp.bfloat16).reshape(group, local_heads, head_size)
    keys = projected[1].astype(jnp.bfloat16).reshape(group, local_heads, head_size)
    values = projected[2].astype(jnp.bfloat16).reshape(group, local_heads, head_size)
    gate_terms = jnp.einsum(
        "td,kdh->kth", gathered, head_gate_weight, preferred_element_type=jnp.float32
    )
    log_keep = jax.nn.log_sigmoid(gate_terms[0] + decay_logit_bias[None, :])
    mix_gate = jax.nn.sigmoid(gate_terms[1])
    running = jnp.cumsum(log_keep, axis=0)
    before = running - log_keep
    start_hot = (positions[None, :] == starts[:, None]).astype(jnp.float32)
    start_level = jnp.sum(start_hot[:, :, None] * before[None, :, :], axis=1)
    level = running - jnp.sum(member[:, :, None] * start_level[None, :, :], axis=1)
    from_state = jnp.einsum("thi,shij->tshj", queries, states, preferred_element_type=jnp.float32)
    carried = jnp.sum(member[:, :, None, None] * from_state, axis=1) * jnp.exp(level)[:, :, None]

    scores = jnp.einsum("qhd,khd->hqk", queries, keys, preferred_element_type=jnp.float32) * scale
    allowed = (segment[:, None] == segment[None, :]) & (positions[None, :] <= positions[:, None])
    masked = jnp.where(allowed[None], scores, -jnp.inf)
    peak = jnp.max(masked, axis=2, keepdims=True)
    weights = jnp.exp(masked - peak)
    probs = (weights / jnp.sum(weights, axis=2, keepdims=True)).astype(jnp.bfloat16)
    attended = jnp.einsum("hqk,khd->qhd", probs, values, preferred_element_type=jnp.float32)
    gap = jnp.where(allowed[None], running.T[:, :, None] - running.T[:, None, :], -jnp.inf)
    memory_w = (scores * jnp.exp(gap)).astype(jnp.bfloat16)
    recalled = jnp.einsum("hqk,khd->qhd", memory_w, values, preferred_element_type=jnp.float32)
    recalled = recalled + carried
    factor = lax.rsqrt(jnp.mean(recalled * recalled, axis=2, keepdims=True) + epsilon)
    combined = attended + mix_gate[:, :, None] * recalled * factor
    head_out = combined.astype(jnp.bfloat16).reshape(group, head_cols)

    partial = jnp.dot(head_out, head_output_weight, preferred_element_type=jnp.float32)
    own = lax.dynamic_slice_in_dim(partial, col * tok_rows, tok_rows, axis=0)
    sent = lax.dynamic_slice_in_dim(partial, (1 - col) * tok_rows, tok_rows, axis=0)
    attn_proj = own + swap(sent)
    mixed = (tokens.astype(jnp.float32) + attn_proj).astype(jnp.bfloat16)
    normed_two = rms_scale(mixed, norm_gain_pair[1])

    def feed_half(weight):
        gate_up = jnp.einsum(
            "td,kdf->ktf", normed_two, weight[:2], preferred_element_type=jnp.float32
        )
        hidden = (jax.nn.silu(gate_up[0]) * gate_up[1]).astype(jnp.bfloat16)
        return jnp.einsum("tf,df->td", hidden, weight[2], preferred_element_type=jnp.float32)

    feed = feed_half(feedforward_weight) + feed_half(ff_other)
    return (mixed.astype(jnp.float32) + feed).astype(jnp.bfloat16)


def solution(mesh):
    n_req = mesh.shape["req"]
    side = round(n_req ** (1.0 / 3.0))
    devices = np.asarray(mesh.devices).reshape(side, side, n_req // (side * side), mesh.shape["col"])
    grid = Mesh(devices, ROWS)
    placed = (
        P(ROWS, None),
        P(),
        P(None, None, "col"),
        P(None, None, "col"),
        P("col"),
        P("col", None, None),
        P(None, None, "col"),
        P(ROWS[:3], None, None),
        P(ROWS[:3], None),
        P(ROWS[:3], None),
        P(ROWS[:3], "col", None, None),
        P("col", None),
        P(None, None, "col"),
    )
    return jax.shard_map(
        on_device, mesh=grid, in_specs=placed, out_specs=P(ROWS, None), check_vma=False
    )
```

```python
import math

import jax
import jax.numpy as jnp
import numpy as np
from jax import lax
from jax.sharding import Mesh
from jax.sharding import PartitionSpec as P

epsilon = 1e-05
ROWS = ("z", "y", "x", "col")


def rms_scale(values, gain):
    widened = values.astype(jnp.float32)
    factor = lax.rsqrt(jnp.mean(widened * widened, axis=-1, keepdims=True) + epsilon)
    return (widened * factor * gain).astype(jnp.bfloat16)


def swap(value):
    return lax.ppermute(value, "col", perm=[(0, 1), (1, 0)])


def pair_rows(mine, other, col):
    first = jnp.where(col == 0, mine, other)
    second = jnp.where(col == 0, other, mine)
    return jnp.concatenate([first, second], axis=0)


def on_device(
    tokens,
    norm_gain_pair,
    query_key_value_weight,
    head_gate_weight,
    decay_logit_bias,
    adapter_down_factor,
    adapter_up_factor,
    lengths,
    request_adapter_index,
    request_cache_index,
    caches,
    head_output_weight,
    feedforward_weight,
):
    tok_rows, width = tokens.shape
    col = lax.axis_index("col")
    col_count = 2
    group = tok_rows * col_count
    head_cols = query_key_value_weight.shape[2]
    local_heads = head_gate_weight.shape[2]
    head_size = head_cols // local_heads
    group_lengths = lengths[0].reshape(-1)
    scale = 1.0 / math.sqrt(head_size)

    ff_other = swap(feedforward_weight)
    down_other = swap(adapter_down_factor)

    z_count = lax.axis_size("z")
    z_here = lax.axis_index("z")
    own_index = request_cache_index[0]
    shifts = range(1, z_count)

    def along_z(value, d):
        return lax.ppermute(value, "z", perm=[(i, (i + d) % z_count) for i in range(z_count)])

    shifted = {d: along_z(own_index, d) for d in shifts}
    line_rows = jnp.stack([own_index] + [shifted[z_count - d] for d in shifts])
    per_plane = caches.shape[0] * lax.axis_size("y") * lax.axis_size("x")
    local = line_rows - z_here * per_plane
    onehot = (local[:, :, None] == jnp.arange(per_plane, dtype=jnp.int32)[None, None, :]).astype(
        jnp.bfloat16
    )
    chunk_count = 2
    chunk = caches.shape[1] // chunk_count
    state_parts = []
    for c in range(chunk_count):
        plane = lax.all_gather(caches[:, c * chunk:(c + 1) * chunk], ("y", "x"), axis=0, tiled=True)
        picked = jnp.einsum(
            "dsn,nhij->dshij", onehot, plane, preferred_element_type=jnp.float32
        ).astype(jnp.bfloat16)
        total = picked[0].astype(jnp.float32)
        for d in shifts:
            total = total + along_z(picked[d], d).astype(jnp.float32)
        state_parts.append(total.astype(jnp.bfloat16))
    states = jnp.concatenate(state_parts, axis=1)

    normalized_rows = rms_scale(tokens, norm_gain_pair[0])
    gathered = pair_rows(normalized_rows, swap(normalized_rows), col)
    positions = jnp.arange(group, dtype=jnp.int32)
    ends = jnp.cumsum(group_lengths)
    starts = ends - group_lengths
    member = (
        (positions[:, None] >= starts[None, :]) & (positions[:, None] < ends[None, :])
    ).astype(jnp.float32)
    segment = jnp.sum((positions[:, None] >= ends[None, :]).astype(jnp.int32), axis=1)
    projected = jnp.einsum(
        "td,kdc->ktc", gathered, query_key_value_weight, preferred_element_type=jnp.float32
    )
    half_adapters = adapter_down_factor.shape[0]
    mine_numbers = col * half_adapters + jnp.arange(half_adapters, dtype=jnp.int32)
    other_numbers = (1 - col) * half_adapters + jnp.arange(half_adapters, dtype=jnp.int32)
    wanted = request_adapter_index[0][:, None]
    select_mine = (wanted == mine_numbers[None, :]).astype(jnp.bfloat16)
    select_other = (wanted == other_numbers[None, :]).astype(jnp.bfloat16)
    chosen = (
        jnp.einsum("sa,adr->sdr", select_mine, adapter_down_factor, preferred_element_type=jnp.float32)
        + jnp.einsum("sa,adr->sdr", select_other, down_other, preferred_element_type=jnp.float32)
    ).astype(jnp.bfloat16)
    per_request = jnp.einsum("td,sdr->tsr", gathered, chosen, preferred_element_type=jnp.float32)
    low_rank_delta = jnp.sum(member[:, :, None] * per_request, axis=1)
    low_rank_delta = low_rank_delta.astype(jnp.bfloat16)
    adapter_onehot = (
        request_adapter_index[0][:, None]
        == jnp.arange(adapter_up_factor.shape[0], dtype=jnp.int32)[None, :]
    ).astype(jnp.bfloat16)
    up_chosen = jnp.einsum(
        "gq,qjl->gjl", adapter_onehot, adapter_up_factor, preferred_element_type=jnp.float32
    ).astype(jnp.bfloat16)
    delta_all = jnp.einsum(
        "tr,src->tsc", low_rank_delta, up_chosen, preferred_element_type=jnp.float32
    )
    delta = jnp.sum(member[:, :, None] * delta_all, axis=1)
    queries = (projected[0] + delta).astype(jnp.bfloat16).reshape(group, local_heads, head_size)
    keys = projected[1].astype(jnp.bfloat16).reshape(group, local_heads, head_size)
    values = projected[2].astype(jnp.bfloat16).reshape(group, local_heads, head_size)
    gate_terms = jnp.einsum(
        "td,kdh->kth", gathered, head_gate_weight, preferred_element_type=jnp.float32
    )
    log_keep = jax.nn.log_sigmoid(gate_terms[0] + decay_logit_bias[None, :])
    mix_gate = jax.nn.sigmoid(gate_terms[1])
    running = jnp.cumsum(log_keep, axis=0)
    before = running - log_keep
    start_hot = (positions[None, :] == starts[:, None]).astype(jnp.float32)
    start_level = jnp.sum(start_hot[:, :, None] * before[None, :, :], axis=1)
    level = running - jnp.sum(member[:, :, None] * start_level[None, :, :], axis=1)
    from_state = jnp.einsum("thi,shij->tshj", queries, states, preferred_element_type=jnp.float32)
    carried = jnp.sum(member[:, :, None, None] * from_state, axis=1) * jnp.exp(level)[:, :, None]

    scores = jnp.einsum("qhd,khd->hqk", queries, keys, preferred_element_type=jnp.float32) * scale
    allowed = (segment[:, None] == segment[None, :]) & (positions[None, :] <= positions[:, None])
    masked = jnp.where(allowed[None], scores, -jnp.inf)
    peak = jnp.max(masked, axis=2, keepdims=True)
    weights = jnp.exp(masked - peak)
    probs = (weights / jnp.sum(weights, axis=2, keepdims=True)).astype(jnp.bfloat16)
    attended = jnp.einsum("hqk,khd->qhd", probs, values, preferred_element_type=jnp.float32)
    gap = jnp.where(allowed[None], running.T[:, :, None] - running.T[:, None, :], -jnp.inf)
    memory_w = (scores * jnp.exp(gap)).astype(jnp.bfloat16)
    recalled = jnp.einsum("hqk,khd->qhd", memory_w, values, preferred_element_type=jnp.float32)
    recalled = recalled + carried
    factor = lax.rsqrt(jnp.mean(recalled * recalled, axis=2, keepdims=True) + epsilon)
    combined = attended + mix_gate[:, :, None] * recalled * factor
    head_out = combined.astype(jnp.bfloat16).reshape(group, head_cols)

    partial = jnp.dot(head_out, head_output_weight, preferred_element_type=jnp.float32)
    own = lax.dynamic_slice_in_dim(partial, col * tok_rows, tok_rows, axis=0)
    sent = lax.dynamic_slice_in_dim(partial, (1 - col) * tok_rows, tok_rows, axis=0)
    attn_proj = own + swap(sent)
    mixed = (tokens.astype(jnp.float32) + attn_proj).astype(jnp.bfloat16)
    normed_two = rms_scale(mixed, norm_gain_pair[1])

    def feed_half(weight):
        gate_up = jnp.einsum(
            "td,kdf->ktf", normed_two, weight[:2], preferred_element_type=jnp.float32
        )
        hidden = (jax.nn.silu(gate_up[0]) * gate_up[1]).astype(jnp.bfloat16)
        return jnp.einsum("tf,df->td", hidden, weight[2], preferred_element_type=jnp.float32)

    feed = feed_half(feedforward_weight) + feed_half(ff_other)
    return (mixed.astype(jnp.float32) + feed).astype(jnp.bfloat16)


def solution(mesh):
    n_req = mesh.shape["req"]
    side = round(n_req ** (1.0 / 3.0))
    devices = np.asarray(mesh.devices).reshape(side, side, n_req // (side * side), mesh.shape["col"])
    grid = Mesh(devices, ROWS)
    placed = (
        P(ROWS, None),
        P(),
        P(None, None, "col"),
        P(None, None, "col"),
        P("col"),
        P("col", None, None),
        P(None, None, "col"),
        P(ROWS[:3], None, None),
        P(ROWS[:3], None),
        P(ROWS[:3], None),
        P(ROWS[:3], "col", None, None),
        P("col", None),
        P(None, None, "col"),
    )
    return jax.shard_map(
        on_device, mesh=grid, in_specs=placed, out_specs=P(ROWS, None), check_vma=False
    )
```

```python
import math

import jax
import jax.numpy as jnp
import numpy as np
from jax import lax
from jax.experimental import pallas as pl
from jax.experimental.pallas import tpu as pltpu
from jax.sharding import Mesh
from jax.sharding import PartitionSpec as P

epsilon = 1e-05
ROWS = ("z", "y", "x", "col")


def rms_scale(values, gain):
    widened = values.astype(jnp.float32)
    factor = lax.rsqrt(jnp.mean(widened * widened, axis=-1, keepdims=True) + epsilon)
    return (widened * factor * gain).astype(jnp.bfloat16)


def swap(value):
    return lax.ppermute(value, "col", perm=[(0, 1), (1, 0)])


def pair_rows(mine, other, col):
    first = jnp.where(col == 0, mine, other)
    second = jnp.where(col == 0, other, mine)
    return jnp.concatenate([first, second], axis=0)


def pick_states(index, valid, plane, lines):
    slots = index.shape[0]
    per_line = slots // lines
    block = plane.shape[1:]

    def body(index_ref, valid_ref, plane_ref, *rest):
        outs = rest[:lines]
        zero_ref, sems = rest[lines:]
        zero_ref[...] = jnp.zeros(block, plane.dtype)
        for s in range(slots):
            dst = outs[s // per_line].at[s % per_line]

            @pl.when(valid_ref[s] != 0)
            def _():
                pltpu.make_async_copy(plane_ref.at[index_ref[s]], dst, sems.at[s]).start()

            @pl.when(valid_ref[s] == 0)
            def _():
                pltpu.make_async_copy(zero_ref, dst, sems.at[s]).start()

        for s in range(slots):
            dst = outs[s // per_line].at[s % per_line]
            pltpu.make_async_copy(zero_ref, dst, sems.at[s]).wait()

    out_shape = [jax.ShapeDtypeStruct((per_line,) + block, plane.dtype) for _ in range(lines)]
    return pl.pallas_call(
        body,
        out_shape=out_shape,
        grid_spec=pltpu.PrefetchScalarGridSpec(
            num_scalar_prefetch=2,
            grid=(),
            in_specs=[pl.BlockSpec(memory_space=pl.ANY)],
            out_specs=[pl.BlockSpec(memory_space=pl.ANY) for _ in range(lines)],
            scratch_shapes=[pltpu.VMEM(block, plane.dtype), pltpu.SemaphoreType.DMA((slots,))],
        ),
    )(index, valid, plane)


def on_device(
    tokens,
    norm_gain_pair,
    query_key_value_weight,
    head_gate_weight,
    decay_logit_bias,
    adapter_down_factor,
    adapter_up_factor,
    lengths,
    request_adapter_index,
    request_cache_index,
    caches,
    head_output_weight,
    feedforward_weight,
):
    tok_rows, width = tokens.shape
    col = lax.axis_index("col")
    col_count = 2
    group = tok_rows * col_count
    head_cols = query_key_value_weight.shape[2]
    local_heads = head_gate_weight.shape[2]
    head_size = head_cols // local_heads
    group_lengths = lengths[0].reshape(-1)
    scale = 1.0 / math.sqrt(head_size)

    ff_other = swap(feedforward_weight)
    down_other = swap(adapter_down_factor)

    plane = lax.all_gather(caches, ("y", "x"), axis=0, tiled=True)
    per_plane = plane.shape[0]
    z_count = lax.axis_size("z")
    z_here = lax.axis_index("z")
    own_index = request_cache_index[0]
    shifts = range(1, z_count)

    def along_z(value, d):
        return lax.ppermute(value, "z", perm=[(i, (i + d) % z_count) for i in range(z_count)])

    shifted = {d: along_z(own_index, d) for d in shifts}
    line_rows = jnp.stack([own_index] + [shifted[z_count - d] for d in shifts])
    local = line_rows - z_here * per_plane
    valid = ((local >= 0) & (local < per_plane)).astype(jnp.int32)
    picked = pick_states(jnp.clip(local, 0, per_plane - 1).reshape(-1), valid.reshape(-1), plane, z_count)
    states = picked[0].astype(jnp.float32)
    for d in shifts:
        states = states + along_z(picked[d], d).astype(jnp.float32)
    states = states.astype(jnp.bfloat16)

    normalized_rows = rms_scale(tokens, norm_gain_pair[0])
    gathered = pair_rows(normalized_rows, swap(normalized_rows), col)
    positions = jnp.arange(group, dtype=jnp.int32)
    ends = jnp.cumsum(group_lengths)
    starts = ends - group_lengths
    member = (
        (positions[:, None] >= starts[None, :]) & (positions[:, None] < ends[None, :])
    ).astype(jnp.float32)
    segment = jnp.sum((positions[:, None] >= ends[None, :]).astype(jnp.int32), axis=1)
    projected = jnp.einsum(
        "td,kdc->ktc", gathered, query_key_value_weight, preferred_element_type=jnp.float32
    )
    half_adapters = adapter_down_factor.shape[0]
    mine_numbers = col * half_adapters + jnp.arange(half_adapters, dtype=jnp.int32)
    other_numbers = (1 - col) * half_adapters + jnp.arange(half_adapters, dtype=jnp.int32)
    wanted = request_adapter_index[0][:, None]
    select_mine = (wanted == mine_numbers[None, :]).astype(jnp.bfloat16)
    select_other = (wanted == other_numbers[None, :]).astype(jnp.bfloat16)
    chosen = (
        jnp.einsum("sa,adr->sdr", select_mine, adapter_down_factor, preferred_element_type=jnp.float32)
        + jnp.einsum("sa,adr->sdr", select_other, down_other, preferred_element_type=jnp.float32)
    ).astype(jnp.bfloat16)
    per_request = jnp.einsum("td,sdr->tsr", gathered, chosen, preferred_element_type=jnp.float32)
    low_rank_delta = jnp.sum(member[:, :, None] * per_request, axis=1)
    low_rank_delta = low_rank_delta.astype(jnp.bfloat16)
    adapter_onehot = (
        request_adapter_index[0][:, None]
        == jnp.arange(adapter_up_factor.shape[0], dtype=jnp.int32)[None, :]
    ).astype(jnp.bfloat16)
    up_chosen = jnp.einsum(
        "gq,qjl->gjl", adapter_onehot, adapter_up_factor, preferred_element_type=jnp.float32
    ).astype(jnp.bfloat16)
    masked_low = low_rank_delta[:, None, :] * member.astype(jnp.bfloat16)[:, :, None]
    delta = jnp.einsum("tsr,src->tc", masked_low, up_chosen, preferred_element_type=jnp.float32)
    queries = (projected[0] + delta).astype(jnp.bfloat16).reshape(group, local_heads, head_size)
    keys = projected[1].astype(jnp.bfloat16).reshape(group, local_heads, head_size)
    values = projected[2].astype(jnp.bfloat16).reshape(group, local_heads, head_size)
    gate_terms = jnp.einsum(
        "td,kdh->kth", gathered, head_gate_weight, preferred_element_type=jnp.float32
    )
    log_keep = jax.nn.log_sigmoid(gate_terms[0] + decay_logit_bias[None, :])
    mix_gate = jax.nn.sigmoid(gate_terms[1])
    running = jnp.cumsum(log_keep, axis=0)
    before = running - log_keep
    start_hot = (positions[None, :] == starts[:, None]).astype(jnp.float32)
    start_level = jnp.sum(start_hot[:, :, None] * before[None, :, :], axis=1)
    level = running - jnp.sum(member[:, :, None] * start_level[None, :, :], axis=1)
    masked_queries = queries[:, None, :, :] * member.astype(jnp.bfloat16)[:, :, None, None]
    from_state = jnp.einsum(
        "tshi,shij->thj", masked_queries, states, preferred_element_type=jnp.float32
    )
    carried = from_state * jnp.exp(level)[:, :, None]

    scores = jnp.einsum("qhd,khd->hqk", queries, keys, preferred_element_type=jnp.float32) * scale
    allowed = (segment[:, None] == segment[None, :]) & (positions[None, :] <= positions[:, None])
    masked = jnp.where(allowed[None], scores, -jnp.inf)
    peak = jnp.max(masked, axis=2, keepdims=True)
    weights = jnp.exp(masked - peak)
    probs = (weights / jnp.sum(weights, axis=2, keepdims=True)).astype(jnp.bfloat16)
    attended = jnp.einsum("hqk,khd->qhd", probs, values, preferred_element_type=jnp.float32)
    gap = jnp.where(allowed[None], running.T[:, :, None] - running.T[:, None, :], -jnp.inf)
    memory_w = (scores * jnp.exp(gap)).astype(jnp.bfloat16)
    recalled = jnp.einsum("hqk,khd->qhd", memory_w, values, preferred_element_type=jnp.float32)
    recalled = recalled + carried
    factor = lax.rsqrt(jnp.mean(recalled * recalled, axis=2, keepdims=True) + epsilon)
    combined = attended + mix_gate[:, :, None] * recalled * factor
    head_out = combined.astype(jnp.bfloat16).reshape(group, head_cols)

    partial = jnp.dot(head_out, head_output_weight, preferred_element_type=jnp.float32)
    own = lax.dynamic_slice_in_dim(partial, col * tok_rows, tok_rows, axis=0)
    sent = lax.dynamic_slice_in_dim(partial, (1 - col) * tok_rows, tok_rows, axis=0)
    attn_proj = own + swap(sent)
    mixed = (tokens.astype(jnp.float32) + attn_proj).astype(jnp.bfloat16)
    normed_two = rms_scale(mixed, norm_gain_pair[1])

    def feed_half(weight):
        gate_up = jnp.einsum(
            "td,kdf->ktf", normed_two, weight[:2], preferred_element_type=jnp.float32
        )
        hidden = (jax.nn.silu(gate_up[0]) * gate_up[1]).astype(jnp.bfloat16)
        return jnp.einsum("tf,df->td", hidden, weight[2], preferred_element_type=jnp.float32)

    feed = feed_half(feedforward_weight) + feed_half(ff_other)
    return (mixed.astype(jnp.float32) + feed).astype(jnp.bfloat16)


def solution(mesh):
    n_req = mesh.shape["req"]
    side = round(n_req ** (1.0 / 3.0))
    devices = np.asarray(mesh.devices).reshape(side, side, n_req // (side * side), mesh.shape["col"])
    grid = Mesh(devices, ROWS)
    placed = (
        P(ROWS, None),
        P(),
        P(None, None, "col"),
        P(None, None, "col"),
        P("col"),
        P("col", None, None),
        P(None, None, "col"),
        P(ROWS[:3], None, None),
        P(ROWS[:3], None),
        P(ROWS[:3], None),
        P(ROWS[:3], "col", None, None),
        P("col", None),
        P(None, None, "col"),
    )
    return jax.shard_map(
        on_device, mesh=grid, in_specs=placed, out_specs=P(ROWS, None), check_vma=False
    )
```

```python
import math

import jax
import jax.numpy as jnp
import numpy as np
from jax import lax
from jax.experimental import pallas as pl
from jax.experimental.pallas import tpu as pltpu
from jax.sharding import Mesh
from jax.sharding import PartitionSpec as P

epsilon = 1e-05
ROWS = ("z", "y", "x", "col")


def rms_scale(values, gain):
    widened = values.astype(jnp.float32)
    factor = lax.rsqrt(jnp.mean(widened * widened, axis=-1, keepdims=True) + epsilon)
    return (widened * factor * gain).astype(jnp.bfloat16)


def swap(value):
    return lax.ppermute(value, "col", perm=[(0, 1), (1, 0)])


def pair_rows(mine, other, col):
    first = jnp.where(col == 0, mine, other)
    second = jnp.where(col == 0, other, mine)
    return jnp.concatenate([first, second], axis=0)


def pick_states(index, valid, plane, lines):
    slots = index.shape[0]
    per_line = slots // lines
    block = plane.shape[1:]

    def body(index_ref, valid_ref, plane_ref, *rest):
        outs = rest[:lines]
        zero_ref, sems = rest[lines:]
        zero_ref[...] = jnp.zeros(block, plane.dtype)
        for s in range(slots):
            dst = outs[s // per_line].at[s % per_line]

            @pl.when(valid_ref[s] != 0)
            def _():
                pltpu.make_async_copy(plane_ref.at[index_ref[s]], dst, sems.at[s]).start()

            @pl.when(valid_ref[s] == 0)
            def _():
                pltpu.make_async_copy(zero_ref, dst, sems.at[s]).start()

        for s in range(slots):
            dst = outs[s // per_line].at[s % per_line]
            pltpu.make_async_copy(zero_ref, dst, sems.at[s]).wait()

    out_shape = [jax.ShapeDtypeStruct((per_line,) + block, plane.dtype) for _ in range(lines)]
    return pl.pallas_call(
        body,
        out_shape=out_shape,
        grid_spec=pltpu.PrefetchScalarGridSpec(
            num_scalar_prefetch=2,
            grid=(),
            in_specs=[pl.BlockSpec(memory_space=pl.ANY)],
            out_specs=[pl.BlockSpec(memory_space=pl.ANY) for _ in range(lines)],
            scratch_shapes=[pltpu.VMEM(block, plane.dtype), pltpu.SemaphoreType.DMA((slots,))],
        ),
    )(index, valid, plane)


def on_device(
    tokens,
    norm_gain_pair,
    query_key_value_weight,
    head_gate_weight,
    decay_logit_bias,
    adapter_down_factor,
    adapter_up_factor,
    lengths,
    request_adapter_index,
    request_cache_index,
    caches,
    head_output_weight,
    feedforward_weight,
):
    tok_rows, width = tokens.shape
    col = lax.axis_index("col")
    col_count = 2
    group = tok_rows * col_count
    head_cols = query_key_value_weight.shape[2]
    local_heads = head_gate_weight.shape[2]
    head_size = head_cols // local_heads
    group_lengths = lengths[0].reshape(-1)
    scale = 1.0 / math.sqrt(head_size)

    down_other = swap(adapter_down_factor)

    plane = lax.all_gather(caches, ("y", "x"), axis=0, tiled=True)
    per_plane = plane.shape[0]
    z_count = lax.axis_size("z")
    z_here = lax.axis_index("z")
    own_index = request_cache_index[0]
    shifts = range(1, z_count)

    def along_z(value, d):
        return lax.ppermute(value, "z", perm=[(i, (i + d) % z_count) for i in range(z_count)])

    shifted = {d: along_z(own_index, d) for d in shifts}
    line_rows = jnp.stack([own_index] + [shifted[z_count - d] for d in shifts])
    local = line_rows - z_here * per_plane
    valid = ((local >= 0) & (local < per_plane)).astype(jnp.int32)
    picked = pick_states(jnp.clip(local, 0, per_plane - 1).reshape(-1), valid.reshape(-1), plane, z_count)
    states = picked[0].astype(jnp.float32)
    for d in shifts:
        states = states + along_z(picked[d], d).astype(jnp.float32)
    states = states.astype(jnp.bfloat16)

    normalized_rows = rms_scale(tokens, norm_gain_pair[0])
    gathered = pair_rows(normalized_rows, swap(normalized_rows), col)
    positions = jnp.arange(group, dtype=jnp.int32)
    ends = jnp.cumsum(group_lengths)
    starts = ends - group_lengths
    member = (
        (positions[:, None] >= starts[None, :]) & (positions[:, None] < ends[None, :])
    ).astype(jnp.float32)
    segment = jnp.sum((positions[:, None] >= ends[None, :]).astype(jnp.int32), axis=1)
    projected = jnp.einsum(
        "td,kdc->ktc", gathered, query_key_value_weight, preferred_element_type=jnp.float32
    )
    half_adapters = adapter_down_factor.shape[0]
    mine_numbers = col * half_adapters + jnp.arange(half_adapters, dtype=jnp.int32)
    other_numbers = (1 - col) * half_adapters + jnp.arange(half_adapters, dtype=jnp.int32)
    wanted = request_adapter_index[0][:, None]
    select_mine = (wanted == mine_numbers[None, :]).astype(jnp.bfloat16)
    select_other = (wanted == other_numbers[None, :]).astype(jnp.bfloat16)
    chosen = (
        jnp.einsum("sa,adr->sdr", select_mine, adapter_down_factor, preferred_element_type=jnp.float32)
        + jnp.einsum("sa,adr->sdr", select_other, down_other, preferred_element_type=jnp.float32)
    ).astype(jnp.bfloat16)
    per_request = jnp.einsum("td,sdr->tsr", gathered, chosen, preferred_element_type=jnp.float32)
    low_rank_delta = jnp.sum(member[:, :, None] * per_request, axis=1)
    low_rank_delta = low_rank_delta.astype(jnp.bfloat16)
    adapter_onehot = (
        request_adapter_index[0][:, None]
        == jnp.arange(adapter_up_factor.shape[0], dtype=jnp.int32)[None, :]
    ).astype(jnp.bfloat16)
    up_chosen = jnp.einsum(
        "gq,qjl->gjl", adapter_onehot, adapter_up_factor, preferred_element_type=jnp.float32
    ).astype(jnp.bfloat16)
    masked_low = low_rank_delta[:, None, :] * member.astype(jnp.bfloat16)[:, :, None]
    delta = jnp.einsum("tsr,src->tc", masked_low, up_chosen, preferred_element_type=jnp.float32)
    queries = (projected[0] + delta).astype(jnp.bfloat16).reshape(group, local_heads, head_size)
    keys = projected[1].astype(jnp.bfloat16).reshape(group, local_heads, head_size)
    values = projected[2].astype(jnp.bfloat16).reshape(group, local_heads, head_size)
    gate_terms = jnp.einsum(
        "td,kdh->kth", gathered, head_gate_weight, preferred_element_type=jnp.float32
    )
    log_keep = jax.nn.log_sigmoid(gate_terms[0] + decay_logit_bias[None, :])
    mix_gate = jax.nn.sigmoid(gate_terms[1])
    running = jnp.cumsum(log_keep, axis=0)
    before = running - log_keep
    start_hot = (positions[None, :] == starts[:, None]).astype(jnp.float32)
    start_level = jnp.sum(start_hot[:, :, None] * before[None, :, :], axis=1)
    level = running - jnp.sum(member[:, :, None] * start_level[None, :, :], axis=1)
    masked_queries = queries[:, None, :, :] * member.astype(jnp.bfloat16)[:, :, None, None]
    from_state = jnp.einsum(
        "tshi,shij->thj", masked_queries, states, preferred_element_type=jnp.float32
    )
    carried = from_state * jnp.exp(level)[:, :, None]

    scores = jnp.einsum("qhd,khd->hqk", queries, keys, preferred_element_type=jnp.float32) * scale
    allowed = (segment[:, None] == segment[None, :]) & (positions[None, :] <= positions[:, None])
    masked = jnp.where(allowed[None], scores, -jnp.inf)
    peak = jnp.max(masked, axis=2, keepdims=True)
    weights = jnp.exp(masked - peak)
    probs = (weights / jnp.sum(weights, axis=2, keepdims=True)).astype(jnp.bfloat16)
    attended = jnp.einsum("hqk,khd->qhd", probs, values, preferred_element_type=jnp.float32)
    gap = jnp.where(allowed[None], running.T[:, :, None] - running.T[:, None, :], -jnp.inf)
    memory_w = (scores * jnp.exp(gap)).astype(jnp.bfloat16)
    recalled = jnp.einsum("hqk,khd->qhd", memory_w, values, preferred_element_type=jnp.float32)
    recalled = recalled + carried
    factor = lax.rsqrt(jnp.mean(recalled * recalled, axis=2, keepdims=True) + epsilon)
    combined = attended + mix_gate[:, :, None] * recalled * factor
    head_out = combined.astype(jnp.bfloat16).reshape(group, head_cols)

    partial = jnp.dot(head_out, head_output_weight, preferred_element_type=jnp.float32)
    own = lax.dynamic_slice_in_dim(partial, col * tok_rows, tok_rows, axis=0)
    sent = lax.dynamic_slice_in_dim(partial, (1 - col) * tok_rows, tok_rows, axis=0)
    attn_proj = own + swap(sent)
    mixed = (tokens.astype(jnp.float32) + attn_proj).astype(jnp.bfloat16)
    normed_two = rms_scale(mixed, norm_gain_pair[1])

    def feed_half(weight):
        gate_up = jnp.einsum(
            "td,kdf->ktf", normed_two, weight[:2], preferred_element_type=jnp.float32
        )
        hidden = (jax.nn.silu(gate_up[0]) * gate_up[1]).astype(jnp.bfloat16)
        return jnp.einsum("tf,df->td", hidden, weight[2], preferred_element_type=jnp.float32)

    feed = feed_half(lax.all_gather(feedforward_weight, "col", axis=2, tiled=True))
    return (mixed.astype(jnp.float32) + feed).astype(jnp.bfloat16)


def solution(mesh):
    n_req = mesh.shape["req"]
    side = round(n_req ** (1.0 / 3.0))
    devices = np.asarray(mesh.devices).reshape(side, side, n_req // (side * side), mesh.shape["col"])
    grid = Mesh(devices, ROWS)
    placed = (
        P(ROWS, None),
        P(),
        P(None, None, "col"),
        P(None, None, "col"),
        P("col"),
        P("col", None, None),
        P(None, None, "col"),
        P(ROWS[:3], None, None),
        P(ROWS[:3], None),
        P(ROWS[:3], None),
        P(ROWS[:3], "col", None, None),
        P("col", None),
        P(None, None, "col"),
    )
    return jax.shard_map(
        on_device, mesh=grid, in_specs=placed, out_specs=P(ROWS, None), check_vma=False
    )
```

```python
import math

import jax
import jax.numpy as jnp
import numpy as np
from jax import lax
from jax.experimental import pallas as pl
from jax.experimental.pallas import tpu as pltpu
from jax.sharding import Mesh
from jax.sharding import PartitionSpec as P

epsilon = 1e-05
ROWS = ("z", "y", "x", "col")


def rms_scale(values, gain):
    widened = values.astype(jnp.float32)
    factor = lax.rsqrt(jnp.mean(widened * widened, axis=-1, keepdims=True) + epsilon)
    return (widened * factor * gain).astype(jnp.bfloat16)


def swap(value):
    return lax.ppermute(value, "col", perm=[(0, 1), (1, 0)])


def pair_rows(mine, other, col):
    first = jnp.where(col == 0, mine, other)
    second = jnp.where(col == 0, other, mine)
    return jnp.concatenate([first, second], axis=0)


def pick_states(index, valid, plane, lines):
    slots = index.shape[0]
    per_line = slots // lines
    block = plane.shape[1:]

    def body(index_ref, valid_ref, plane_ref, *rest):
        outs = rest[:lines]
        zero_ref, sems = rest[lines:]
        zero_ref[...] = jnp.zeros(block, plane.dtype)
        for s in range(slots):
            dst = outs[s // per_line].at[s % per_line]

            @pl.when(valid_ref[s] != 0)
            def _():
                pltpu.make_async_copy(plane_ref.at[index_ref[s]], dst, sems.at[s]).start()

            @pl.when(valid_ref[s] == 0)
            def _():
                pltpu.make_async_copy(zero_ref, dst, sems.at[s]).start()

        for s in range(slots):
            dst = outs[s // per_line].at[s % per_line]
            pltpu.make_async_copy(zero_ref, dst, sems.at[s]).wait()

    out_shape = [jax.ShapeDtypeStruct((per_line,) + block, plane.dtype) for _ in range(lines)]
    return pl.pallas_call(
        body,
        out_shape=out_shape,
        grid_spec=pltpu.PrefetchScalarGridSpec(
            num_scalar_prefetch=2,
            grid=(),
            in_specs=[pl.BlockSpec(memory_space=pl.ANY)],
            out_specs=[pl.BlockSpec(memory_space=pl.ANY) for _ in range(lines)],
            scratch_shapes=[pltpu.VMEM(block, plane.dtype), pltpu.SemaphoreType.DMA((slots,))],
        ),
    )(index, valid, plane)


def on_device(
    tokens,
    norm_gain_pair,
    query_key_value_weight,
    head_gate_weight,
    decay_logit_bias,
    adapter_down_factor,
    adapter_up_factor,
    lengths,
    request_adapter_index,
    request_cache_index,
    caches,
    head_output_weight,
    feedforward_weight,
):
    tok_rows, width = tokens.shape
    col = lax.axis_index("col")
    col_count = 2
    group = tok_rows * col_count
    head_cols = query_key_value_weight.shape[2]
    local_heads = head_gate_weight.shape[2]
    head_size = head_cols // local_heads
    group_lengths = lengths[0].reshape(-1)
    scale = 1.0 / math.sqrt(head_size)

    down_other = swap(adapter_down_factor)

    plane = lax.all_gather(caches, ("y", "x"), axis=0, tiled=True)
    per_plane = plane.shape[0]

    normalized_rows = rms_scale(tokens, norm_gain_pair[0])
    gathered = pair_rows(normalized_rows, swap(normalized_rows), col)
    positions = jnp.arange(group, dtype=jnp.int32)
    ends = jnp.cumsum(group_lengths)
    starts = ends - group_lengths
    member = (
        (positions[:, None] >= starts[None, :]) & (positions[:, None] < ends[None, :])
    ).astype(jnp.float32)
    segment = jnp.sum((positions[:, None] >= ends[None, :]).astype(jnp.int32), axis=1)
    projected = jnp.einsum(
        "td,kdc->ktc", gathered, query_key_value_weight, preferred_element_type=jnp.float32
    )
    half_adapters = adapter_down_factor.shape[0]
    mine_numbers = col * half_adapters + jnp.arange(half_adapters, dtype=jnp.int32)
    other_numbers = (1 - col) * half_adapters + jnp.arange(half_adapters, dtype=jnp.int32)
    wanted = request_adapter_index[0][:, None]
    select_mine = (wanted == mine_numbers[None, :]).astype(jnp.bfloat16)
    select_other = (wanted == other_numbers[None, :]).astype(jnp.bfloat16)
    chosen = (
        jnp.einsum("sa,adr->sdr", select_mine, adapter_down_factor, preferred_element_type=jnp.float32)
        + jnp.einsum("sa,adr->sdr", select_other, down_other, preferred_element_type=jnp.float32)
    ).astype(jnp.bfloat16)
    per_request = jnp.einsum("td,sdr->tsr", gathered, chosen, preferred_element_type=jnp.float32)
    low_rank_delta = jnp.sum(member[:, :, None] * per_request, axis=1)
    low_rank_delta = low_rank_delta.astype(jnp.bfloat16)
    adapter_onehot = (
        request_adapter_index[0][:, None]
        == jnp.arange(adapter_up_factor.shape[0], dtype=jnp.int32)[None, :]
    ).astype(jnp.bfloat16)
    up_chosen = jnp.einsum(
        "gq,qjl->gjl", adapter_onehot, adapter_up_factor, preferred_element_type=jnp.float32
    ).astype(jnp.bfloat16)
    masked_low = low_rank_delta[:, None, :] * member.astype(jnp.bfloat16)[:, :, None]
    delta = jnp.einsum("tsr,src->tc", masked_low, up_chosen, preferred_element_type=jnp.float32)
    queries = (projected[0] + delta).astype(jnp.bfloat16).reshape(group, local_heads, head_size)
    plane, queries = lax.optimization_barrier((plane, queries))
    z_count = lax.axis_size("z")
    z_here = lax.axis_index("z")
    own_index = request_cache_index[0]
    shifts = range(1, z_count)

    def along_z(value, d):
        return lax.ppermute(value, "z", perm=[(i, (i + d) % z_count) for i in range(z_count)])

    shifted = {d: along_z(own_index, d) for d in shifts}
    line_rows = jnp.stack([own_index] + [shifted[z_count - d] for d in shifts])
    local = line_rows - z_here * per_plane
    valid = ((local >= 0) & (local < per_plane)).astype(jnp.int32)
    picked = pick_states(jnp.clip(local, 0, per_plane - 1).reshape(-1), valid.reshape(-1), plane, z_count)
    ff_weight, _ = lax.optimization_barrier((feedforward_weight, picked[-1]))
    states = picked[0].astype(jnp.float32)
    for d in shifts:
        states = states + along_z(picked[d], d).astype(jnp.float32)
    states = states.astype(jnp.bfloat16)
    keys = projected[1].astype(jnp.bfloat16).reshape(group, local_heads, head_size)
    values = projected[2].astype(jnp.bfloat16).reshape(group, local_heads, head_size)
    gate_terms = jnp.einsum(
        "td,kdh->kth", gathered, head_gate_weight, preferred_element_type=jnp.float32
    )
    log_keep = jax.nn.log_sigmoid(gate_terms[0] + decay_logit_bias[None, :])
    mix_gate = jax.nn.sigmoid(gate_terms[1])
    running = jnp.cumsum(log_keep, axis=0)
    before = running - log_keep
    start_hot = (positions[None, :] == starts[:, None]).astype(jnp.float32)
    start_level = jnp.sum(start_hot[:, :, None] * before[None, :, :], axis=1)
    level = running - jnp.sum(member[:, :, None] * start_level[None, :, :], axis=1)
    masked_queries = queries[:, None, :, :] * member.astype(jnp.bfloat16)[:, :, None, None]
    from_state = jnp.einsum(
        "tshi,shij->thj", masked_queries, states, preferred_element_type=jnp.float32
    )
    carried = from_state * jnp.exp(level)[:, :, None]

    scores = jnp.einsum("qhd,khd->hqk", queries, keys, preferred_element_type=jnp.float32) * scale
    allowed = (segment[:, None] == segment[None, :]) & (positions[None, :] <= positions[:, None])
    masked = jnp.where(allowed[None], scores, -jnp.inf)
    peak = jnp.max(masked, axis=2, keepdims=True)
    weights = jnp.exp(masked - peak)
    probs = (weights / jnp.sum(weights, axis=2, keepdims=True)).astype(jnp.bfloat16)
    attended = jnp.einsum("hqk,khd->qhd", probs, values, preferred_element_type=jnp.float32)
    gap = jnp.where(allowed[None], running.T[:, :, None] - running.T[:, None, :], -jnp.inf)
    memory_w = (scores * jnp.exp(gap)).astype(jnp.bfloat16)
    recalled = jnp.einsum("hqk,khd->qhd", memory_w, values, preferred_element_type=jnp.float32)
    recalled = recalled + carried
    factor = lax.rsqrt(jnp.mean(recalled * recalled, axis=2, keepdims=True) + epsilon)
    combined = attended + mix_gate[:, :, None] * recalled * factor
    head_out = combined.astype(jnp.bfloat16).reshape(group, head_cols)

    partial = jnp.dot(head_out, head_output_weight, preferred_element_type=jnp.float32)
    own = lax.dynamic_slice_in_dim(partial, col * tok_rows, tok_rows, axis=0)
    sent = lax.dynamic_slice_in_dim(partial, (1 - col) * tok_rows, tok_rows, axis=0)
    attn_proj = own + swap(sent)
    mixed = (tokens.astype(jnp.float32) + attn_proj).astype(jnp.bfloat16)
    normed_two = rms_scale(mixed, norm_gain_pair[1])

    def feed_half(weight):
        gate_up = jnp.einsum(
            "td,kdf->ktf", normed_two, weight[:2], preferred_element_type=jnp.float32
        )
        hidden = (jax.nn.silu(gate_up[0]) * gate_up[1]).astype(jnp.bfloat16)
        return jnp.einsum("tf,df->td", hidden, weight[2], preferred_element_type=jnp.float32)

    feed = feed_half(lax.all_gather(ff_weight, "col", axis=2, tiled=True))
    return (mixed.astype(jnp.float32) + feed).astype(jnp.bfloat16)


def solution(mesh):
    n_req = mesh.shape["req"]
    side = round(n_req ** (1.0 / 3.0))
    devices = np.asarray(mesh.devices).reshape(side, side, n_req // (side * side), mesh.shape["col"])
    grid = Mesh(devices, ROWS)
    placed = (
        P(ROWS, None),
        P(),
        P(None, None, "col"),
        P(None, None, "col"),
        P("col"),
        P("col", None, None),
        P(None, None, "col"),
        P(ROWS[:3], None, None),
        P(ROWS[:3], None),
        P(ROWS[:3], None),
        P(ROWS[:3], "col", None, None),
        P("col", None),
        P(None, None, "col"),
    )
    return jax.shard_map(
        on_device, mesh=grid, in_specs=placed, out_specs=P(ROWS, None), check_vma=False
    )
```

```python
import math

import jax
import jax.numpy as jnp
import numpy as np
from jax import lax
from jax.experimental import pallas as pl
from jax.experimental.pallas import tpu as pltpu
from jax.sharding import Mesh
from jax.sharding import PartitionSpec as P

epsilon = 1e-05
ROWS = ("z", "y", "x", "col")


def rms_scale(values, gain):
    widened = values.astype(jnp.float32)
    factor = lax.rsqrt(jnp.mean(widened * widened, axis=-1, keepdims=True) + epsilon)
    return (widened * factor * gain).astype(jnp.bfloat16)


def swap(value):
    return lax.ppermute(value, "col", perm=[(0, 1), (1, 0)])


def pair_rows(mine, other, col):
    first = jnp.where(col == 0, mine, other)
    second = jnp.where(col == 0, other, mine)
    return jnp.concatenate([first, second], axis=0)


def pick_states(index, valid, plane, lines):
    slots = index.shape[0]
    per_line = slots // lines
    block = plane.shape[1:]

    def body(index_ref, valid_ref, plane_ref, out_ref, zero_ref, sems):
        zero_ref[...] = jnp.zeros(block, plane.dtype)
        for s in range(slots):
            dst = out_ref.at[s // per_line, s % per_line]

            @pl.when(valid_ref[s] != 0)
            def _():
                pltpu.make_async_copy(plane_ref.at[index_ref[s]], dst, sems.at[s]).start()

            @pl.when(valid_ref[s] == 0)
            def _():
                pltpu.make_async_copy(zero_ref, dst, sems.at[s]).start()

        for s in range(slots):
            dst = out_ref.at[s // per_line, s % per_line]
            pltpu.make_async_copy(zero_ref, dst, sems.at[s]).wait()

    return pl.pallas_call(
        body,
        out_shape=jax.ShapeDtypeStruct((lines, per_line) + block, plane.dtype),
        grid_spec=pltpu.PrefetchScalarGridSpec(
            num_scalar_prefetch=2,
            grid=(),
            in_specs=[pl.BlockSpec(memory_space=pl.ANY)],
            out_specs=pl.BlockSpec(memory_space=pl.ANY),
            scratch_shapes=[pltpu.VMEM(block, plane.dtype), pltpu.SemaphoreType.DMA((slots,))],
        ),
    )(index, valid, plane)


def on_device(
    tokens,
    norm_gain_pair,
    query_key_value_weight,
    head_gate_weight,
    decay_logit_bias,
    adapter_down_factor,
    adapter_up_factor,
    lengths,
    request_adapter_index,
    request_cache_index,
    caches,
    head_output_weight,
    feedforward_weight,
):
    tok_rows, width = tokens.shape
    col = lax.axis_index("col")
    col_count = 2
    group = tok_rows * col_count
    head_cols = query_key_value_weight.shape[2]
    local_heads = head_gate_weight.shape[2]
    head_size = head_cols // local_heads
    group_lengths = lengths[0].reshape(-1)
    scale = 1.0 / math.sqrt(head_size)

    ff_other = swap(feedforward_weight)
    down_other = swap(adapter_down_factor)

    plane = lax.all_gather(caches, ("y", "x"), axis=0, tiled=True)
    per_plane = plane.shape[0]

    normalized_rows = rms_scale(tokens, norm_gain_pair[0])
    gathered = pair_rows(normalized_rows, swap(normalized_rows), col)
    positions = jnp.arange(group, dtype=jnp.int32)
    ends = jnp.cumsum(group_lengths)
    starts = ends - group_lengths
    member = (
        (positions[:, None] >= starts[None, :]) & (positions[:, None] < ends[None, :])
    ).astype(jnp.float32)
    segment = jnp.sum((positions[:, None] >= ends[None, :]).astype(jnp.int32), axis=1)
    projected = jnp.einsum(
        "td,kdc->ktc", gathered, query_key_value_weight, preferred_element_type=jnp.float32
    )
    half_adapters = adapter_down_factor.shape[0]
    mine_numbers = col * half_adapters + jnp.arange(half_adapters, dtype=jnp.int32)
    other_numbers = (1 - col) * half_adapters + jnp.arange(half_adapters, dtype=jnp.int32)
    wanted = request_adapter_index[0][:, None]
    select_mine = (wanted == mine_numbers[None, :]).astype(jnp.bfloat16)
    select_other = (wanted == other_numbers[None, :]).astype(jnp.bfloat16)
    chosen = (
        jnp.einsum("sa,adr->sdr", select_mine, adapter_down_factor, preferred_element_type=jnp.float32)
        + jnp.einsum("sa,adr->sdr", select_other, down_other, preferred_element_type=jnp.float32)
    ).astype(jnp.bfloat16)
    per_request = jnp.einsum("td,sdr->tsr", gathered, chosen, preferred_element_type=jnp.float32)
    low_rank_delta = jnp.sum(member[:, :, None] * per_request, axis=1)
    low_rank_delta = low_rank_delta.astype(jnp.bfloat16)
    adapter_onehot = (
        request_adapter_index[0][:, None]
        == jnp.arange(adapter_up_factor.shape[0], dtype=jnp.int32)[None, :]
    ).astype(jnp.bfloat16)
    up_chosen = jnp.einsum(
        "gq,qjl->gjl", adapter_onehot, adapter_up_factor, preferred_element_type=jnp.float32
    ).astype(jnp.bfloat16)
    masked_low = low_rank_delta[:, None, :] * member.astype(jnp.bfloat16)[:, :, None]
    delta = jnp.einsum("tsr,src->tc", masked_low, up_chosen, preferred_element_type=jnp.float32)
    queries = (projected[0] + delta).astype(jnp.bfloat16).reshape(group, local_heads, head_size)
    plane, queries = lax.optimization_barrier((plane, queries))
    z_count = lax.axis_size("z")
    z_here = lax.axis_index("z")
    own_index = request_cache_index[0]
    shifts = range(1, z_count)

    def along_z(value, d):
        return lax.ppermute(value, "z", perm=[(i, (i + d) % z_count) for i in range(z_count)])

    behind = jnp.stack([own_index] + [along_z(own_index, d) for d in shifts])
    line_rows = jnp.take(behind, (z_here - jnp.arange(z_count, dtype=jnp.int32)) % z_count, axis=0)
    local = line_rows - z_here * per_plane
    valid = ((local >= 0) & (local < per_plane)).astype(jnp.int32)
    slots = pick_states(jnp.clip(local, 0, per_plane - 1).reshape(-1), valid.reshape(-1), plane, z_count)
    states = lax.psum_scatter(slots, "z", scatter_dimension=0, tiled=True)[0]
    keys = projected[1].astype(jnp.bfloat16).reshape(group, local_heads, head_size)
    values = projected[2].astype(jnp.bfloat16).reshape(group, local_heads, head_size)
    gate_terms = jnp.einsum(
        "td,kdh->kth", gathered, head_gate_weight, preferred_element_type=jnp.float32
    )
    log_keep = jax.nn.log_sigmoid(gate_terms[0] + decay_logit_bias[None, :])
    mix_gate = jax.nn.sigmoid(gate_terms[1])
    running = jnp.cumsum(log_keep, axis=0)
    before = running - log_keep
    start_hot = (positions[None, :] == starts[:, None]).astype(jnp.float32)
    start_level = jnp.sum(start_hot[:, :, None] * before[None, :, :], axis=1)
    level = running - jnp.sum(member[:, :, None] * start_level[None, :, :], axis=1)
    masked_queries = queries[:, None, :, :] * member.astype(jnp.bfloat16)[:, :, None, None]
    from_state = jnp.einsum(
        "tshi,shij->thj", masked_queries, states, preferred_element_type=jnp.float32
    )
    carried = from_state * jnp.exp(level)[:, :, None]

    scores = jnp.einsum("qhd,khd->hqk", queries, keys, preferred_element_type=jnp.float32) * scale
    allowed = (segment[:, None] == segment[None, :]) & (positions[None, :] <= positions[:, None])
    masked = jnp.where(allowed[None], scores, -jnp.inf)
    peak = jnp.max(masked, axis=2, keepdims=True)
    weights = jnp.exp(masked - peak)
    probs = (weights / jnp.sum(weights, axis=2, keepdims=True)).astype(jnp.bfloat16)
    attended = jnp.einsum("hqk,khd->qhd", probs, values, preferred_element_type=jnp.float32)
    gap = jnp.where(allowed[None], running.T[:, :, None] - running.T[:, None, :], -jnp.inf)
    memory_w = (scores * jnp.exp(gap)).astype(jnp.bfloat16)
    recalled = jnp.einsum("hqk,khd->qhd", memory_w, values, preferred_element_type=jnp.float32)
    recalled = recalled + carried
    factor = lax.rsqrt(jnp.mean(recalled * recalled, axis=2, keepdims=True) + epsilon)
    combined = attended + mix_gate[:, :, None] * recalled * factor
    head_out = combined.astype(jnp.bfloat16).reshape(group, head_cols)

    partial = jnp.dot(head_out, head_output_weight, preferred_element_type=jnp.float32)
    own = lax.dynamic_slice_in_dim(partial, col * tok_rows, tok_rows, axis=0)
    sent = lax.dynamic_slice_in_dim(partial, (1 - col) * tok_rows, tok_rows, axis=0)
    attn_proj = own + swap(sent)
    mixed = (tokens.astype(jnp.float32) + attn_proj).astype(jnp.bfloat16)
    normed_two = rms_scale(mixed, norm_gain_pair[1])

    def feed_half(weight):
        gate_up = jnp.einsum(
            "td,kdf->ktf", normed_two, weight[:2], preferred_element_type=jnp.float32
        )
        hidden = (jax.nn.silu(gate_up[0]) * gate_up[1]).astype(jnp.bfloat16)
        return jnp.einsum("tf,df->td", hidden, weight[2], preferred_element_type=jnp.float32)

    feed = feed_half(feedforward_weight) + feed_half(ff_other)
    return (mixed.astype(jnp.float32) + feed).astype(jnp.bfloat16)


def solution(mesh):
    n_req = mesh.shape["req"]
    side = round(n_req ** (1.0 / 3.0))
    devices = np.asarray(mesh.devices).reshape(side, side, n_req // (side * side), mesh.shape["col"])
    grid = Mesh(devices, ROWS)
    placed = (
        P(ROWS, None),
        P(),
        P(None, None, "col"),
        P(None, None, "col"),
        P("col"),
        P("col", None, None),
        P(None, None, "col"),
        P(ROWS[:3], None, None),
        P(ROWS[:3], None),
        P(ROWS[:3], None),
        P(ROWS[:3], "col", None, None),
        P("col", None),
        P(None, None, "col"),
    )
    return jax.shard_map(
        on_device, mesh=grid, in_specs=placed, out_specs=P(ROWS, None), check_vma=False
    )
```

```python
import math

import jax
import jax.numpy as jnp
import numpy as np
from jax import lax
from jax.experimental import pallas as pl
from jax.experimental.pallas import tpu as pltpu
from jax.sharding import Mesh
from jax.sharding import PartitionSpec as P

epsilon = 1e-05
ROWS = ("z", "y", "x", "col")


def rms_scale(values, gain):
    widened = values.astype(jnp.float32)
    factor = lax.rsqrt(jnp.mean(widened * widened, axis=-1, keepdims=True) + epsilon)
    return (widened * factor * gain).astype(jnp.bfloat16)


def swap(value):
    return lax.ppermute(value, "col", perm=[(0, 1), (1, 0)])


def pair_rows(mine, other, col):
    first = jnp.where(col == 0, mine, other)
    second = jnp.where(col == 0, other, mine)
    return jnp.concatenate([first, second], axis=0)


def pick_states(index, valid, plane, lines):
    slots = index.shape[0]
    per_line = slots // lines
    block = plane.shape[1:]

    def body(index_ref, valid_ref, plane_ref, out_ref, zero_ref, sems):
        zero_ref[...] = jnp.zeros(block, plane.dtype)
        for s in range(slots):
            dst = out_ref.at[s // per_line, s % per_line]

            @pl.when(valid_ref[s] != 0)
            def _():
                pltpu.make_async_copy(plane_ref.at[index_ref[s]], dst, sems.at[s]).start()

            @pl.when(valid_ref[s] == 0)
            def _():
                pltpu.make_async_copy(zero_ref, dst, sems.at[s]).start()

        for s in range(slots):
            dst = out_ref.at[s // per_line, s % per_line]
            pltpu.make_async_copy(zero_ref, dst, sems.at[s]).wait()

    return pl.pallas_call(
        body,
        out_shape=jax.ShapeDtypeStruct((lines, per_line) + block, plane.dtype),
        grid_spec=pltpu.PrefetchScalarGridSpec(
            num_scalar_prefetch=2,
            grid=(),
            in_specs=[pl.BlockSpec(memory_space=pl.ANY)],
            out_specs=pl.BlockSpec(memory_space=pl.ANY),
            scratch_shapes=[pltpu.VMEM(block, plane.dtype), pltpu.SemaphoreType.DMA((slots,))],
        ),
    )(index, valid, plane)


def on_device(
    tokens,
    norm_gain_pair,
    query_key_value_weight,
    head_gate_weight,
    decay_logit_bias,
    adapter_down_factor,
    adapter_up_factor,
    lengths,
    request_adapter_index,
    request_cache_index,
    caches,
    head_output_weight,
    feedforward_weight,
):
    tok_rows, width = tokens.shape
    col = lax.axis_index("col")
    col_count = 2
    group = tok_rows * col_count
    head_cols = query_key_value_weight.shape[2]
    local_heads = head_gate_weight.shape[2]
    head_size = head_cols // local_heads
    group_lengths = lengths[0].reshape(-1)
    scale = 1.0 / math.sqrt(head_size)

    down_other = swap(adapter_down_factor)

    plane = lax.all_gather(caches, ("y", "x"), axis=0, tiled=True)
    per_plane = plane.shape[0]

    normalized_rows = rms_scale(tokens, norm_gain_pair[0])
    gathered = pair_rows(normalized_rows, swap(normalized_rows), col)
    positions = jnp.arange(group, dtype=jnp.int32)
    ends = jnp.cumsum(group_lengths)
    starts = ends - group_lengths
    member = (
        (positions[:, None] >= starts[None, :]) & (positions[:, None] < ends[None, :])
    ).astype(jnp.float32)
    segment = jnp.sum((positions[:, None] >= ends[None, :]).astype(jnp.int32), axis=1)
    projected = jnp.einsum(
        "td,kdc->ktc", gathered, query_key_value_weight, preferred_element_type=jnp.float32
    )
    half_adapters = adapter_down_factor.shape[0]
    mine_numbers = col * half_adapters + jnp.arange(half_adapters, dtype=jnp.int32)
    other_numbers = (1 - col) * half_adapters + jnp.arange(half_adapters, dtype=jnp.int32)
    wanted = request_adapter_index[0][:, None]
    select_mine = (wanted == mine_numbers[None, :]).astype(jnp.bfloat16)
    select_other = (wanted == other_numbers[None, :]).astype(jnp.bfloat16)
    chosen = (
        jnp.einsum("sa,adr->sdr", select_mine, adapter_down_factor, preferred_element_type=jnp.float32)
        + jnp.einsum("sa,adr->sdr", select_other, down_other, preferred_element_type=jnp.float32)
    ).astype(jnp.bfloat16)
    per_request = jnp.einsum("td,sdr->tsr", gathered, chosen, preferred_element_type=jnp.float32)
    low_rank_delta = jnp.sum(member[:, :, None] * per_request, axis=1)
    low_rank_delta = low_rank_delta.astype(jnp.bfloat16)
    adapter_onehot = (
        request_adapter_index[0][:, None]
        == jnp.arange(adapter_up_factor.shape[0], dtype=jnp.int32)[None, :]
    ).astype(jnp.bfloat16)
    up_chosen = jnp.einsum(
        "gq,qjl->gjl", adapter_onehot, adapter_up_factor, preferred_element_type=jnp.float32
    ).astype(jnp.bfloat16)
    masked_low = low_rank_delta[:, None, :] * member.astype(jnp.bfloat16)[:, :, None]
    delta = jnp.einsum("tsr,src->tc", masked_low, up_chosen, preferred_element_type=jnp.float32)
    queries = (projected[0] + delta).astype(jnp.bfloat16).reshape(group, local_heads, head_size)
    plane, queries = lax.optimization_barrier((plane, queries))
    z_count = lax.axis_size("z")
    z_here = lax.axis_index("z")
    own_index = request_cache_index[0]
    shifts = range(1, z_count)

    def along_z(value, d):
        return lax.ppermute(value, "z", perm=[(i, (i + d) % z_count) for i in range(z_count)])

    behind = jnp.stack([own_index] + [along_z(own_index, d) for d in shifts])
    line_rows = jnp.take(behind, (z_here - jnp.arange(z_count, dtype=jnp.int32)) % z_count, axis=0)
    local = line_rows - z_here * per_plane
    valid = ((local >= 0) & (local < per_plane)).astype(jnp.int32)
    slots = pick_states(jnp.clip(local, 0, per_plane - 1).reshape(-1), valid.reshape(-1), plane, z_count)
    states = lax.psum_scatter(slots, "z", scatter_dimension=0, tiled=True)[0]
    keys = projected[1].astype(jnp.bfloat16).reshape(group, local_heads, head_size)
    values = projected[2].astype(jnp.bfloat16).reshape(group, local_heads, head_size)
    gate_terms = jnp.einsum(
        "td,kdh->kth", gathered, head_gate_weight, preferred_element_type=jnp.float32
    )
    log_keep = jax.nn.log_sigmoid(gate_terms[0] + decay_logit_bias[None, :])
    mix_gate = jax.nn.sigmoid(gate_terms[1])
    running = jnp.cumsum(log_keep, axis=0)
    before = running - log_keep
    start_hot = (positions[None, :] == starts[:, None]).astype(jnp.float32)
    start_level = jnp.sum(start_hot[:, :, None] * before[None, :, :], axis=1)
    level = running - jnp.sum(member[:, :, None] * start_level[None, :, :], axis=1)
    masked_queries = queries[:, None, :, :] * member.astype(jnp.bfloat16)[:, :, None, None]
    from_state = jnp.einsum(
        "tshi,shij->thj", masked_queries, states, preferred_element_type=jnp.float32
    )
    carried = from_state * jnp.exp(level)[:, :, None]

    scores = jnp.einsum("qhd,khd->hqk", queries, keys, preferred_element_type=jnp.float32) * scale
    allowed = (segment[:, None] == segment[None, :]) & (positions[None, :] <= positions[:, None])
    masked = jnp.where(allowed[None], scores, -jnp.inf)
    peak = jnp.max(masked, axis=2, keepdims=True)
    weights = jnp.exp(masked - peak)
    probs = (weights / jnp.sum(weights, axis=2, keepdims=True)).astype(jnp.bfloat16)
    attended = jnp.einsum("hqk,khd->qhd", probs, values, preferred_element_type=jnp.float32)
    gap = jnp.where(allowed[None], running.T[:, :, None] - running.T[:, None, :], -jnp.inf)
    memory_w = (scores * jnp.exp(gap)).astype(jnp.bfloat16)
    recalled = jnp.einsum("hqk,khd->qhd", memory_w, values, preferred_element_type=jnp.float32)
    recalled = recalled + carried
    factor = lax.rsqrt(jnp.mean(recalled * recalled, axis=2, keepdims=True) + epsilon)
    combined = attended + mix_gate[:, :, None] * recalled * factor
    head_out = combined.astype(jnp.bfloat16).reshape(group, head_cols)

    partial = jnp.dot(head_out, head_output_weight, preferred_element_type=jnp.float32)
    own = lax.dynamic_slice_in_dim(partial, col * tok_rows, tok_rows, axis=0)
    sent = lax.dynamic_slice_in_dim(partial, (1 - col) * tok_rows, tok_rows, axis=0)
    attn_proj = own + swap(sent)
    mixed = (tokens.astype(jnp.float32) + attn_proj).astype(jnp.bfloat16)
    normed_two = rms_scale(mixed, norm_gain_pair[1])

    rows_two = pair_rows(normed_two, swap(normed_two), col)
    gate_up = jnp.einsum(
        "td,kdf->ktf", rows_two, feedforward_weight[:2], preferred_element_type=jnp.float32
    )
    hidden = (jax.nn.silu(gate_up[0]) * gate_up[1]).astype(jnp.bfloat16)
    feed_part = jnp.einsum(
        "tf,df->td", hidden, feedforward_weight[2], preferred_element_type=jnp.float32
    )
    feed_own = lax.dynamic_slice_in_dim(feed_part, col * tok_rows, tok_rows, axis=0)
    feed_sent = lax.dynamic_slice_in_dim(feed_part, (1 - col) * tok_rows, tok_rows, axis=0)
    feed = feed_own + swap(feed_sent)
    return (mixed.astype(jnp.float32) + feed).astype(jnp.bfloat16)


def solution(mesh):
    n_req = mesh.shape["req"]
    side = round(n_req ** (1.0 / 3.0))
    devices = np.asarray(mesh.devices).reshape(side, side, n_req // (side * side), mesh.shape["col"])
    grid = Mesh(devices, ROWS)
    placed = (
        P(ROWS, None),
        P(),
        P(None, None, "col"),
        P(None, None, "col"),
        P("col"),
        P("col", None, None),
        P(None, None, "col"),
        P(ROWS[:3], None, None),
        P(ROWS[:3], None),
        P(ROWS[:3], None),
        P(ROWS[:3], "col", None, None),
        P("col", None),
        P(None, None, "col"),
    )
    return jax.shard_map(
        on_device, mesh=grid, in_specs=placed, out_specs=P(ROWS, None), check_vma=False
    )
```

```python
import math

import jax
import jax.numpy as jnp
import numpy as np
from jax import lax
from jax.experimental import pallas as pl
from jax.experimental.pallas import tpu as pltpu
from jax.sharding import Mesh
from jax.sharding import PartitionSpec as P

epsilon = 1e-05
ROWS = ("z", "y", "x", "col")


def rms_scale(values, gain):
    widened = values.astype(jnp.float32)
    factor = lax.rsqrt(jnp.mean(widened * widened, axis=-1, keepdims=True) + epsilon)
    return (widened * factor * gain).astype(jnp.bfloat16)


def swap(value):
    return lax.ppermute(value, "col", perm=[(0, 1), (1, 0)])


def pair_rows(mine, other, col):
    first = jnp.where(col == 0, mine, other)
    second = jnp.where(col == 0, other, mine)
    return jnp.concatenate([first, second], axis=0)


def pick_states(index, valid, plane, lines):
    slots = index.shape[0]
    per_line = slots // lines
    block = plane.shape[1:]

    def body(index_ref, valid_ref, plane_ref, out_ref, zero_ref, sems):
        zero_ref[...] = jnp.zeros(block, plane.dtype)
        for s in range(slots):
            dst = out_ref.at[s // per_line, s % per_line]

            @pl.when(valid_ref[s] != 0)
            def _():
                pltpu.make_async_copy(plane_ref.at[index_ref[s]], dst, sems.at[s]).start()

            @pl.when(valid_ref[s] == 0)
            def _():
                pltpu.make_async_copy(zero_ref, dst, sems.at[s]).start()

        for s in range(slots):
            dst = out_ref.at[s // per_line, s % per_line]
            pltpu.make_async_copy(zero_ref, dst, sems.at[s]).wait()

    return pl.pallas_call(
        body,
        out_shape=jax.ShapeDtypeStruct((lines, per_line) + block, plane.dtype),
        grid_spec=pltpu.PrefetchScalarGridSpec(
            num_scalar_prefetch=2,
            grid=(),
            in_specs=[pl.BlockSpec(memory_space=pl.ANY)],
            out_specs=pl.BlockSpec(memory_space=pl.ANY),
            scratch_shapes=[pltpu.VMEM(block, plane.dtype), pltpu.SemaphoreType.DMA((slots,))],
        ),
    )(index, valid, plane)


def on_device(
    tokens,
    norm_gain_pair,
    query_key_value_weight,
    head_gate_weight,
    decay_logit_bias,
    adapter_down_factor,
    adapter_up_factor,
    lengths,
    request_adapter_index,
    request_cache_index,
    caches,
    head_output_weight,
    feedforward_weight,
):
    tok_rows, width = tokens.shape
    col = lax.axis_index("col")
    col_count = 2
    group = tok_rows * col_count
    head_cols = query_key_value_weight.shape[2]
    local_heads = head_gate_weight.shape[2]
    head_size = head_cols // local_heads
    group_lengths = lengths[0].reshape(-1)
    scale = 1.0 / math.sqrt(head_size)

    down_other = swap(adapter_down_factor)

    plane = lax.all_gather(jnp.swapaxes(caches, -1, -2), ("y", "x"), axis=0, tiled=True)
    per_plane = plane.shape[0]

    normalized_rows = rms_scale(tokens, norm_gain_pair[0])
    gathered = pair_rows(normalized_rows, swap(normalized_rows), col)
    positions = jnp.arange(group, dtype=jnp.int32)
    ends = jnp.cumsum(group_lengths)
    starts = ends - group_lengths
    member = (
        (positions[:, None] >= starts[None, :]) & (positions[:, None] < ends[None, :])
    ).astype(jnp.float32)
    segment = jnp.sum((positions[:, None] >= ends[None, :]).astype(jnp.int32), axis=1)
    projected = jnp.einsum(
        "td,kdc->ktc", gathered, query_key_value_weight, preferred_element_type=jnp.float32
    )
    half_adapters = adapter_down_factor.shape[0]
    mine_numbers = col * half_adapters + jnp.arange(half_adapters, dtype=jnp.int32)
    other_numbers = (1 - col) * half_adapters + jnp.arange(half_adapters, dtype=jnp.int32)
    wanted = request_adapter_index[0][:, None]
    select_mine = (wanted == mine_numbers[None, :]).astype(jnp.bfloat16)
    select_other = (wanted == other_numbers[None, :]).astype(jnp.bfloat16)
    chosen = (
        jnp.einsum("sa,adr->sdr", select_mine, adapter_down_factor, preferred_element_type=jnp.float32)
        + jnp.einsum("sa,adr->sdr", select_other, down_other, preferred_element_type=jnp.float32)
    ).astype(jnp.bfloat16)
    per_request = jnp.einsum("td,sdr->tsr", gathered, chosen, preferred_element_type=jnp.float32)
    low_rank_delta = jnp.sum(member[:, :, None] * per_request, axis=1)
    low_rank_delta = low_rank_delta.astype(jnp.bfloat16)
    adapter_onehot = (
        request_adapter_index[0][:, None]
        == jnp.arange(adapter_up_factor.shape[0], dtype=jnp.int32)[None, :]
    ).astype(jnp.bfloat16)
    up_chosen = jnp.einsum(
        "gq,qjl->gjl", adapter_onehot, adapter_up_factor, preferred_element_type=jnp.float32
    ).astype(jnp.bfloat16)
    masked_low = low_rank_delta[:, None, :] * member.astype(jnp.bfloat16)[:, :, None]
    delta = jnp.einsum("tsr,src->tc", masked_low, up_chosen, preferred_element_type=jnp.float32)
    queries = (projected[0] + delta).astype(jnp.bfloat16).reshape(group, local_heads, head_size)
    plane, queries = lax.optimization_barrier((plane, queries))
    z_count = lax.axis_size("z")
    z_here = lax.axis_index("z")
    own_index = request_cache_index[0]
    shifts = range(1, z_count)

    def along_z(value, d):
        return lax.ppermute(value, "z", perm=[(i, (i + d) % z_count) for i in range(z_count)])

    behind = jnp.stack([own_index] + [along_z(own_index, d) for d in shifts])
    line_rows = jnp.take(behind, (z_here - jnp.arange(z_count, dtype=jnp.int32)) % z_count, axis=0)
    local = line_rows - z_here * per_plane
    valid = ((local >= 0) & (local < per_plane)).astype(jnp.int32)
    picked = jnp.take(plane, jnp.clip(local, 0, per_plane - 1).reshape(-1), axis=0)
    keep = valid.reshape(-1).astype(plane.dtype)[:, None, None, None]
    slots = (picked * keep).reshape((z_count, -1) + plane.shape[1:])
    states = lax.psum_scatter(slots, "z", scatter_dimension=0, tiled=True)[0]
    keys = projected[1].astype(jnp.bfloat16).reshape(group, local_heads, head_size)
    values = projected[2].astype(jnp.bfloat16).reshape(group, local_heads, head_size)
    gate_terms = jnp.einsum(
        "td,kdh->kth", gathered, head_gate_weight, preferred_element_type=jnp.float32
    )
    log_keep = jax.nn.log_sigmoid(gate_terms[0] + decay_logit_bias[None, :])
    mix_gate = jax.nn.sigmoid(gate_terms[1])
    running = jnp.cumsum(log_keep, axis=0)
    before = running - log_keep
    start_hot = (positions[None, :] == starts[:, None]).astype(jnp.float32)
    start_level = jnp.sum(start_hot[:, :, None] * before[None, :, :], axis=1)
    level = running - jnp.sum(member[:, :, None] * start_level[None, :, :], axis=1)
    masked_queries = queries[:, None, :, :] * member.astype(jnp.bfloat16)[:, :, None, None]
    from_state = jnp.einsum(
        "tshi,shji->thj", masked_queries, states, preferred_element_type=jnp.float32
    )
    carried = from_state * jnp.exp(level)[:, :, None]

    scores = jnp.einsum("qhd,khd->hqk", queries, keys, preferred_element_type=jnp.float32) * scale
    allowed = (segment[:, None] == segment[None, :]) & (positions[None, :] <= positions[:, None])
    masked = jnp.where(allowed[None], scores, -jnp.inf)
    peak = jnp.max(masked, axis=2, keepdims=True)
    weights = jnp.exp(masked - peak)
    probs = (weights / jnp.sum(weights, axis=2, keepdims=True)).astype(jnp.bfloat16)
    attended = jnp.einsum("hqk,khd->qhd", probs, values, preferred_element_type=jnp.float32)
    gap = jnp.where(allowed[None], running.T[:, :, None] - running.T[:, None, :], -jnp.inf)
    memory_w = (scores * jnp.exp(gap)).astype(jnp.bfloat16)
    recalled = jnp.einsum("hqk,khd->qhd", memory_w, values, preferred_element_type=jnp.float32)
    recalled = recalled + carried
    factor = lax.rsqrt(jnp.mean(recalled * recalled, axis=2, keepdims=True) + epsilon)
    combined = attended + mix_gate[:, :, None] * recalled * factor
    head_out = combined.astype(jnp.bfloat16).reshape(group, head_cols)

    partial = jnp.dot(head_out, head_output_weight, preferred_element_type=jnp.float32)
    own = lax.dynamic_slice_in_dim(partial, col * tok_rows, tok_rows, axis=0)
    sent = lax.dynamic_slice_in_dim(partial, (1 - col) * tok_rows, tok_rows, axis=0)
    attn_proj = own + swap(sent)
    mixed = (tokens.astype(jnp.float32) + attn_proj).astype(jnp.bfloat16)
    normed_two = rms_scale(mixed, norm_gain_pair[1])

    rows_two = pair_rows(normed_two, swap(normed_two), col)
    gate_up = jnp.einsum(
        "td,kdf->ktf", rows_two, feedforward_weight[:2], preferred_element_type=jnp.float32
    )
    hidden = (jax.nn.silu(gate_up[0]) * gate_up[1]).astype(jnp.bfloat16)
    feed_part = jnp.einsum(
        "tf,df->td", hidden, feedforward_weight[2], preferred_element_type=jnp.float32
    )
    feed_own = lax.dynamic_slice_in_dim(feed_part, col * tok_rows, tok_rows, axis=0)
    feed_sent = lax.dynamic_slice_in_dim(feed_part, (1 - col) * tok_rows, tok_rows, axis=0)
    feed = feed_own + swap(feed_sent)
    return (mixed.astype(jnp.float32) + feed).astype(jnp.bfloat16)


def solution(mesh):
    n_req = mesh.shape["req"]
    side = round(n_req ** (1.0 / 3.0))
    devices = np.asarray(mesh.devices).reshape(side, side, n_req // (side * side), mesh.shape["col"])
    grid = Mesh(devices, ROWS)
    placed = (
        P(ROWS, None),
        P(),
        P(None, None, "col"),
        P(None, None, "col"),
        P("col"),
        P("col", None, None),
        P(None, None, "col"),
        P(ROWS[:3], None, None),
        P(ROWS[:3], None),
        P(ROWS[:3], None),
        P(ROWS[:3], "col", None, None),
        P("col", None),
        P(None, None, "col"),
    )
    return jax.shard_map(
        on_device, mesh=grid, in_specs=placed, out_specs=P(ROWS, None), check_vma=False
    )
```

```python
import math

import jax
import jax.numpy as jnp
import numpy as np
from jax import lax
from jax.experimental import pallas as pl
from jax.experimental.pallas import tpu as pltpu
from jax.sharding import Mesh
from jax.sharding import PartitionSpec as P

epsilon = 1e-05
ROWS = ("z", "y", "x", "col")


def rms_scale(values, gain):
    widened = values.astype(jnp.float32)
    factor = lax.rsqrt(jnp.mean(widened * widened, axis=-1, keepdims=True) + epsilon)
    return (widened * factor * gain).astype(jnp.bfloat16)


def swap(value):
    return lax.ppermute(value, "col", perm=[(0, 1), (1, 0)])


def pair_rows(mine, other, col):
    first = jnp.where(col == 0, mine, other)
    second = jnp.where(col == 0, other, mine)
    return jnp.concatenate([first, second], axis=0)


def pick_states(index, valid, plane, lines):
    slots = index.shape[0]
    per_line = slots // lines
    block = plane.shape[1:]

    def body(index_ref, valid_ref, plane_ref, out_ref, zero_ref, sems):
        zero_ref[...] = jnp.zeros(block, plane.dtype)
        for s in range(slots):
            dst = out_ref.at[s // per_line, s % per_line]

            @pl.when(valid_ref[s] != 0)
            def _():
                pltpu.make_async_copy(plane_ref.at[index_ref[s]], dst, sems.at[s]).start()

            @pl.when(valid_ref[s] == 0)
            def _():
                pltpu.make_async_copy(zero_ref, dst, sems.at[s]).start()

        for s in range(slots):
            dst = out_ref.at[s // per_line, s % per_line]
            pltpu.make_async_copy(zero_ref, dst, sems.at[s]).wait()

    return pl.pallas_call(
        body,
        out_shape=jax.ShapeDtypeStruct((lines, per_line) + block, plane.dtype),
        grid_spec=pltpu.PrefetchScalarGridSpec(
            num_scalar_prefetch=2,
            grid=(),
            in_specs=[pl.BlockSpec(memory_space=pl.ANY)],
            out_specs=pl.BlockSpec(memory_space=pl.ANY),
            scratch_shapes=[pltpu.VMEM(block, plane.dtype), pltpu.SemaphoreType.DMA((slots,))],
        ),
    )(index, valid, plane)


def ring_gather(value, axis):
    count = lax.axis_size(axis)
    here = lax.axis_index(axis)

    def shift(v, d):
        return lax.ppermute(v, axis, perm=[(i, (i + d) % count) for i in range(count)])

    from_before = shift(value, 1)
    from_after = shift(value, -1)
    half = value.shape[0] // 2
    two_away = jnp.concatenate([shift(from_before[:half], 1), shift(from_after[half:], -1)], axis=0)
    by_offset = jnp.stack([value, from_after, two_away, from_before])
    return jnp.take(by_offset, (jnp.arange(count, dtype=jnp.int32) - here) % count, axis=0)


def on_device(
    tokens,
    norm_gain_pair,
    query_key_value_weight,
    head_gate_weight,
    decay_logit_bias,
    adapter_down_factor,
    adapter_up_factor,
    lengths,
    request_adapter_index,
    request_cache_index,
    caches,
    head_output_weight,
    feedforward_weight,
):
    tok_rows, width = tokens.shape
    col = lax.axis_index("col")
    col_count = 2
    group = tok_rows * col_count
    head_cols = query_key_value_weight.shape[2]
    local_heads = head_gate_weight.shape[2]
    head_size = head_cols // local_heads
    group_lengths = lengths[0].reshape(-1)
    scale = 1.0 / math.sqrt(head_size)

    down_other = swap(adapter_down_factor)

    moved = jnp.swapaxes(caches, -1, -2)
    split = moved.shape[1] // 2
    plane = lax.all_gather(moved[:, :split], ("y", "x"), axis=0, tiled=True)
    plane_two = ring_gather(ring_gather(moved[:, split:], "y"), "x")
    per_plane = plane.shape[0]

    normalized_rows = rms_scale(tokens, norm_gain_pair[0])
    gathered = pair_rows(normalized_rows, swap(normalized_rows), col)
    positions = jnp.arange(group, dtype=jnp.int32)
    ends = jnp.cumsum(group_lengths)
    starts = ends - group_lengths
    member = (
        (positions[:, None] >= starts[None, :]) & (positions[:, None] < ends[None, :])
    ).astype(jnp.float32)
    segment = jnp.sum((positions[:, None] >= ends[None, :]).astype(jnp.int32), axis=1)
    projected = jnp.einsum(
        "td,kdc->ktc", gathered, query_key_value_weight, preferred_element_type=jnp.float32
    )
    half_adapters = adapter_down_factor.shape[0]
    mine_numbers = col * half_adapters + jnp.arange(half_adapters, dtype=jnp.int32)
    other_numbers = (1 - col) * half_adapters + jnp.arange(half_adapters, dtype=jnp.int32)
    wanted = request_adapter_index[0][:, None]
    select_mine = (wanted == mine_numbers[None, :]).astype(jnp.bfloat16)
    select_other = (wanted == other_numbers[None, :]).astype(jnp.bfloat16)
    chosen = (
        jnp.einsum("sa,adr->sdr", select_mine, adapter_down_factor, preferred_element_type=jnp.float32)
        + jnp.einsum("sa,adr->sdr", select_other, down_other, preferred_element_type=jnp.float32)
    ).astype(jnp.bfloat16)
    per_request = jnp.einsum("td,sdr->tsr", gathered, chosen, preferred_element_type=jnp.float32)
    low_rank_delta = jnp.sum(member[:, :, None] * per_request, axis=1)
    low_rank_delta = low_rank_delta.astype(jnp.bfloat16)
    adapter_onehot = (
        request_adapter_index[0][:, None]
        == jnp.arange(adapter_up_factor.shape[0], dtype=jnp.int32)[None, :]
    ).astype(jnp.bfloat16)
    up_chosen = jnp.einsum(
        "gq,qjl->gjl", adapter_onehot, adapter_up_factor, preferred_element_type=jnp.float32
    ).astype(jnp.bfloat16)
    masked_low = low_rank_delta[:, None, :] * member.astype(jnp.bfloat16)[:, :, None]
    delta = jnp.einsum("tsr,src->tc", masked_low, up_chosen, preferred_element_type=jnp.float32)
    queries = (projected[0] + delta).astype(jnp.bfloat16).reshape(group, local_heads, head_size)
    plane, queries = lax.optimization_barrier((plane, queries))
    z_count = lax.axis_size("z")
    z_here = lax.axis_index("z")
    own_index = request_cache_index[0]
    shifts = range(1, z_count)

    def along_z(value, d):
        return lax.ppermute(value, "z", perm=[(i, (i + d) % z_count) for i in range(z_count)])

    behind = jnp.stack([own_index] + [along_z(own_index, d) for d in shifts])
    line_rows = jnp.take(behind, (z_here - jnp.arange(z_count, dtype=jnp.int32)) % z_count, axis=0)
    local = line_rows - z_here * per_plane
    valid = ((local >= 0) & (local < per_plane)).astype(jnp.int32)
    flat = jnp.clip(local, 0, per_plane - 1).reshape(-1)
    per_chip = caches.shape[0]
    x_count = lax.axis_size("x")
    y_count = lax.axis_size("y")
    y_of = flat // (per_chip * x_count)
    x_of = (flat // per_chip) % x_count
    flat_two = (x_of * y_count + y_of) * per_chip + flat % per_chip
    keep = valid.reshape(-1).astype(plane.dtype)[:, None, None, None]
    picked = jnp.take(plane, flat, axis=0) * keep
    picked_two = jnp.take(plane_two.reshape((-1,) + plane_two.shape[3:]), flat_two, axis=0) * keep
    slots = jnp.concatenate([picked, picked_two], axis=1).reshape((z_count, -1) + moved.shape[1:])
    states = lax.psum_scatter(slots, "z", scatter_dimension=0, tiled=True)[0]
    keys = projected[1].astype(jnp.bfloat16).reshape(group, local_heads, head_size)
    values = projected[2].astype(jnp.bfloat16).reshape(group, local_heads, head_size)
    gate_terms = jnp.einsum(
        "td,kdh->kth", gathered, head_gate_weight, preferred_element_type=jnp.float32
    )
    log_keep = jax.nn.log_sigmoid(gate_terms[0] + decay_logit_bias[None, :])
    mix_gate = jax.nn.sigmoid(gate_terms[1])
    running = jnp.cumsum(log_keep, axis=0)
    before = running - log_keep
    start_hot = (positions[None, :] == starts[:, None]).astype(jnp.float32)
    start_level = jnp.sum(start_hot[:, :, None] * before[None, :, :], axis=1)
    level = running - jnp.sum(member[:, :, None] * start_level[None, :, :], axis=1)
    masked_queries = queries[:, None, :, :] * member.astype(jnp.bfloat16)[:, :, None, None]
    from_state = jnp.einsum(
        "tshi,shji->thj", masked_queries, states, preferred_element_type=jnp.float32
    )
    carried = from_state * jnp.exp(level)[:, :, None]

    scores = jnp.einsum("qhd,khd->hqk", queries, keys, preferred_element_type=jnp.float32) * scale
    allowed = (segment[:, None] == segment[None, :]) & (positions[None, :] <= positions[:, None])
    masked = jnp.where(allowed[None], scores, -jnp.inf)
    peak = jnp.max(masked, axis=2, keepdims=True)
    weights = jnp.exp(masked - peak)
    probs = (weights / jnp.sum(weights, axis=2, keepdims=True)).astype(jnp.bfloat16)
    attended = jnp.einsum("hqk,khd->qhd", probs, values, preferred_element_type=jnp.float32)
    gap = jnp.where(allowed[None], running.T[:, :, None] - running.T[:, None, :], -jnp.inf)
    memory_w = (scores * jnp.exp(gap)).astype(jnp.bfloat16)
    recalled = jnp.einsum("hqk,khd->qhd", memory_w, values, preferred_element_type=jnp.float32)
    recalled = recalled + carried
    factor = lax.rsqrt(jnp.mean(recalled * recalled, axis=2, keepdims=True) + epsilon)
    combined = attended + mix_gate[:, :, None] * recalled * factor
    head_out = combined.astype(jnp.bfloat16).reshape(group, head_cols)

    partial = jnp.dot(head_out, head_output_weight, preferred_element_type=jnp.float32)
    own = lax.dynamic_slice_in_dim(partial, col * tok_rows, tok_rows, axis=0)
    sent = lax.dynamic_slice_in_dim(partial, (1 - col) * tok_rows, tok_rows, axis=0)
    attn_proj = own + swap(sent)
    mixed = (tokens.astype(jnp.float32) + attn_proj).astype(jnp.bfloat16)
    normed_two = rms_scale(mixed, norm_gain_pair[1])

    rows_two = pair_rows(normed_two, swap(normed_two), col)
    gate_up = jnp.einsum(
        "td,kdf->ktf", rows_two, feedforward_weight[:2], preferred_element_type=jnp.float32
    )
    hidden = (jax.nn.silu(gate_up[0]) * gate_up[1]).astype(jnp.bfloat16)
    feed_part = jnp.einsum(
        "tf,df->td", hidden, feedforward_weight[2], preferred_element_type=jnp.float32
    )
    feed_own = lax.dynamic_slice_in_dim(feed_part, col * tok_rows, tok_rows, axis=0)
    feed_sent = lax.dynamic_slice_in_dim(feed_part, (1 - col) * tok_rows, tok_rows, axis=0)
    feed = feed_own + swap(feed_sent)
    return (mixed.astype(jnp.float32) + feed).astype(jnp.bfloat16)


def solution(mesh):
    n_req = mesh.shape["req"]
    side = round(n_req ** (1.0 / 3.0))
    devices = np.asarray(mesh.devices).reshape(side, side, n_req // (side * side), mesh.shape["col"])
    grid = Mesh(devices, ROWS)
    placed = (
        P(ROWS, None),
        P(),
        P(None, None, "col"),
        P(None, None, "col"),
        P("col"),
        P("col", None, None),
        P(None, None, "col"),
        P(ROWS[:3], None, None),
        P(ROWS[:3], None),
        P(ROWS[:3], None),
        P(ROWS[:3], "col", None, None),
        P("col", None),
        P(None, None, "col"),
    )
    return jax.shard_map(
        on_device, mesh=grid, in_specs=placed, out_specs=P(ROWS, None), check_vma=False
    )
```

```python
import math

import jax
import jax.numpy as jnp
import numpy as np
from jax import lax
from jax.experimental import pallas as pl
from jax.experimental.pallas import tpu as pltpu
from jax.sharding import Mesh
from jax.sharding import PartitionSpec as P

epsilon = 1e-05
ROWS = ("z", "y", "x", "col")


def rms_scale(values, gain):
    widened = values.astype(jnp.float32)
    factor = lax.rsqrt(jnp.mean(widened * widened, axis=-1, keepdims=True) + epsilon)
    return (widened * factor * gain).astype(jnp.bfloat16)


def swap(value):
    return lax.ppermute(value, "col", perm=[(0, 1), (1, 0)])


def pair_rows(mine, other, col):
    first = jnp.where(col == 0, mine, other)
    second = jnp.where(col == 0, other, mine)
    return jnp.concatenate([first, second], axis=0)


def pick_states(index, valid, plane, lines):
    slots = index.shape[0]
    per_line = slots // lines
    block = plane.shape[1:]

    def body(index_ref, valid_ref, plane_ref, out_ref, zero_ref, sems):
        zero_ref[...] = jnp.zeros(block, plane.dtype)
        for s in range(slots):
            dst = out_ref.at[s // per_line, s % per_line]

            @pl.when(valid_ref[s] != 0)
            def _():
                pltpu.make_async_copy(plane_ref.at[index_ref[s]], dst, sems.at[s]).start()

            @pl.when(valid_ref[s] == 0)
            def _():
                pltpu.make_async_copy(zero_ref, dst, sems.at[s]).start()

        for s in range(slots):
            dst = out_ref.at[s // per_line, s % per_line]
            pltpu.make_async_copy(zero_ref, dst, sems.at[s]).wait()

    return pl.pallas_call(
        body,
        out_shape=jax.ShapeDtypeStruct((lines, per_line) + block, plane.dtype),
        grid_spec=pltpu.PrefetchScalarGridSpec(
            num_scalar_prefetch=2,
            grid=(),
            in_specs=[pl.BlockSpec(memory_space=pl.ANY)],
            out_specs=pl.BlockSpec(memory_space=pl.ANY),
            scratch_shapes=[pltpu.VMEM(block, plane.dtype), pltpu.SemaphoreType.DMA((slots,))],
        ),
    )(index, valid, plane)


def on_device(
    tokens,
    norm_gain_pair,
    query_key_value_weight,
    head_gate_weight,
    decay_logit_bias,
    adapter_down_factor,
    adapter_up_factor,
    lengths,
    request_adapter_index,
    request_cache_index,
    caches,
    head_output_weight,
    feedforward_weight,
):
    tok_rows, width = tokens.shape
    col = lax.axis_index("col")
    col_count = 2
    group = tok_rows * col_count
    head_cols = query_key_value_weight.shape[2]
    local_heads = head_gate_weight.shape[2]
    head_size = head_cols // local_heads
    group_lengths = lengths[0].reshape(-1)
    scale = 1.0 / math.sqrt(head_size)

    down_other = swap(adapter_down_factor)

    plane = lax.all_gather(jnp.swapaxes(caches, -1, -2), ("y", "x"), axis=0, tiled=True)
    per_plane = plane.shape[0]

    normalized_rows = rms_scale(tokens, norm_gain_pair[0])
    gathered = pair_rows(normalized_rows, swap(normalized_rows), col)
    positions = jnp.arange(group, dtype=jnp.int32)
    ends = jnp.cumsum(group_lengths)
    starts = ends - group_lengths
    member = (
        (positions[:, None] >= starts[None, :]) & (positions[:, None] < ends[None, :])
    ).astype(jnp.float32)
    segment = jnp.sum((positions[:, None] >= ends[None, :]).astype(jnp.int32), axis=1)
    projected = jnp.einsum(
        "td,kdc->ktc", gathered, query_key_value_weight, preferred_element_type=jnp.float32
    )
    half_adapters = adapter_down_factor.shape[0]
    mine_numbers = col * half_adapters + jnp.arange(half_adapters, dtype=jnp.int32)
    other_numbers = (1 - col) * half_adapters + jnp.arange(half_adapters, dtype=jnp.int32)
    wanted = request_adapter_index[0][:, None]
    select_mine = (wanted == mine_numbers[None, :]).astype(jnp.bfloat16)
    select_other = (wanted == other_numbers[None, :]).astype(jnp.bfloat16)
    chosen = (
        jnp.einsum("sa,adr->sdr", select_mine, adapter_down_factor, preferred_element_type=jnp.float32)
        + jnp.einsum("sa,adr->sdr", select_other, down_other, preferred_element_type=jnp.float32)
    ).astype(jnp.bfloat16)
    per_request = jnp.einsum("td,sdr->tsr", gathered, chosen, preferred_element_type=jnp.float32)
    low_rank_delta = jnp.sum(member[:, :, None] * per_request, axis=1)
    low_rank_delta = low_rank_delta.astype(jnp.bfloat16)
    adapter_onehot = (
        request_adapter_index[0][:, None]
        == jnp.arange(adapter_up_factor.shape[0], dtype=jnp.int32)[None, :]
    ).astype(jnp.bfloat16)
    up_chosen = jnp.einsum(
        "gq,qjl->gjl", adapter_onehot, adapter_up_factor, preferred_element_type=jnp.float32
    ).astype(jnp.bfloat16)
    masked_low = low_rank_delta[:, None, :] * member.astype(jnp.bfloat16)[:, :, None]
    delta = jnp.einsum("tsr,src->tc", masked_low, up_chosen, preferred_element_type=jnp.float32)
    queries = (projected[0] + delta).astype(jnp.bfloat16).reshape(group, local_heads, head_size)
    plane, queries = lax.optimization_barrier((plane, queries))
    z_count = lax.axis_size("z")
    z_here = lax.axis_index("z")
    own_index = request_cache_index[0]
    shifts = range(1, z_count)

    def along_z(value, d):
        return lax.ppermute(value, "z", perm=[(i, (i + d) % z_count) for i in range(z_count)])

    behind = jnp.stack([own_index] + [along_z(own_index, d) for d in shifts])
    line_rows = jnp.take(behind, (z_here - jnp.arange(z_count, dtype=jnp.int32)) % z_count, axis=0)
    local = line_rows - z_here * per_plane
    valid = ((local >= 0) & (local < per_plane)).astype(jnp.int32)
    picked = jnp.take(plane, jnp.clip(local, 0, per_plane - 1).reshape(-1), axis=0)
    keep = valid.reshape(-1).astype(plane.dtype)[:, None, None, None]
    slots = (picked * keep).reshape((z_count, -1) + plane.shape[1:])
    states = lax.psum_scatter(slots, "z", scatter_dimension=0, tiled=True)[0]
    keys = projected[1].astype(jnp.bfloat16).reshape(group, local_heads, head_size)
    values = projected[2].astype(jnp.bfloat16).reshape(group, local_heads, head_size)
    gate_terms = jnp.einsum(
        "td,kdh->kth", gathered, head_gate_weight, preferred_element_type=jnp.float32
    )
    log_keep = jax.nn.log_sigmoid(gate_terms[0] + decay_logit_bias[None, :])
    mix_gate = jax.nn.sigmoid(gate_terms[1])
    running = jnp.cumsum(log_keep, axis=0)
    before = running - log_keep
    start_hot = (positions[None, :] == starts[:, None]).astype(jnp.float32)
    start_level = jnp.sum(start_hot[:, :, None] * before[None, :, :], axis=1)
    level = running - jnp.sum(member[:, :, None] * start_level[None, :, :], axis=1)
    masked_queries = queries[:, None, :, :] * member.astype(jnp.bfloat16)[:, :, None, None]
    from_state = jnp.einsum(
        "tshi,shji->thj", masked_queries, states, preferred_element_type=jnp.float32
    )
    carried = from_state * jnp.exp(level)[:, :, None]

    scores = jnp.einsum("qhd,khd->hqk", queries, keys, preferred_element_type=jnp.float32) * scale
    allowed = (segment[:, None] == segment[None, :]) & (positions[None, :] <= positions[:, None])
    masked = jnp.where(allowed[None], scores, -jnp.inf)
    peak = jnp.max(masked, axis=2, keepdims=True)
    weights = jnp.exp(masked - peak)
    probs = (weights / jnp.sum(weights, axis=2, keepdims=True)).astype(jnp.bfloat16)
    attended = jnp.einsum("hqk,khd->qhd", probs, values, preferred_element_type=jnp.float32)
    gap = jnp.where(allowed[None], running.T[:, :, None] - running.T[:, None, :], -jnp.inf)
    memory_w = (scores * jnp.exp(gap)).astype(jnp.bfloat16)
    recalled = jnp.einsum("hqk,khd->qhd", memory_w, values, preferred_element_type=jnp.float32)
    recalled = recalled + carried
    factor = lax.rsqrt(jnp.mean(recalled * recalled, axis=2, keepdims=True) + epsilon)
    combined = attended + mix_gate[:, :, None] * recalled * factor
    head_out = combined.astype(jnp.bfloat16).reshape(group, head_cols)

    head_partner = lax.dynamic_slice_in_dim(head_out, (1 - col) * tok_rows, tok_rows, axis=0)
    head_own = lax.dynamic_slice_in_dim(head_out, col * tok_rows, tok_rows, axis=0)
    proj_partner = swap(jnp.dot(head_partner, head_output_weight, preferred_element_type=jnp.float32))
    attn_proj = jnp.dot(head_own, head_output_weight, preferred_element_type=jnp.float32) + proj_partner
    mixed = (tokens.astype(jnp.float32) + attn_proj).astype(jnp.bfloat16)
    normed_two = rms_scale(mixed, norm_gain_pair[1])

    def feed_part(rows):
        gate_up = jnp.einsum(
            "td,kdf->ktf", rows, feedforward_weight[:2], preferred_element_type=jnp.float32
        )
        hidden = (jax.nn.silu(gate_up[0]) * gate_up[1]).astype(jnp.bfloat16)
        return jnp.einsum(
            "tf,df->td", hidden, feedforward_weight[2], preferred_element_type=jnp.float32
        )

    partner_two = swap(normed_two)
    half = tok_rows // 2
    for_partner = [
        swap(feed_part(partner_two[:half])),
        swap(feed_part(partner_two[half:])),
    ]
    feed = feed_part(normed_two) + jnp.concatenate(for_partner, axis=0)
    return (mixed.astype(jnp.float32) + feed).astype(jnp.bfloat16)


def solution(mesh):
    n_req = mesh.shape["req"]
    side = round(n_req ** (1.0 / 3.0))
    devices = np.asarray(mesh.devices).reshape(side, side, n_req // (side * side), mesh.shape["col"])
    grid = Mesh(devices, ROWS)
    placed = (
        P(ROWS, None),
        P(),
        P(None, None, "col"),
        P(None, None, "col"),
        P("col"),
        P("col", None, None),
        P(None, None, "col"),
        P(ROWS[:3], None, None),
        P(ROWS[:3], None),
        P(ROWS[:3], None),
        P(ROWS[:3], "col", None, None),
        P("col", None),
        P(None, None, "col"),
    )
    return jax.shard_map(
        on_device, mesh=grid, in_specs=placed, out_specs=P(ROWS, None), check_vma=False
    )
```

```python
import math

import jax
import jax.numpy as jnp
import numpy as np
from jax import lax
from jax.experimental import pallas as pl
from jax.experimental.pallas import tpu as pltpu
from jax.sharding import Mesh
from jax.sharding import PartitionSpec as P

epsilon = 1e-05
ROWS = ("z", "y", "x", "col")


def rms_scale(values, gain):
    widened = values.astype(jnp.float32)
    factor = lax.rsqrt(jnp.mean(widened * widened, axis=-1, keepdims=True) + epsilon)
    return (widened * factor * gain).astype(jnp.bfloat16)


def swap(value):
    return lax.ppermute(value, "col", perm=[(0, 1), (1, 0)])


def pair_rows(mine, other, col):
    first = jnp.where(col == 0, mine, other)
    second = jnp.where(col == 0, other, mine)
    return jnp.concatenate([first, second], axis=0)


def pick_states(index, valid, plane, lines):
    slots = index.shape[0]
    per_line = slots // lines
    block = plane.shape[1:]

    def body(index_ref, valid_ref, plane_ref, out_ref, zero_ref, sems):
        zero_ref[...] = jnp.zeros(block, plane.dtype)
        for s in range(slots):
            dst = out_ref.at[s // per_line, s % per_line]

            @pl.when(valid_ref[s] != 0)
            def _():
                pltpu.make_async_copy(plane_ref.at[index_ref[s]], dst, sems.at[s]).start()

            @pl.when(valid_ref[s] == 0)
            def _():
                pltpu.make_async_copy(zero_ref, dst, sems.at[s]).start()

        for s in range(slots):
            dst = out_ref.at[s // per_line, s % per_line]
            pltpu.make_async_copy(zero_ref, dst, sems.at[s]).wait()

    return pl.pallas_call(
        body,
        out_shape=jax.ShapeDtypeStruct((lines, per_line) + block, plane.dtype),
        grid_spec=pltpu.PrefetchScalarGridSpec(
            num_scalar_prefetch=2,
            grid=(),
            in_specs=[pl.BlockSpec(memory_space=pl.ANY)],
            out_specs=pl.BlockSpec(memory_space=pl.ANY),
            scratch_shapes=[pltpu.VMEM(block, plane.dtype), pltpu.SemaphoreType.DMA((slots,))],
        ),
    )(index, valid, plane)


def on_device(
    tokens,
    norm_gain_pair,
    query_key_value_weight,
    head_gate_weight,
    decay_logit_bias,
    adapter_down_factor,
    adapter_up_factor,
    lengths,
    request_adapter_index,
    request_cache_index,
    caches,
    head_output_weight,
    feedforward_weight,
):
    tok_rows, width = tokens.shape
    col = lax.axis_index("col")
    col_count = 2
    group = tok_rows * col_count
    head_cols = query_key_value_weight.shape[2]
    local_heads = head_gate_weight.shape[2]
    head_size = head_cols // local_heads
    group_lengths = lengths[0].reshape(-1)
    scale = 1.0 / math.sqrt(head_size)

    down_other = swap(adapter_down_factor)
    out_weight_other = swap(head_output_weight)

    plane = lax.all_gather(jnp.swapaxes(caches, -1, -2), ("y", "x"), axis=0, tiled=True)
    per_plane = plane.shape[0]

    normalized_rows = rms_scale(tokens, norm_gain_pair[0])
    gathered = pair_rows(normalized_rows, swap(normalized_rows), col)
    positions = jnp.arange(group, dtype=jnp.int32)
    ends = jnp.cumsum(group_lengths)
    starts = ends - group_lengths
    member = (
        (positions[:, None] >= starts[None, :]) & (positions[:, None] < ends[None, :])
    ).astype(jnp.float32)
    segment = jnp.sum((positions[:, None] >= ends[None, :]).astype(jnp.int32), axis=1)
    projected = jnp.einsum(
        "td,kdc->ktc", gathered, query_key_value_weight, preferred_element_type=jnp.float32
    )
    half_adapters = adapter_down_factor.shape[0]
    mine_numbers = col * half_adapters + jnp.arange(half_adapters, dtype=jnp.int32)
    other_numbers = (1 - col) * half_adapters + jnp.arange(half_adapters, dtype=jnp.int32)
    wanted = request_adapter_index[0][:, None]
    select_mine = (wanted == mine_numbers[None, :]).astype(jnp.bfloat16)
    select_other = (wanted == other_numbers[None, :]).astype(jnp.bfloat16)
    chosen = (
        jnp.einsum("sa,adr->sdr", select_mine, adapter_down_factor, preferred_element_type=jnp.float32)
        + jnp.einsum("sa,adr->sdr", select_other, down_other, preferred_element_type=jnp.float32)
    ).astype(jnp.bfloat16)
    per_request = jnp.einsum("td,sdr->tsr", gathered, chosen, preferred_element_type=jnp.float32)
    low_rank_delta = jnp.sum(member[:, :, None] * per_request, axis=1)
    low_rank_delta = low_rank_delta.astype(jnp.bfloat16)
    adapter_onehot = (
        request_adapter_index[0][:, None]
        == jnp.arange(adapter_up_factor.shape[0], dtype=jnp.int32)[None, :]
    ).astype(jnp.bfloat16)
    up_chosen = jnp.einsum(
        "gq,qjl->gjl", adapter_onehot, adapter_up_factor, preferred_element_type=jnp.float32
    ).astype(jnp.bfloat16)
    masked_low = low_rank_delta[:, None, :] * member.astype(jnp.bfloat16)[:, :, None]
    delta = jnp.einsum("tsr,src->tc", masked_low, up_chosen, preferred_element_type=jnp.float32)
    queries = (projected[0] + delta).astype(jnp.bfloat16).reshape(group, local_heads, head_size)
    plane, queries = lax.optimization_barrier((plane, queries))
    z_count = lax.axis_size("z")
    z_here = lax.axis_index("z")
    own_index = request_cache_index[0]
    shifts = range(1, z_count)

    def along_z(value, d):
        return lax.ppermute(value, "z", perm=[(i, (i + d) % z_count) for i in range(z_count)])

    behind = jnp.stack([own_index] + [along_z(own_index, d) for d in shifts])
    line_rows = jnp.take(behind, (z_here - jnp.arange(z_count, dtype=jnp.int32)) % z_count, axis=0)
    local = line_rows - z_here * per_plane
    valid = ((local >= 0) & (local < per_plane)).astype(jnp.int32)
    picked = jnp.take(plane, jnp.clip(local, 0, per_plane - 1).reshape(-1), axis=0)
    keep = valid.reshape(-1).astype(plane.dtype)[:, None, None, None]
    slots = (picked * keep).reshape((z_count, -1) + plane.shape[1:])
    states = lax.psum_scatter(slots, "z", scatter_dimension=0, tiled=True)[0]
    keys = projected[1].astype(jnp.bfloat16).reshape(group, local_heads, head_size)
    values = projected[2].astype(jnp.bfloat16).reshape(group, local_heads, head_size)
    gate_terms = jnp.einsum(
        "td,kdh->kth", gathered, head_gate_weight, preferred_element_type=jnp.float32
    )
    log_keep = jax.nn.log_sigmoid(gate_terms[0] + decay_logit_bias[None, :])
    mix_gate = jax.nn.sigmoid(gate_terms[1])
    running = jnp.cumsum(log_keep, axis=0)
    before = running - log_keep
    start_hot = (positions[None, :] == starts[:, None]).astype(jnp.float32)
    start_level = jnp.sum(start_hot[:, :, None] * before[None, :, :], axis=1)
    level = running - jnp.sum(member[:, :, None] * start_level[None, :, :], axis=1)
    masked_queries = queries[:, None, :, :] * member.astype(jnp.bfloat16)[:, :, None, None]
    from_state = jnp.einsum(
        "tshi,shji->thj", masked_queries, states, preferred_element_type=jnp.float32
    )
    carried = from_state * jnp.exp(level)[:, :, None]

    scores = jnp.einsum("qhd,khd->hqk", queries, keys, preferred_element_type=jnp.float32) * scale
    allowed = (segment[:, None] == segment[None, :]) & (positions[None, :] <= positions[:, None])
    masked = jnp.where(allowed[None], scores, -jnp.inf)
    peak = jnp.max(masked, axis=2, keepdims=True)
    weights = jnp.exp(masked - peak)
    probs = (weights / jnp.sum(weights, axis=2, keepdims=True)).astype(jnp.bfloat16)
    attended = jnp.einsum("hqk,khd->qhd", probs, values, preferred_element_type=jnp.float32)
    gap = jnp.where(allowed[None], running.T[:, :, None] - running.T[:, None, :], -jnp.inf)
    memory_w = (scores * jnp.exp(gap)).astype(jnp.bfloat16)
    recalled = jnp.einsum("hqk,khd->qhd", memory_w, values, preferred_element_type=jnp.float32)
    recalled = recalled + carried
    factor = lax.rsqrt(jnp.mean(recalled * recalled, axis=2, keepdims=True) + epsilon)
    combined = attended + mix_gate[:, :, None] * recalled * factor
    head_out = combined.astype(jnp.bfloat16).reshape(group, head_cols)

    head_own = lax.dynamic_slice_in_dim(head_out, col * tok_rows, tok_rows, axis=0)
    head_sent = lax.dynamic_slice_in_dim(head_out, (1 - col) * tok_rows, tok_rows, axis=0)
    attn_proj = jnp.dot(head_own, head_output_weight, preferred_element_type=jnp.float32) + jnp.dot(
        swap(head_sent), out_weight_other, preferred_element_type=jnp.float32
    )
    mixed = (tokens.astype(jnp.float32) + attn_proj).astype(jnp.bfloat16)
    normed_two = rms_scale(mixed, norm_gain_pair[1])

    rows_two = pair_rows(normed_two, swap(normed_two), col)
    gate_up = jnp.einsum(
        "td,kdf->ktf", rows_two, feedforward_weight[:2], preferred_element_type=jnp.float32
    )
    hidden = (jax.nn.silu(gate_up[0]) * gate_up[1]).astype(jnp.bfloat16)
    feed_part = jnp.einsum(
        "tf,df->td", hidden, feedforward_weight[2], preferred_element_type=jnp.float32
    )
    feed_own = lax.dynamic_slice_in_dim(feed_part, col * tok_rows, tok_rows, axis=0)
    feed_sent = lax.dynamic_slice_in_dim(feed_part, (1 - col) * tok_rows, tok_rows, axis=0)
    feed = feed_own + swap(feed_sent)
    return (mixed.astype(jnp.float32) + feed).astype(jnp.bfloat16)


def solution(mesh):
    n_req = mesh.shape["req"]
    side = round(n_req ** (1.0 / 3.0))
    devices = np.asarray(mesh.devices).reshape(side, side, n_req // (side * side), mesh.shape["col"])
    grid = Mesh(devices, ROWS)
    placed = (
        P(ROWS, None),
        P(),
        P(None, None, "col"),
        P(None, None, "col"),
        P("col"),
        P("col", None, None),
        P(None, None, "col"),
        P(ROWS[:3], None, None),
        P(ROWS[:3], None),
        P(ROWS[:3], None),
        P(ROWS[:3], "col", None, None),
        P("col", None),
        P(None, None, "col"),
    )
    return jax.shard_map(
        on_device, mesh=grid, in_specs=placed, out_specs=P(ROWS, None), check_vma=False
    )
```

```python
import math

import jax
import jax.numpy as jnp
import numpy as np
from jax import lax
from jax.experimental import pallas as pl
from jax.experimental.pallas import tpu as pltpu
from jax.sharding import Mesh
from jax.sharding import PartitionSpec as P

epsilon = 1e-05
ROWS = ("z", "y", "x", "col")


def rms_scale(values, gain):
    widened = values.astype(jnp.float32)
    factor = lax.rsqrt(jnp.mean(widened * widened, axis=-1, keepdims=True) + epsilon)
    return (widened * factor * gain).astype(jnp.bfloat16)


def swap(value):
    return lax.ppermute(value, "col", perm=[(0, 1), (1, 0)])


def pair_rows(mine, other, col):
    first = jnp.where(col == 0, mine, other)
    second = jnp.where(col == 0, other, mine)
    return jnp.concatenate([first, second], axis=0)


def pick_states(index, valid, plane, lines):
    slots = index.shape[0]
    per_line = slots // lines
    block = plane.shape[1:]

    def body(index_ref, valid_ref, plane_ref, out_ref, zero_ref, sems):
        zero_ref[...] = jnp.zeros(block, plane.dtype)
        for s in range(slots):
            dst = out_ref.at[s // per_line, s % per_line]

            @pl.when(valid_ref[s] != 0)
            def _():
                pltpu.make_async_copy(plane_ref.at[index_ref[s]], dst, sems.at[s]).start()

            @pl.when(valid_ref[s] == 0)
            def _():
                pltpu.make_async_copy(zero_ref, dst, sems.at[s]).start()

        for s in range(slots):
            dst = out_ref.at[s // per_line, s % per_line]
            pltpu.make_async_copy(zero_ref, dst, sems.at[s]).wait()

    return pl.pallas_call(
        body,
        out_shape=jax.ShapeDtypeStruct((lines, per_line) + block, plane.dtype),
        grid_spec=pltpu.PrefetchScalarGridSpec(
            num_scalar_prefetch=2,
            grid=(),
            in_specs=[pl.BlockSpec(memory_space=pl.ANY)],
            out_specs=pl.BlockSpec(memory_space=pl.ANY),
            scratch_shapes=[pltpu.VMEM(block, plane.dtype), pltpu.SemaphoreType.DMA((slots,))],
        ),
    )(index, valid, plane)


def on_device(
    tokens,
    norm_gain_pair,
    query_key_value_weight,
    head_gate_weight,
    decay_logit_bias,
    adapter_down_factor,
    adapter_up_factor,
    lengths,
    request_adapter_index,
    request_cache_index,
    caches,
    head_output_weight,
    feedforward_weight,
):
    tok_rows, width = tokens.shape
    col = lax.axis_index("col")
    col_count = 2
    group = tok_rows * col_count
    head_cols = query_key_value_weight.shape[2]
    local_heads = head_gate_weight.shape[2]
    head_size = head_cols // local_heads
    group_lengths = lengths[0].reshape(-1)
    scale = 1.0 / math.sqrt(head_size)

    down_other = swap(adapter_down_factor)
    out_weight_other = swap(head_output_weight)

    plane = lax.all_gather(jnp.swapaxes(caches, -1, -2), ("y", "x"), axis=0, tiled=True)
    per_plane = plane.shape[0]

    normalized_rows = rms_scale(tokens, norm_gain_pair[0])
    gathered = pair_rows(normalized_rows, swap(normalized_rows), col)
    positions = jnp.arange(group, dtype=jnp.int32)
    ends = jnp.cumsum(group_lengths)
    starts = ends - group_lengths
    member = (
        (positions[:, None] >= starts[None, :]) & (positions[:, None] < ends[None, :])
    ).astype(jnp.float32)
    segment = jnp.sum((positions[:, None] >= ends[None, :]).astype(jnp.int32), axis=1)
    projected = jnp.einsum(
        "td,kdc->ktc", gathered, query_key_value_weight, preferred_element_type=jnp.float32
    )
    half_adapters = adapter_down_factor.shape[0]
    mine_numbers = col * half_adapters + jnp.arange(half_adapters, dtype=jnp.int32)
    other_numbers = (1 - col) * half_adapters + jnp.arange(half_adapters, dtype=jnp.int32)
    wanted = request_adapter_index[0][:, None]
    select_mine = (wanted == mine_numbers[None, :]).astype(jnp.bfloat16)
    select_other = (wanted == other_numbers[None, :]).astype(jnp.bfloat16)
    chosen = (
        jnp.einsum("sa,adr->sdr", select_mine, adapter_down_factor, preferred_element_type=jnp.float32)
        + jnp.einsum("sa,adr->sdr", select_other, down_other, preferred_element_type=jnp.float32)
    ).astype(jnp.bfloat16)
    per_request = jnp.einsum("td,sdr->tsr", gathered, chosen, preferred_element_type=jnp.float32)
    low_rank_delta = jnp.sum(member[:, :, None] * per_request, axis=1)
    low_rank_delta = low_rank_delta.astype(jnp.bfloat16)
    adapter_onehot = (
        request_adapter_index[0][:, None]
        == jnp.arange(adapter_up_factor.shape[0], dtype=jnp.int32)[None, :]
    ).astype(jnp.bfloat16)
    up_chosen = jnp.einsum(
        "gq,qjl->gjl", adapter_onehot, adapter_up_factor, preferred_element_type=jnp.float32
    ).astype(jnp.bfloat16)
    masked_low = low_rank_delta[:, None, :] * member.astype(jnp.bfloat16)[:, :, None]
    delta = jnp.einsum("tsr,src->tc", masked_low, up_chosen, preferred_element_type=jnp.float32)
    queries = (projected[0] + delta).astype(jnp.bfloat16).reshape(group, local_heads, head_size)
    plane, queries = lax.optimization_barrier((plane, queries))
    z_count = lax.axis_size("z")
    z_here = lax.axis_index("z")
    own_index = request_cache_index[0]
    shifts = range(1, z_count)

    def along_z(value, d):
        return lax.ppermute(value, "z", perm=[(i, (i + d) % z_count) for i in range(z_count)])

    behind = jnp.stack([own_index] + [along_z(own_index, d) for d in shifts])
    line_rows = jnp.take(behind, (z_here - jnp.arange(z_count, dtype=jnp.int32)) % z_count, axis=0)
    local = line_rows - z_here * per_plane
    valid = ((local >= 0) & (local < per_plane)).astype(jnp.int32)
    picked = jnp.take(plane, jnp.clip(local, 0, per_plane - 1).reshape(-1), axis=0)
    keep = valid.reshape(-1).astype(plane.dtype)[:, None, None, None]
    slots = (picked * keep).reshape((z_count, -1) + plane.shape[1:])
    states = lax.psum_scatter(slots, "z", scatter_dimension=0, tiled=True)[0]
    keys = projected[1].astype(jnp.bfloat16).reshape(group, local_heads, head_size)
    values = projected[2].astype(jnp.bfloat16).reshape(group, local_heads, head_size)
    gate_terms = jnp.einsum(
        "td,kdh->kth", gathered, head_gate_weight, preferred_element_type=jnp.float32
    )
    log_keep = jax.nn.log_sigmoid(gate_terms[0] + decay_logit_bias[None, :])
    mix_gate = jax.nn.sigmoid(gate_terms[1])
    running = jnp.cumsum(log_keep, axis=0)
    before = running - log_keep
    start_hot = (positions[None, :] == starts[:, None]).astype(jnp.float32)
    start_level = jnp.sum(start_hot[:, :, None] * before[None, :, :], axis=1)
    level = running - jnp.sum(member[:, :, None] * start_level[None, :, :], axis=1)
    masked_queries = queries[:, None, :, :] * member.astype(jnp.bfloat16)[:, :, None, None]
    masked_queries, mix_gate = lax.optimization_barrier((masked_queries, mix_gate))
    from_state = jnp.einsum(
        "tshi,shji->thj", masked_queries, states, preferred_element_type=jnp.float32
    )
    carried = from_state * jnp.exp(level)[:, :, None]

    scores = jnp.einsum("qhd,khd->hqk", queries, keys, preferred_element_type=jnp.float32) * scale
    allowed = (segment[:, None] == segment[None, :]) & (positions[None, :] <= positions[:, None])
    masked = jnp.where(allowed[None], scores, -jnp.inf)
    peak = jnp.max(masked, axis=2, keepdims=True)
    weights = jnp.exp(masked - peak)
    probs = (weights / jnp.sum(weights, axis=2, keepdims=True)).astype(jnp.bfloat16)
    attended = jnp.einsum("hqk,khd->qhd", probs, values, preferred_element_type=jnp.float32)
    gap = jnp.where(allowed[None], running.T[:, :, None] - running.T[:, None, :], -jnp.inf)
    memory_w = (scores * jnp.exp(gap)).astype(jnp.bfloat16)
    recalled = jnp.einsum("hqk,khd->qhd", memory_w, values, preferred_element_type=jnp.float32)
    recalled = recalled + carried
    factor = lax.rsqrt(jnp.mean(recalled * recalled, axis=2, keepdims=True) + epsilon)
    combined = attended + mix_gate[:, :, None] * recalled * factor
    head_out = combined.astype(jnp.bfloat16).reshape(group, head_cols)

    head_own = lax.dynamic_slice_in_dim(head_out, col * tok_rows, tok_rows, axis=0)
    head_sent = lax.dynamic_slice_in_dim(head_out, (1 - col) * tok_rows, tok_rows, axis=0)
    attn_proj = jnp.dot(head_own, head_output_weight, preferred_element_type=jnp.float32) + jnp.dot(
        swap(head_sent), out_weight_other, preferred_element_type=jnp.float32
    )
    mixed = (tokens.astype(jnp.float32) + attn_proj).astype(jnp.bfloat16)
    normed_two = rms_scale(mixed, norm_gain_pair[1])

    rows_two = pair_rows(normed_two, swap(normed_two), col)
    gate_up = jnp.einsum(
        "td,kdf->ktf", rows_two, feedforward_weight[:2], preferred_element_type=jnp.float32
    )
    hidden = (jax.nn.silu(gate_up[0]) * gate_up[1]).astype(jnp.bfloat16)
    feed_part = jnp.einsum(
        "tf,df->td", hidden, feedforward_weight[2], preferred_element_type=jnp.float32
    )
    feed_own = lax.dynamic_slice_in_dim(feed_part, col * tok_rows, tok_rows, axis=0)
    feed_sent = lax.dynamic_slice_in_dim(feed_part, (1 - col) * tok_rows, tok_rows, axis=0)
    feed = feed_own + swap(feed_sent)
    return (mixed.astype(jnp.float32) + feed).astype(jnp.bfloat16)


def solution(mesh):
    n_req = mesh.shape["req"]
    side = round(n_req ** (1.0 / 3.0))
    devices = np.asarray(mesh.devices).reshape(side, side, n_req // (side * side), mesh.shape["col"])
    grid = Mesh(devices, ROWS)
    placed = (
        P(ROWS, None),
        P(),
        P(None, None, "col"),
        P(None, None, "col"),
        P("col"),
        P("col", None, None),
        P(None, None, "col"),
        P(ROWS[:3], None, None),
        P(ROWS[:3], None),
        P(ROWS[:3], None),
        P(ROWS[:3], "col", None, None),
        P("col", None),
        P(None, None, "col"),
    )
    return jax.shard_map(
        on_device, mesh=grid, in_specs=placed, out_specs=P(ROWS, None), check_vma=False
    )
```

```python
import math

import jax
import jax.numpy as jnp
import numpy as np
from jax import lax
from jax.experimental import pallas as pl
from jax.experimental.pallas import tpu as pltpu
from jax.sharding import Mesh
from jax.sharding import PartitionSpec as P

epsilon = 1e-05
ROWS = ("z", "y", "x", "col")


def rms_scale(values, gain):
    widened = values.astype(jnp.float32)
    factor = lax.rsqrt(jnp.mean(widened * widened, axis=-1, keepdims=True) + epsilon)
    return (widened * factor * gain).astype(jnp.bfloat16)


def swap(value):
    return lax.ppermute(value, "col", perm=[(0, 1), (1, 0)])


def pair_rows(mine, other, col):
    first = jnp.where(col == 0, mine, other)
    second = jnp.where(col == 0, other, mine)
    return jnp.concatenate([first, second], axis=0)


def pick_states(index, valid, plane, lines):
    slots = index.shape[0]
    per_line = slots // lines
    block = plane.shape[1:]

    def body(index_ref, valid_ref, plane_ref, out_ref, zero_ref, sems):
        zero_ref[...] = jnp.zeros(block, plane.dtype)
        for s in range(slots):
            dst = out_ref.at[s // per_line, s % per_line]

            @pl.when(valid_ref[s] != 0)
            def _():
                pltpu.make_async_copy(plane_ref.at[index_ref[s]], dst, sems.at[s]).start()

            @pl.when(valid_ref[s] == 0)
            def _():
                pltpu.make_async_copy(zero_ref, dst, sems.at[s]).start()

        for s in range(slots):
            dst = out_ref.at[s // per_line, s % per_line]
            pltpu.make_async_copy(zero_ref, dst, sems.at[s]).wait()

    return pl.pallas_call(
        body,
        out_shape=jax.ShapeDtypeStruct((lines, per_line) + block, plane.dtype),
        grid_spec=pltpu.PrefetchScalarGridSpec(
            num_scalar_prefetch=2,
            grid=(),
            in_specs=[pl.BlockSpec(memory_space=pl.ANY)],
            out_specs=pl.BlockSpec(memory_space=pl.ANY),
            scratch_shapes=[pltpu.VMEM(block, plane.dtype), pltpu.SemaphoreType.DMA((slots,))],
        ),
    )(index, valid, plane)


def on_device(
    tokens,
    norm_gain_pair,
    query_key_value_weight,
    head_gate_weight,
    decay_logit_bias,
    adapter_down_factor,
    adapter_up_factor,
    lengths,
    request_adapter_index,
    request_cache_index,
    caches,
    head_output_weight,
    feedforward_weight,
):
    tok_rows, width = tokens.shape
    col = lax.axis_index("col")
    col_count = 2
    group = tok_rows * col_count
    head_cols = query_key_value_weight.shape[2]
    local_heads = head_gate_weight.shape[2]
    head_size = head_cols // local_heads
    group_lengths = lengths[0].reshape(-1)
    scale = 1.0 / math.sqrt(head_size)

    down_other = swap(adapter_down_factor)
    out_weight_other = swap(head_output_weight)

    plane = lax.all_gather(jnp.swapaxes(caches, -1, -2), ("y", "x"), axis=0, tiled=True)
    per_plane = plane.shape[0]

    normalized_rows = rms_scale(tokens, norm_gain_pair[0])
    gathered = pair_rows(normalized_rows, swap(normalized_rows), col)
    positions = jnp.arange(group, dtype=jnp.int32)
    ends = jnp.cumsum(group_lengths)
    starts = ends - group_lengths
    member = (
        (positions[:, None] >= starts[None, :]) & (positions[:, None] < ends[None, :])
    ).astype(jnp.float32)
    segment = jnp.sum((positions[:, None] >= ends[None, :]).astype(jnp.int32), axis=1)
    projected = jnp.einsum(
        "td,kdc->ktc", gathered, query_key_value_weight, preferred_element_type=jnp.float32
    )
    half_adapters = adapter_down_factor.shape[0]
    mine_numbers = col * half_adapters + jnp.arange(half_adapters, dtype=jnp.int32)
    other_numbers = (1 - col) * half_adapters + jnp.arange(half_adapters, dtype=jnp.int32)
    wanted = request_adapter_index[0][:, None]
    select_mine = (wanted == mine_numbers[None, :]).astype(jnp.bfloat16)
    select_other = (wanted == other_numbers[None, :]).astype(jnp.bfloat16)
    chosen = (
        jnp.einsum("sa,adr->sdr", select_mine, adapter_down_factor, preferred_element_type=jnp.float32)
        + jnp.einsum("sa,adr->sdr", select_other, down_other, preferred_element_type=jnp.float32)
    ).astype(jnp.bfloat16)
    per_request = jnp.einsum("td,sdr->tsr", gathered, chosen, preferred_element_type=jnp.float32)
    low_rank_delta = jnp.sum(member[:, :, None] * per_request, axis=1)
    low_rank_delta = low_rank_delta.astype(jnp.bfloat16)
    adapter_onehot = (
        request_adapter_index[0][:, None]
        == jnp.arange(adapter_up_factor.shape[0], dtype=jnp.int32)[None, :]
    ).astype(jnp.bfloat16)
    up_chosen = jnp.einsum(
        "gq,qjl->gjl", adapter_onehot, adapter_up_factor, preferred_element_type=jnp.float32
    ).astype(jnp.bfloat16)
    masked_low = low_rank_delta[:, None, :] * member.astype(jnp.bfloat16)[:, :, None]
    delta = jnp.einsum("tsr,src->tc", masked_low, up_chosen, preferred_element_type=jnp.float32)
    queries = (projected[0] + delta).astype(jnp.bfloat16).reshape(group, local_heads, head_size)
    plane, queries = lax.optimization_barrier((plane, queries))
    z_count = lax.axis_size("z")
    z_here = lax.axis_index("z")
    own_index = request_cache_index[0]
    shifts = range(1, z_count)

    def along_z(value, d):
        return lax.ppermute(value, "z", perm=[(i, (i + d) % z_count) for i in range(z_count)])

    behind = jnp.stack([own_index] + [along_z(own_index, d) for d in shifts])
    line_rows = jnp.take(behind, (z_here - jnp.arange(z_count, dtype=jnp.int32)) % z_count, axis=0)
    local = line_rows - z_here * per_plane
    valid = ((local >= 0) & (local < per_plane)).astype(jnp.int32)
    picked = jnp.take(plane, jnp.clip(local, 0, per_plane - 1).reshape(-1), axis=0)
    keep = valid.reshape(-1).astype(plane.dtype)[:, None, None, None]
    slots = (picked * keep).reshape((z_count, -1) + plane.shape[1:])
    states = lax.psum_scatter(slots, "z", scatter_dimension=0, tiled=True)[0]
    keys = projected[1].astype(jnp.bfloat16).reshape(group, local_heads, head_size)
    values = projected[2].astype(jnp.bfloat16).reshape(group, local_heads, head_size)
    gate_terms = jnp.einsum(
        "td,kdh->kth", gathered, head_gate_weight, preferred_element_type=jnp.float32
    )
    log_keep = jax.nn.log_sigmoid(gate_terms[0] + decay_logit_bias[None, :])
    mix_gate = jax.nn.sigmoid(gate_terms[1])
    running = jnp.cumsum(log_keep, axis=0)
    before = running - log_keep
    start_hot = (positions[None, :] == starts[:, None]).astype(jnp.float32)
    start_level = jnp.sum(start_hot[:, :, None] * before[None, :, :], axis=1)
    level = running - jnp.sum(member[:, :, None] * start_level[None, :, :], axis=1)
    masked_queries = queries[:, None, :, :] * member.astype(jnp.bfloat16)[:, :, None, None]
    masked_queries, mix_gate = lax.optimization_barrier((masked_queries, mix_gate))
    from_state = jnp.einsum(
        "tshi,shji->thj", masked_queries, states, preferred_element_type=jnp.float32
    )
    carried = from_state * jnp.exp(level)[:, :, None]

    scores = jnp.einsum("qhd,khd->hqk", queries, keys, preferred_element_type=jnp.float32) * scale
    allowed = (segment[:, None] == segment[None, :]) & (positions[None, :] <= positions[:, None])
    masked = jnp.where(allowed[None], scores, -jnp.inf)
    peak = jnp.max(masked, axis=2, keepdims=True)
    weights = jnp.exp(masked - peak)
    probs = (weights / jnp.sum(weights, axis=2, keepdims=True)).astype(jnp.bfloat16)
    attended = jnp.einsum("hqk,khd->qhd", probs, values, preferred_element_type=jnp.float32)
    gap = jnp.where(allowed[None], running.T[:, :, None] - running.T[:, None, :], -jnp.inf)
    memory_w = (scores * jnp.exp(gap)).astype(jnp.bfloat16)
    recalled = jnp.einsum("hqk,khd->qhd", memory_w, values, preferred_element_type=jnp.float32)
    recalled = recalled + carried
    factor = lax.rsqrt(jnp.mean(recalled * recalled, axis=2, keepdims=True) + epsilon)
    combined = attended + mix_gate[:, :, None] * recalled * factor
    head_out = combined.astype(jnp.bfloat16).reshape(group, head_cols)

    head_own = lax.dynamic_slice_in_dim(head_out, col * tok_rows, tok_rows, axis=0)
    head_sent = lax.dynamic_slice_in_dim(head_out, (1 - col) * tok_rows, tok_rows, axis=0)
    attn_proj = jnp.dot(head_own, head_output_weight, preferred_element_type=jnp.float32) + jnp.dot(
        swap(head_sent), out_weight_other, preferred_element_type=jnp.float32
    )
    mixed = (tokens.astype(jnp.float32) + attn_proj).astype(jnp.bfloat16)
    normed_two = rms_scale(mixed, norm_gain_pair[1])

    def feed_part(rows):
        gate_up = jnp.einsum(
            "td,kdf->ktf", rows, feedforward_weight[:2], preferred_element_type=jnp.float32
        )
        hidden = (jax.nn.silu(gate_up[0]) * gate_up[1]).astype(jnp.bfloat16)
        return jnp.einsum(
            "tf,df->td", hidden, feedforward_weight[2], preferred_element_type=jnp.float32
        )

    from_partner = swap(feed_part(swap(normed_two)))
    feed = feed_part(normed_two) + from_partner
    return (mixed.astype(jnp.float32) + feed).astype(jnp.bfloat16)


def solution(mesh):
    n_req = mesh.shape["req"]
    side = round(n_req ** (1.0 / 3.0))
    devices = np.asarray(mesh.devices).reshape(side, side, n_req // (side * side), mesh.shape["col"])
    grid = Mesh(devices, ROWS)
    placed = (
        P(ROWS, None),
        P(),
        P(None, None, "col"),
        P(None, None, "col"),
        P("col"),
        P("col", None, None),
        P(None, None, "col"),
        P(ROWS[:3], None, None),
        P(ROWS[:3], None),
        P(ROWS[:3], None),
        P(ROWS[:3], "col", None, None),
        P("col", None),
        P(None, None, "col"),
    )
    return jax.shard_map(
        on_device, mesh=grid, in_specs=placed, out_specs=P(ROWS, None), check_vma=False
    )
```

```python
import math

import jax
import jax.numpy as jnp
import numpy as np
from jax import lax
from jax.experimental import pallas as pl
from jax.experimental.pallas import tpu as pltpu
from jax.sharding import Mesh
from jax.sharding import PartitionSpec as P

epsilon = 1e-05
ROWS = ("z", "y", "x", "col")


def rms_scale(values, gain):
    widened = values.astype(jnp.float32)
    factor = lax.rsqrt(jnp.mean(widened * widened, axis=-1, keepdims=True) + epsilon)
    return (widened * factor * gain).astype(jnp.bfloat16)


def swap(value):
    return lax.ppermute(value, "col", perm=[(0, 1), (1, 0)])


def pair_rows(mine, other, col):
    first = jnp.where(col == 0, mine, other)
    second = jnp.where(col == 0, other, mine)
    return jnp.concatenate([first, second], axis=0)


def pick_states(index, valid, plane, lines):
    slots = index.shape[0]
    per_line = slots // lines
    block = plane.shape[1:]

    def body(index_ref, valid_ref, plane_ref, out_ref, zero_ref, sems):
        zero_ref[...] = jnp.zeros(block, plane.dtype)
        for s in range(slots):
            dst = out_ref.at[s // per_line, s % per_line]

            @pl.when(valid_ref[s] != 0)
            def _():
                pltpu.make_async_copy(plane_ref.at[index_ref[s]], dst, sems.at[s]).start()

            @pl.when(valid_ref[s] == 0)
            def _():
                pltpu.make_async_copy(zero_ref, dst, sems.at[s]).start()

        for s in range(slots):
            dst = out_ref.at[s // per_line, s % per_line]
            pltpu.make_async_copy(zero_ref, dst, sems.at[s]).wait()

    return pl.pallas_call(
        body,
        out_shape=jax.ShapeDtypeStruct((lines, per_line) + block, plane.dtype),
        grid_spec=pltpu.PrefetchScalarGridSpec(
            num_scalar_prefetch=2,
            grid=(),
            in_specs=[pl.BlockSpec(memory_space=pl.ANY)],
            out_specs=pl.BlockSpec(memory_space=pl.ANY),
            scratch_shapes=[pltpu.VMEM(block, plane.dtype), pltpu.SemaphoreType.DMA((slots,))],
        ),
    )(index, valid, plane)


def on_device(
    tokens,
    norm_gain_pair,
    query_key_value_weight,
    head_gate_weight,
    decay_logit_bias,
    adapter_down_factor,
    adapter_up_factor,
    lengths,
    request_adapter_index,
    request_cache_index,
    caches,
    head_output_weight,
    feedforward_weight,
):
    tok_rows, width = tokens.shape
    col = lax.axis_index("col")
    col_count = 2
    group = tok_rows * col_count
    head_cols = query_key_value_weight.shape[2]
    local_heads = head_gate_weight.shape[2]
    head_size = head_cols // local_heads
    group_lengths = lengths[0].reshape(-1)
    scale = 1.0 / math.sqrt(head_size)

    down_other = swap(adapter_down_factor)
    out_weight_other = swap(head_output_weight)

    plane = lax.all_gather(jnp.swapaxes(caches, -1, -2), ("y", "x"), axis=0, tiled=True)
    per_plane = plane.shape[0]

    normalized_rows = rms_scale(tokens, norm_gain_pair[0])
    gathered = pair_rows(normalized_rows, swap(normalized_rows), col)
    positions = jnp.arange(group, dtype=jnp.int32)
    ends = jnp.cumsum(group_lengths)
    starts = ends - group_lengths
    member = (
        (positions[:, None] >= starts[None, :]) & (positions[:, None] < ends[None, :])
    ).astype(jnp.float32)
    segment = jnp.sum((positions[:, None] >= ends[None, :]).astype(jnp.int32), axis=1)
    projected = jnp.einsum(
        "td,kdc->ktc", gathered, query_key_value_weight, preferred_element_type=jnp.float32
    )
    half_adapters = adapter_down_factor.shape[0]
    mine_numbers = col * half_adapters + jnp.arange(half_adapters, dtype=jnp.int32)
    other_numbers = (1 - col) * half_adapters + jnp.arange(half_adapters, dtype=jnp.int32)
    wanted = request_adapter_index[0][:, None]
    select_mine = (wanted == mine_numbers[None, :]).astype(jnp.bfloat16)
    select_other = (wanted == other_numbers[None, :]).astype(jnp.bfloat16)
    chosen = (
        jnp.einsum("sa,adr->sdr", select_mine, adapter_down_factor, preferred_element_type=jnp.float32)
        + jnp.einsum("sa,adr->sdr", select_other, down_other, preferred_element_type=jnp.float32)
    ).astype(jnp.bfloat16)
    per_request = jnp.einsum("td,sdr->tsr", gathered, chosen, preferred_element_type=jnp.float32)
    low_rank_delta = jnp.sum(member[:, :, None] * per_request, axis=1)
    low_rank_delta = low_rank_delta.astype(jnp.bfloat16)
    adapter_onehot = (
        request_adapter_index[0][:, None]
        == jnp.arange(adapter_up_factor.shape[0], dtype=jnp.int32)[None, :]
    ).astype(jnp.bfloat16)
    up_chosen = jnp.einsum(
        "gq,qjl->gjl", adapter_onehot, adapter_up_factor, preferred_element_type=jnp.float32
    ).astype(jnp.bfloat16)
    masked_low = low_rank_delta[:, None, :] * member.astype(jnp.bfloat16)[:, :, None]
    delta = jnp.einsum("tsr,src->tc", masked_low, up_chosen, preferred_element_type=jnp.float32)
    queries = (projected[0] + delta).astype(jnp.bfloat16).reshape(group, local_heads, head_size)
    plane, queries = lax.optimization_barrier((plane, queries))
    z_count = lax.axis_size("z")
    z_here = lax.axis_index("z")
    own_index = request_cache_index[0]
    shifts = range(1, z_count)

    def along_z(value, d):
        return lax.ppermute(value, "z", perm=[(i, (i + d) % z_count) for i in range(z_count)])

    behind = jnp.stack([own_index] + [along_z(own_index, d) for d in shifts])
    line_rows = jnp.take(behind, (z_here - jnp.arange(z_count, dtype=jnp.int32)) % z_count, axis=0)
    local = line_rows - z_here * per_plane
    valid = ((local >= 0) & (local < per_plane)).astype(jnp.int32)
    picked = jnp.take(plane, jnp.clip(local, 0, per_plane - 1).reshape(-1), axis=0)
    keep = valid.reshape(-1).astype(plane.dtype)[:, None, None, None]
    slots = (picked * keep).reshape((z_count, -1) + plane.shape[1:])
    received = lax.all_to_all(slots, "z", 0, 0, tiled=True)
    states = jnp.sum(received.astype(jnp.float32), axis=0).astype(jnp.bfloat16)
    keys = projected[1].astype(jnp.bfloat16).reshape(group, local_heads, head_size)
    values = projected[2].astype(jnp.bfloat16).reshape(group, local_heads, head_size)
    gate_terms = jnp.einsum(
        "td,kdh->kth", gathered, head_gate_weight, preferred_element_type=jnp.float32
    )
    log_keep = jax.nn.log_sigmoid(gate_terms[0] + decay_logit_bias[None, :])
    mix_gate = jax.nn.sigmoid(gate_terms[1])
    running = jnp.cumsum(log_keep, axis=0)
    before = running - log_keep
    start_hot = (positions[None, :] == starts[:, None]).astype(jnp.float32)
    start_level = jnp.sum(start_hot[:, :, None] * before[None, :, :], axis=1)
    level = running - jnp.sum(member[:, :, None] * start_level[None, :, :], axis=1)
    masked_queries = queries[:, None, :, :] * member.astype(jnp.bfloat16)[:, :, None, None]
    masked_queries, mix_gate = lax.optimization_barrier((masked_queries, mix_gate))
    from_state = jnp.einsum(
        "tshi,shji->thj", masked_queries, states, preferred_element_type=jnp.float32
    )
    carried = from_state * jnp.exp(level)[:, :, None]

    scores = jnp.einsum("qhd,khd->hqk", queries, keys, preferred_element_type=jnp.float32) * scale
    allowed = (segment[:, None] == segment[None, :]) & (positions[None, :] <= positions[:, None])
    masked = jnp.where(allowed[None], scores, -jnp.inf)
    peak = jnp.max(masked, axis=2, keepdims=True)
    weights = jnp.exp(masked - peak)
    probs = (weights / jnp.sum(weights, axis=2, keepdims=True)).astype(jnp.bfloat16)
    attended = jnp.einsum("hqk,khd->qhd", probs, values, preferred_element_type=jnp.float32)
    gap = jnp.where(allowed[None], running.T[:, :, None] - running.T[:, None, :], -jnp.inf)
    memory_w = (scores * jnp.exp(gap)).astype(jnp.bfloat16)
    recalled = jnp.einsum("hqk,khd->qhd", memory_w, values, preferred_element_type=jnp.float32)
    recalled = recalled + carried
    factor = lax.rsqrt(jnp.mean(recalled * recalled, axis=2, keepdims=True) + epsilon)
    combined = attended + mix_gate[:, :, None] * recalled * factor
    head_out = combined.astype(jnp.bfloat16).reshape(group, head_cols)

    head_own = lax.dynamic_slice_in_dim(head_out, col * tok_rows, tok_rows, axis=0)
    head_sent = lax.dynamic_slice_in_dim(head_out, (1 - col) * tok_rows, tok_rows, axis=0)
    attn_proj = jnp.dot(head_own, head_output_weight, preferred_element_type=jnp.float32) + jnp.dot(
        swap(head_sent), out_weight_other, preferred_element_type=jnp.float32
    )
    mixed = (tokens.astype(jnp.float32) + attn_proj).astype(jnp.bfloat16)
    normed_two = rms_scale(mixed, norm_gain_pair[1])

    def feed_part(rows):
        gate_up = jnp.einsum(
            "td,kdf->ktf", rows, feedforward_weight[:2], preferred_element_type=jnp.float32
        )
        hidden = (jax.nn.silu(gate_up[0]) * gate_up[1]).astype(jnp.bfloat16)
        return jnp.einsum(
            "tf,df->td", hidden, feedforward_weight[2], preferred_element_type=jnp.float32
        )

    from_partner = swap(feed_part(swap(normed_two)))
    feed = feed_part(normed_two) + from_partner
    return (mixed.astype(jnp.float32) + feed).astype(jnp.bfloat16)


def solution(mesh):
    n_req = mesh.shape["req"]
    side = round(n_req ** (1.0 / 3.0))
    devices = np.asarray(mesh.devices).reshape(side, side, n_req // (side * side), mesh.shape["col"])
    grid = Mesh(devices, ROWS)
    placed = (
        P(ROWS, None),
        P(),
        P(None, None, "col"),
        P(None, None, "col"),
        P("col"),
        P("col", None, None),
        P(None, None, "col"),
        P(ROWS[:3], None, None),
        P(ROWS[:3], None),
        P(ROWS[:3], None),
        P(ROWS[:3], "col", None, None),
        P("col", None),
        P(None, None, "col"),
    )
    return jax.shard_map(
        on_device, mesh=grid, in_specs=placed, out_specs=P(ROWS, None), check_vma=False
    )
```

```python
import math

import jax
import jax.numpy as jnp
import numpy as np
from jax import lax
from jax.experimental import pallas as pl
from jax.experimental.pallas import tpu as pltpu
from jax.sharding import Mesh
from jax.sharding import PartitionSpec as P

epsilon = 1e-05
ROWS = ("z", "y", "x", "col")


def rms_scale(values, gain):
    widened = values.astype(jnp.float32)
    factor = lax.rsqrt(jnp.mean(widened * widened, axis=-1, keepdims=True) + epsilon)
    return (widened * factor * gain).astype(jnp.bfloat16)


def swap(value):
    return lax.ppermute(value, "col", perm=[(0, 1), (1, 0)])


def pair_rows(mine, other, col):
    first = jnp.where(col == 0, mine, other)
    second = jnp.where(col == 0, other, mine)
    return jnp.concatenate([first, second], axis=0)


def pick_states(index, valid, plane, lines):
    slots = index.shape[0]
    per_line = slots // lines
    block = plane.shape[1:]

    def body(index_ref, valid_ref, plane_ref, out_ref, zero_ref, sems):
        zero_ref[...] = jnp.zeros(block, plane.dtype)
        for s in range(slots):
            dst = out_ref.at[s // per_line, s % per_line]

            @pl.when(valid_ref[s] != 0)
            def _():
                pltpu.make_async_copy(plane_ref.at[index_ref[s]], dst, sems.at[s]).start()

            @pl.when(valid_ref[s] == 0)
            def _():
                pltpu.make_async_copy(zero_ref, dst, sems.at[s]).start()

        for s in range(slots):
            dst = out_ref.at[s // per_line, s % per_line]
            pltpu.make_async_copy(zero_ref, dst, sems.at[s]).wait()

    return pl.pallas_call(
        body,
        out_shape=jax.ShapeDtypeStruct((lines, per_line) + block, plane.dtype),
        grid_spec=pltpu.PrefetchScalarGridSpec(
            num_scalar_prefetch=2,
            grid=(),
            in_specs=[pl.BlockSpec(memory_space=pl.ANY)],
            out_specs=pl.BlockSpec(memory_space=pl.ANY),
            scratch_shapes=[pltpu.VMEM(block, plane.dtype), pltpu.SemaphoreType.DMA((slots,))],
        ),
    )(index, valid, plane)


def on_device(
    tokens,
    norm_gain_pair,
    query_key_value_weight,
    head_gate_weight,
    decay_logit_bias,
    adapter_down_factor,
    adapter_up_factor,
    lengths,
    request_adapter_index,
    request_cache_index,
    caches,
    head_output_weight,
    feedforward_weight,
):
    tok_rows, width = tokens.shape
    col = lax.axis_index("col")
    col_count = 2
    group = tok_rows * col_count
    head_cols = query_key_value_weight.shape[2]
    local_heads = head_gate_weight.shape[2]
    head_size = head_cols // local_heads
    group_lengths = lengths[0].reshape(-1)
    scale = 1.0 / math.sqrt(head_size)

    down_other = swap(adapter_down_factor)
    out_weight_other = swap(head_output_weight)

    plane = lax.all_gather(jnp.swapaxes(caches, -1, -2), ("y", "x"), axis=0, tiled=True)
    per_plane = plane.shape[0]

    normalized_rows = rms_scale(tokens, norm_gain_pair[0])
    gathered = pair_rows(normalized_rows, swap(normalized_rows), col)
    positions = jnp.arange(group, dtype=jnp.int32)
    ends = jnp.cumsum(group_lengths)
    starts = ends - group_lengths
    member = (
        (positions[:, None] >= starts[None, :]) & (positions[:, None] < ends[None, :])
    ).astype(jnp.float32)
    segment = jnp.sum((positions[:, None] >= ends[None, :]).astype(jnp.int32), axis=1)
    projected = jnp.einsum(
        "td,kdc->ktc", gathered, query_key_value_weight, preferred_element_type=jnp.float32
    )
    half_adapters = adapter_down_factor.shape[0]
    mine_numbers = col * half_adapters + jnp.arange(half_adapters, dtype=jnp.int32)
    other_numbers = (1 - col) * half_adapters + jnp.arange(half_adapters, dtype=jnp.int32)
    wanted = request_adapter_index[0][:, None]
    select_mine = (wanted == mine_numbers[None, :]).astype(jnp.bfloat16)
    select_other = (wanted == other_numbers[None, :]).astype(jnp.bfloat16)
    chosen = (
        jnp.einsum("sa,adr->sdr", select_mine, adapter_down_factor, preferred_element_type=jnp.float32)
        + jnp.einsum("sa,adr->sdr", select_other, down_other, preferred_element_type=jnp.float32)
    ).astype(jnp.bfloat16)
    per_request = jnp.einsum("td,sdr->tsr", gathered, chosen, preferred_element_type=jnp.float32)
    low_rank_delta = jnp.sum(member[:, :, None] * per_request, axis=1)
    low_rank_delta = low_rank_delta.astype(jnp.bfloat16)
    adapter_onehot = (
        request_adapter_index[0][:, None]
        == jnp.arange(adapter_up_factor.shape[0], dtype=jnp.int32)[None, :]
    ).astype(jnp.bfloat16)
    up_chosen = jnp.einsum(
        "gq,qjl->gjl", adapter_onehot, adapter_up_factor, preferred_element_type=jnp.float32
    ).astype(jnp.bfloat16)
    masked_low = low_rank_delta[:, None, :] * member.astype(jnp.bfloat16)[:, :, None]
    delta = jnp.einsum("tsr,src->tc", masked_low, up_chosen, preferred_element_type=jnp.float32)
    queries = (projected[0] + delta).astype(jnp.bfloat16).reshape(group, local_heads, head_size)
    plane, queries = lax.optimization_barrier((plane, queries))
    z_count = lax.axis_size("z")
    z_here = lax.axis_index("z")
    own_index = request_cache_index[0]
    shifts = range(1, z_count)

    def along_z(value, d):
        return lax.ppermute(value, "z", perm=[(i, (i + d) % z_count) for i in range(z_count)])

    behind = jnp.stack([own_index] + [along_z(own_index, d) for d in shifts])
    line_rows = jnp.take(behind, (z_here - jnp.arange(z_count, dtype=jnp.int32)) % z_count, axis=0)
    local = line_rows - z_here * per_plane
    valid = ((local >= 0) & (local < per_plane)).astype(jnp.int32)
    picked = jnp.take(plane, jnp.clip(local, 0, per_plane - 1).reshape(-1), axis=0)
    keep = valid.reshape(-1).astype(plane.dtype)[:, None, None, None]
    slots = (picked * keep).reshape((z_count, -1) + plane.shape[1:])
    states = lax.psum_scatter(slots, "z", scatter_dimension=0, tiled=True)[0]
    keys = projected[1].astype(jnp.bfloat16).reshape(group, local_heads, head_size)
    values = projected[2].astype(jnp.bfloat16).reshape(group, local_heads, head_size)
    gate_terms = jnp.einsum(
        "td,kdh->kth", gathered, head_gate_weight, preferred_element_type=jnp.float32
    )
    log_keep = jax.nn.log_sigmoid(gate_terms[0] + decay_logit_bias[None, :])
    mix_gate = jax.nn.sigmoid(gate_terms[1])
    running = jnp.cumsum(log_keep, axis=0)
    before = running - log_keep
    start_hot = (positions[None, :] == starts[:, None]).astype(jnp.float32)
    start_level = jnp.sum(start_hot[:, :, None] * before[None, :, :], axis=1)
    level = running - jnp.sum(member[:, :, None] * start_level[None, :, :], axis=1)
    masked_queries = queries[:, None, :, :] * member.astype(jnp.bfloat16)[:, :, None, None]
    masked_queries, mix_gate = lax.optimization_barrier((masked_queries, mix_gate))
    from_state = jnp.einsum(
        "tshi,shji->thj", masked_queries, states, preferred_element_type=jnp.float32
    )
    carried = from_state * jnp.exp(level)[:, :, None]

    scores = jnp.einsum("qhd,khd->hqk", queries, keys, preferred_element_type=jnp.float32) * scale
    allowed = (segment[:, None] == segment[None, :]) & (positions[None, :] <= positions[:, None])
    masked = jnp.where(allowed[None], scores, -jnp.inf)
    peak = jnp.max(masked, axis=2, keepdims=True)
    weights = jnp.exp(masked - peak)
    probs = (weights / jnp.sum(weights, axis=2, keepdims=True)).astype(jnp.bfloat16)
    attended = jnp.einsum("hqk,khd->qhd", probs, values, preferred_element_type=jnp.float32)
    gap = jnp.where(allowed[None], running.T[:, :, None] - running.T[:, None, :], -jnp.inf)
    memory_w = (scores * jnp.exp(gap)).astype(jnp.bfloat16)
    recalled = jnp.einsum("hqk,khd->qhd", memory_w, values, preferred_element_type=jnp.float32)
    recalled = recalled + carried
    factor = lax.rsqrt(jnp.mean(recalled * recalled, axis=2, keepdims=True) + epsilon)
    combined = attended + mix_gate[:, :, None] * recalled * factor
    head_out = combined.astype(jnp.bfloat16).reshape(group, head_cols)

    head_own = lax.dynamic_slice_in_dim(head_out, col * tok_rows, tok_rows, axis=0)
    head_sent = lax.dynamic_slice_in_dim(head_out, (1 - col) * tok_rows, tok_rows, axis=0)
    attn_proj = jnp.dot(head_own, head_output_weight, preferred_element_type=jnp.float32) + jnp.dot(
        swap(head_sent), out_weight_other, preferred_element_type=jnp.float32
    )
    mixed = (tokens.astype(jnp.float32) + attn_proj).astype(jnp.bfloat16)
    normed_two = rms_scale(mixed, norm_gain_pair[1])

    def feed_part(rows):
        gate_up = jnp.einsum(
            "td,kdf->ktf", rows, feedforward_weight[:2], preferred_element_type=jnp.float32
        )
        hidden = (jax.nn.silu(gate_up[0]) * gate_up[1]).astype(jnp.bfloat16)
        return jnp.einsum(
            "tf,df->td", hidden, feedforward_weight[2], preferred_element_type=jnp.float32
        )

    half = normed_two.shape[0] // 2
    own_first = feed_part(normed_two[:half])
    own_first, partner_two = lax.optimization_barrier((own_first, swap(normed_two)))
    from_partner = swap(feed_part(partner_two))
    feed = jnp.concatenate([own_first, feed_part(normed_two[half:])], axis=0) + from_partner
    return (mixed.astype(jnp.float32) + feed).astype(jnp.bfloat16)


def solution(mesh):
    n_req = mesh.shape["req"]
    side = round(n_req ** (1.0 / 3.0))
    devices = np.asarray(mesh.devices).reshape(side, side, n_req // (side * side), mesh.shape["col"])
    grid = Mesh(devices, ROWS)
    placed = (
        P(ROWS, None),
        P(),
        P(None, None, "col"),
        P(None, None, "col"),
        P("col"),
        P("col", None, None),
        P(None, None, "col"),
        P(ROWS[:3], None, None),
        P(ROWS[:3], None),
        P(ROWS[:3], None),
        P(ROWS[:3], "col", None, None),
        P("col", None),
        P(None, None, "col"),
    )
    return jax.shard_map(
        on_device, mesh=grid, in_specs=placed, out_specs=P(ROWS, None), check_vma=False
    )
```

```python
import math

import jax
import jax.numpy as jnp
import numpy as np
from jax import lax
from jax.experimental import pallas as pl
from jax.experimental.pallas import tpu as pltpu
from jax.sharding import Mesh
from jax.sharding import PartitionSpec as P

epsilon = 1e-05
ROWS = ("z", "y", "x", "col")


def rms_scale(values, gain):
    widened = values.astype(jnp.float32)
    factor = lax.rsqrt(jnp.mean(widened * widened, axis=-1, keepdims=True) + epsilon)
    return (widened * factor * gain).astype(jnp.bfloat16)


def swap(value):
    return lax.ppermute(value, "col", perm=[(0, 1), (1, 0)])


def pair_rows(mine, other, col):
    first = jnp.where(col == 0, mine, other)
    second = jnp.where(col == 0, other, mine)
    return jnp.concatenate([first, second], axis=0)


def pick_states(index, valid, plane, lines):
    slots = index.shape[0]
    per_line = slots // lines
    block = plane.shape[1:]

    def body(index_ref, valid_ref, plane_ref, out_ref, zero_ref, sems):
        zero_ref[...] = jnp.zeros(block, plane.dtype)
        for s in range(slots):
            dst = out_ref.at[s // per_line, s % per_line]

            @pl.when(valid_ref[s] != 0)
            def _():
                pltpu.make_async_copy(plane_ref.at[index_ref[s]], dst, sems.at[s]).start()

            @pl.when(valid_ref[s] == 0)
            def _():
                pltpu.make_async_copy(zero_ref, dst, sems.at[s]).start()

        for s in range(slots):
            dst = out_ref.at[s // per_line, s % per_line]
            pltpu.make_async_copy(zero_ref, dst, sems.at[s]).wait()

    return pl.pallas_call(
        body,
        out_shape=jax.ShapeDtypeStruct((lines, per_line) + block, plane.dtype),
        grid_spec=pltpu.PrefetchScalarGridSpec(
            num_scalar_prefetch=2,
            grid=(),
            in_specs=[pl.BlockSpec(memory_space=pl.ANY)],
            out_specs=pl.BlockSpec(memory_space=pl.ANY),
            scratch_shapes=[pltpu.VMEM(block, plane.dtype), pltpu.SemaphoreType.DMA((slots,))],
        ),
    )(index, valid, plane)


def on_device(
    tokens,
    norm_gain_pair,
    query_key_value_weight,
    head_gate_weight,
    decay_logit_bias,
    adapter_down_factor,
    adapter_up_factor,
    lengths,
    request_adapter_index,
    request_cache_index,
    caches,
    head_output_weight,
    feedforward_weight,
):
    tok_rows, width = tokens.shape
    col = lax.axis_index("col")
    col_count = 2
    group = tok_rows * col_count
    head_cols = query_key_value_weight.shape[2]
    local_heads = head_gate_weight.shape[2]
    head_size = head_cols // local_heads
    group_lengths = lengths[0].reshape(-1)
    scale = 1.0 / math.sqrt(head_size)

    down_other = swap(adapter_down_factor)
    out_weight_other = swap(head_output_weight)

    plane = lax.all_gather(jnp.swapaxes(caches, -1, -2), ("y", "x"), axis=0, tiled=True)
    per_plane = plane.shape[0]

    normalized_rows = rms_scale(tokens, norm_gain_pair[0])
    gathered = pair_rows(normalized_rows, swap(normalized_rows), col)
    positions = jnp.arange(group, dtype=jnp.int32)
    ends = jnp.cumsum(group_lengths)
    starts = ends - group_lengths
    member = (
        (positions[:, None] >= starts[None, :]) & (positions[:, None] < ends[None, :])
    ).astype(jnp.float32)
    segment = jnp.sum((positions[:, None] >= ends[None, :]).astype(jnp.int32), axis=1)
    projected = jnp.einsum(
        "td,kdc->ktc", gathered, query_key_value_weight, preferred_element_type=jnp.float32
    )
    half_adapters = adapter_down_factor.shape[0]
    mine_numbers = col * half_adapters + jnp.arange(half_adapters, dtype=jnp.int32)
    other_numbers = (1 - col) * half_adapters + jnp.arange(half_adapters, dtype=jnp.int32)
    wanted = request_adapter_index[0][:, None]
    select_mine = (wanted == mine_numbers[None, :]).astype(jnp.bfloat16)
    select_other = (wanted == other_numbers[None, :]).astype(jnp.bfloat16)
    chosen = (
        jnp.einsum("sa,adr->sdr", select_mine, adapter_down_factor, preferred_element_type=jnp.float32)
        + jnp.einsum("sa,adr->sdr", select_other, down_other, preferred_element_type=jnp.float32)
    ).astype(jnp.bfloat16)
    per_request = jnp.einsum("td,sdr->tsr", gathered, chosen, preferred_element_type=jnp.float32)
    low_rank_delta = jnp.sum(member[:, :, None] * per_request, axis=1)
    low_rank_delta = low_rank_delta.astype(jnp.bfloat16)
    adapter_onehot = (
        request_adapter_index[0][:, None]
        == jnp.arange(adapter_up_factor.shape[0], dtype=jnp.int32)[None, :]
    ).astype(jnp.bfloat16)
    up_chosen = jnp.einsum(
        "gq,qjl->gjl", adapter_onehot, adapter_up_factor, preferred_element_type=jnp.float32
    ).astype(jnp.bfloat16)
    masked_low = low_rank_delta[:, None, :] * member.astype(jnp.bfloat16)[:, :, None]
    delta = jnp.einsum("tsr,src->tc", masked_low, up_chosen, preferred_element_type=jnp.float32)
    queries = (projected[0] + delta).astype(jnp.bfloat16).reshape(group, local_heads, head_size)
    plane, queries = lax.optimization_barrier((plane, queries))
    z_count = lax.axis_size("z")
    z_here = lax.axis_index("z")
    own_index = request_cache_index[0]
    shifts = range(1, z_count)

    def along_z(value, d):
        return lax.ppermute(value, "z", perm=[(i, (i + d) % z_count) for i in range(z_count)])

    behind = jnp.stack([own_index] + [along_z(own_index, d) for d in shifts])
    line_rows = jnp.take(behind, (z_here - jnp.arange(z_count, dtype=jnp.int32)) % z_count, axis=0)
    local = line_rows - z_here * per_plane
    valid = ((local >= 0) & (local < per_plane)).astype(jnp.int32)
    picked = jnp.take(plane, jnp.clip(local, 0, per_plane - 1).reshape(-1), axis=0)
    keep = valid.reshape(-1).astype(plane.dtype)[:, None, None, None]
    slots = (picked * keep).reshape((z_count, -1) + plane.shape[1:])
    lead = slots.shape[2] - 1
    states_lead = lax.psum_scatter(slots[:, :, :lead], "z", scatter_dimension=0, tiled=True)[0]
    tail_slots = slots[:, :, lead:]
    states_tail = jnp.take(tail_slots, z_here, axis=0).astype(jnp.float32)
    for d in shifts:
        outgoing = jnp.take(tail_slots, (z_here + d) % z_count, axis=0)
        states_tail = states_tail + along_z(outgoing, d).astype(jnp.float32)
    states = jnp.concatenate([states_lead, states_tail.astype(jnp.bfloat16)], axis=1)
    keys = projected[1].astype(jnp.bfloat16).reshape(group, local_heads, head_size)
    values = projected[2].astype(jnp.bfloat16).reshape(group, local_heads, head_size)
    gate_terms = jnp.einsum(
        "td,kdh->kth", gathered, head_gate_weight, preferred_element_type=jnp.float32
    )
    log_keep = jax.nn.log_sigmoid(gate_terms[0] + decay_logit_bias[None, :])
    mix_gate = jax.nn.sigmoid(gate_terms[1])
    running = jnp.cumsum(log_keep, axis=0)
    before = running - log_keep
    start_hot = (positions[None, :] == starts[:, None]).astype(jnp.float32)
    start_level = jnp.sum(start_hot[:, :, None] * before[None, :, :], axis=1)
    level = running - jnp.sum(member[:, :, None] * start_level[None, :, :], axis=1)
    masked_queries = queries[:, None, :, :] * member.astype(jnp.bfloat16)[:, :, None, None]
    masked_queries, mix_gate = lax.optimization_barrier((masked_queries, mix_gate))
    from_state = jnp.einsum(
        "tshi,shji->thj", masked_queries, states, preferred_element_type=jnp.float32
    )
    carried = from_state * jnp.exp(level)[:, :, None]

    scores = jnp.einsum("qhd,khd->hqk", queries, keys, preferred_element_type=jnp.float32) * scale
    allowed = (segment[:, None] == segment[None, :]) & (positions[None, :] <= positions[:, None])
    masked = jnp.where(allowed[None], scores, -jnp.inf)
    peak = jnp.max(masked, axis=2, keepdims=True)
    weights = jnp.exp(masked - peak)
    probs = (weights / jnp.sum(weights, axis=2, keepdims=True)).astype(jnp.bfloat16)
    attended = jnp.einsum("hqk,khd->qhd", probs, values, preferred_element_type=jnp.float32)
    gap = jnp.where(allowed[None], running.T[:, :, None] - running.T[:, None, :], -jnp.inf)
    memory_w = (scores * jnp.exp(gap)).astype(jnp.bfloat16)
    recalled = jnp.einsum("hqk,khd->qhd", memory_w, values, preferred_element_type=jnp.float32)
    recalled = recalled + carried
    factor = lax.rsqrt(jnp.mean(recalled * recalled, axis=2, keepdims=True) + epsilon)
    combined = attended + mix_gate[:, :, None] * recalled * factor
    head_out = combined.astype(jnp.bfloat16).reshape(group, head_cols)

    head_own = lax.dynamic_slice_in_dim(head_out, col * tok_rows, tok_rows, axis=0)
    head_sent = lax.dynamic_slice_in_dim(head_out, (1 - col) * tok_rows, tok_rows, axis=0)
    attn_proj = jnp.dot(head_own, head_output_weight, preferred_element_type=jnp.float32) + jnp.dot(
        swap(head_sent), out_weight_other, preferred_element_type=jnp.float32
    )
    mixed = (tokens.astype(jnp.float32) + attn_proj).astype(jnp.bfloat16)
    normed_two = rms_scale(mixed, norm_gain_pair[1])

    def feed_part(rows):
        gate_up = jnp.einsum(
            "td,kdf->ktf", rows, feedforward_weight[:2], preferred_element_type=jnp.float32
        )
        hidden = (jax.nn.silu(gate_up[0]) * gate_up[1]).astype(jnp.bfloat16)
        return jnp.einsum(
            "tf,df->td", hidden, feedforward_weight[2], preferred_element_type=jnp.float32
        )

    half = normed_two.shape[0] // 2
    own_first = feed_part(normed_two[:half])
    own_first, partner_two = lax.optimization_barrier((own_first, swap(normed_two)))
    from_partner = swap(feed_part(partner_two))
    feed = jnp.concatenate([own_first, feed_part(normed_two[half:])], axis=0) + from_partner
    return (mixed.astype(jnp.float32) + feed).astype(jnp.bfloat16)


def solution(mesh):
    n_req = mesh.shape["req"]
    side = round(n_req ** (1.0 / 3.0))
    devices = np.asarray(mesh.devices).reshape(side, side, n_req // (side * side), mesh.shape["col"])
    grid = Mesh(devices, ROWS)
    placed = (
        P(ROWS, None),
        P(),
        P(None, None, "col"),
        P(None, None, "col"),
        P("col"),
        P("col", None, None),
        P(None, None, "col"),
        P(ROWS[:3], None, None),
        P(ROWS[:3], None),
        P(ROWS[:3], None),
        P(ROWS[:3], "col", None, None),
        P("col", None),
        P(None, None, "col"),
    )
    return jax.shard_map(
        on_device, mesh=grid, in_specs=placed, out_specs=P(ROWS, None), check_vma=False
    )
```

```python
import math

import jax
import jax.numpy as jnp
import numpy as np
from jax import lax
from jax.experimental import pallas as pl
from jax.experimental.pallas import tpu as pltpu
from jax.sharding import Mesh
from jax.sharding import PartitionSpec as P

epsilon = 1e-05
ROWS = ("z", "y", "x", "col")


def rms_scale(values, gain):
    widened = values.astype(jnp.float32)
    factor = lax.rsqrt(jnp.mean(widened * widened, axis=-1, keepdims=True) + epsilon)
    return (widened * factor * gain).astype(jnp.bfloat16)


def swap(value):
    return lax.ppermute(value, "col", perm=[(0, 1), (1, 0)])


def pair_rows(mine, other, col):
    first = jnp.where(col == 0, mine, other)
    second = jnp.where(col == 0, other, mine)
    return jnp.concatenate([first, second], axis=0)


def pick_states(index, valid, plane, lines):
    slots = index.shape[0]
    per_line = slots // lines
    block = plane.shape[1:]

    def body(index_ref, valid_ref, plane_ref, out_ref, zero_ref, sems):
        zero_ref[...] = jnp.zeros(block, plane.dtype)
        for s in range(slots):
            dst = out_ref.at[s // per_line, s % per_line]

            @pl.when(valid_ref[s] != 0)
            def _():
                pltpu.make_async_copy(plane_ref.at[index_ref[s]], dst, sems.at[s]).start()

            @pl.when(valid_ref[s] == 0)
            def _():
                pltpu.make_async_copy(zero_ref, dst, sems.at[s]).start()

        for s in range(slots):
            dst = out_ref.at[s // per_line, s % per_line]
            pltpu.make_async_copy(zero_ref, dst, sems.at[s]).wait()

    return pl.pallas_call(
        body,
        out_shape=jax.ShapeDtypeStruct((lines, per_line) + block, plane.dtype),
        grid_spec=pltpu.PrefetchScalarGridSpec(
            num_scalar_prefetch=2,
            grid=(),
            in_specs=[pl.BlockSpec(memory_space=pl.ANY)],
            out_specs=pl.BlockSpec(memory_space=pl.ANY),
            scratch_shapes=[pltpu.VMEM(block, plane.dtype), pltpu.SemaphoreType.DMA((slots,))],
        ),
    )(index, valid, plane)


def on_device(
    tokens,
    norm_gain_pair,
    query_key_value_weight,
    head_gate_weight,
    decay_logit_bias,
    adapter_down_factor,
    adapter_up_factor,
    lengths,
    request_adapter_index,
    request_cache_index,
    caches,
    head_output_weight,
    feedforward_weight,
):
    tok_rows, width = tokens.shape
    col = lax.axis_index("col")
    col_count = 2
    group = tok_rows * col_count
    head_cols = query_key_value_weight.shape[2]
    local_heads = head_gate_weight.shape[2]
    head_size = head_cols // local_heads
    group_lengths = lengths[0].reshape(-1)
    scale = 1.0 / math.sqrt(head_size)

    down_other = swap(adapter_down_factor)
    out_weight_other = swap(head_output_weight)

    plane = lax.all_gather(jnp.swapaxes(caches, -1, -2), ("y", "x"), axis=0, tiled=True)
    per_plane = plane.shape[0]

    normalized_rows = rms_scale(tokens, norm_gain_pair[0])
    gathered = pair_rows(normalized_rows, swap(normalized_rows), col)
    positions = jnp.arange(group, dtype=jnp.int32)
    ends = jnp.cumsum(group_lengths)
    starts = ends - group_lengths
    member = (
        (positions[:, None] >= starts[None, :]) & (positions[:, None] < ends[None, :])
    ).astype(jnp.float32)
    segment = jnp.sum((positions[:, None] >= ends[None, :]).astype(jnp.int32), axis=1)
    projected = jnp.einsum(
        "td,kdc->ktc", gathered, query_key_value_weight, preferred_element_type=jnp.float32
    )
    half_adapters = adapter_down_factor.shape[0]
    mine_numbers = col * half_adapters + jnp.arange(half_adapters, dtype=jnp.int32)
    other_numbers = (1 - col) * half_adapters + jnp.arange(half_adapters, dtype=jnp.int32)
    wanted = request_adapter_index[0][:, None]
    select_mine = (wanted == mine_numbers[None, :]).astype(jnp.bfloat16)
    select_other = (wanted == other_numbers[None, :]).astype(jnp.bfloat16)
    chosen = (
        jnp.einsum("sa,adr->sdr", select_mine, adapter_down_factor, preferred_element_type=jnp.float32)
        + jnp.einsum("sa,adr->sdr", select_other, down_other, preferred_element_type=jnp.float32)
    ).astype(jnp.bfloat16)
    per_request = jnp.einsum("td,sdr->tsr", gathered, chosen, preferred_element_type=jnp.float32)
    low_rank_delta = jnp.sum(member[:, :, None] * per_request, axis=1)
    low_rank_delta = low_rank_delta.astype(jnp.bfloat16)
    adapter_onehot = (
        request_adapter_index[0][:, None]
        == jnp.arange(adapter_up_factor.shape[0], dtype=jnp.int32)[None, :]
    ).astype(jnp.bfloat16)
    up_chosen = jnp.einsum(
        "gq,qjl->gjl", adapter_onehot, adapter_up_factor, preferred_element_type=jnp.float32
    ).astype(jnp.bfloat16)
    masked_low = low_rank_delta[:, None, :] * member.astype(jnp.bfloat16)[:, :, None]
    delta = jnp.einsum("tsr,src->tc", masked_low, up_chosen, preferred_element_type=jnp.float32)
    queries = (projected[0] + delta).astype(jnp.bfloat16).reshape(group, local_heads, head_size)
    plane, queries = lax.optimization_barrier((plane, queries))
    z_count = lax.axis_size("z")
    z_here = lax.axis_index("z")
    own_index = request_cache_index[0]
    shifts = range(1, z_count)

    def along_z(value, d):
        return lax.ppermute(value, "z", perm=[(i, (i + d) % z_count) for i in range(z_count)])

    behind = jnp.stack([own_index] + [along_z(own_index, d) for d in shifts])
    line_rows = jnp.take(behind, (z_here - jnp.arange(z_count, dtype=jnp.int32)) % z_count, axis=0)
    local = line_rows - z_here * per_plane
    valid = ((local >= 0) & (local < per_plane)).astype(jnp.int32)
    picked = jnp.take(plane, jnp.clip(local, 0, per_plane - 1).reshape(-1), axis=0)
    keep = valid.reshape(-1).astype(plane.dtype)[:, None, None, None]
    slots = (picked * keep).reshape((z_count, -1) + plane.shape[1:])
    states = lax.psum_scatter(slots, "z", scatter_dimension=0, tiled=True)[0]
    keys = projected[1].astype(jnp.bfloat16).reshape(group, local_heads, head_size)
    values = projected[2].astype(jnp.bfloat16).reshape(group, local_heads, head_size)
    gate_terms = jnp.einsum(
        "td,kdh->kth", gathered, head_gate_weight, preferred_element_type=jnp.float32
    )
    log_keep = jax.nn.log_sigmoid(gate_terms[0] + decay_logit_bias[None, :])
    mix_gate = jax.nn.sigmoid(gate_terms[1])
    running = jnp.cumsum(log_keep, axis=0)
    before = running - log_keep
    start_hot = (positions[None, :] == starts[:, None]).astype(jnp.float32)
    start_level = jnp.sum(start_hot[:, :, None] * before[None, :, :], axis=1)
    level = running - jnp.sum(member[:, :, None] * start_level[None, :, :], axis=1)
    per_core = group_lengths.shape[0] // col_count
    halves = member.reshape(col_count, tok_rows, col_count, per_core)
    half_member = jnp.stack([halves[c, :, c] for c in range(col_count)])
    masked_queries = (
        queries.reshape(col_count, tok_rows, 1, local_heads, head_size)
        * half_member.astype(jnp.bfloat16)[:, :, :, None, None]
    )
    masked_queries, mix_gate = lax.optimization_barrier((masked_queries, mix_gate))
    from_state = jnp.einsum(
        "ctshi,cshji->cthj",
        masked_queries,
        states.reshape((col_count, per_core) + states.shape[1:]),
        preferred_element_type=jnp.float32,
    ).reshape(group, local_heads, head_size)
    carried = from_state * jnp.exp(level)[:, :, None]

    scores = jnp.einsum("qhd,khd->hqk", queries, keys, preferred_element_type=jnp.float32) * scale
    allowed = (segment[:, None] == segment[None, :]) & (positions[None, :] <= positions[:, None])
    masked = jnp.where(allowed[None], scores, -jnp.inf)
    peak = jnp.max(masked, axis=2, keepdims=True)
    weights = jnp.exp(masked - peak)
    probs = (weights / jnp.sum(weights, axis=2, keepdims=True)).astype(jnp.bfloat16)
    attended = jnp.einsum("hqk,khd->qhd", probs, values, preferred_element_type=jnp.float32)
    gap = jnp.where(allowed[None], running.T[:, :, None] - running.T[:, None, :], -jnp.inf)
    memory_w = (scores * jnp.exp(gap)).astype(jnp.bfloat16)
    recalled = jnp.einsum("hqk,khd->qhd", memory_w, values, preferred_element_type=jnp.float32)
    recalled = recalled + carried
    factor = lax.rsqrt(jnp.mean(recalled * recalled, axis=2, keepdims=True) + epsilon)
    combined = attended + mix_gate[:, :, None] * recalled * factor
    head_out = combined.astype(jnp.bfloat16).reshape(group, head_cols)

    head_own = lax.dynamic_slice_in_dim(head_out, col * tok_rows, tok_rows, axis=0)
    head_sent = lax.dynamic_slice_in_dim(head_out, (1 - col) * tok_rows, tok_rows, axis=0)
    attn_proj = jnp.dot(head_own, head_output_weight, preferred_element_type=jnp.float32) + jnp.dot(
        swap(head_sent), out_weight_other, preferred_element_type=jnp.float32
    )
    mixed = (tokens.astype(jnp.float32) + attn_proj).astype(jnp.bfloat16)
    normed_two = rms_scale(mixed, norm_gain_pair[1])

    def feed_part(rows):
        gate_up = jnp.einsum(
            "td,kdf->ktf", rows, feedforward_weight[:2], preferred_element_type=jnp.float32
        )
        hidden = (jax.nn.silu(gate_up[0]) * gate_up[1]).astype(jnp.bfloat16)
        return jnp.einsum(
            "tf,df->td", hidden, feedforward_weight[2], preferred_element_type=jnp.float32
        )

    half = normed_two.shape[0] // 2
    own_first = feed_part(normed_two[:half])
    own_first, partner_two = lax.optimization_barrier((own_first, swap(normed_two)))
    from_partner = swap(feed_part(partner_two))
    feed = jnp.concatenate([own_first, feed_part(normed_two[half:])], axis=0) + from_partner
    return (mixed.astype(jnp.float32) + feed).astype(jnp.bfloat16)


def solution(mesh):
    n_req = mesh.shape["req"]
    side = round(n_req ** (1.0 / 3.0))
    devices = np.asarray(mesh.devices).reshape(side, side, n_req // (side * side), mesh.shape["col"])
    grid = Mesh(devices, ROWS)
    placed = (
        P(ROWS, None),
        P(),
        P(None, None, "col"),
        P(None, None, "col"),
        P("col"),
        P("col", None, None),
        P(None, None, "col"),
        P(ROWS[:3], None, None),
        P(ROWS[:3], None),
        P(ROWS[:3], None),
        P(ROWS[:3], "col", None, None),
        P("col", None),
        P(None, None, "col"),
    )
    return jax.shard_map(
        on_device, mesh=grid, in_specs=placed, out_specs=P(ROWS, None), check_vma=False
    )
```
